128 devices in a mesh: region: 128 (over y, z, x, core).
Axes of the slice: x: 4, y: 4, z: 4, core: 2. Of those that a mesh axis runs over, the one named last changes fastest.
Arguments:
- mixing_ratio: bfloat16 [150, 1048576], P(None, 'region'), may hold values from 0.049804688 to 5
- send_rows: int32 [128, 8, 128], P('region'), may hold values from 0 to 8191, as said below
- migrant_count: int32 [128, 8], P('region'), may hold values from 1 to 128, as said below
- arrival_slot: int32 [128, 8, 128], P('region'), may hold values from 0 to 8191, as said below
- halo_blocks: int32 [128, 2, 16], P('region'), may hold values from 0 to 63
- neighbour_block: int32 [8192, 3], P('region'), may hold values from 0 to 95
- mix_weight: bfloat16 [8192, 4, 128, 128], P('region'), may hold values from 0 to 0.0078125
- inverse_temp: float32 [1048576], P('region'), may hold values from -1 to 1
- reactant_order: float32 [256, 150], replicated, may hold values from 0 to 0.05
- log_prefactor: float32 [256], replicated, may hold values from -1 to 1
- activation_energy: float32 [256], replicated, may hold values from 0.2 to 1.5
- production: float32 [150, 256], replicated, may hold values from 0 to 0.0078125
- loss_coefficient: float32 [150, 256], replicated, may hold values from 0 to 0.0078125
Outputs:
- updated_ratio: float32 [150, 1048576], P(None, 'region')
The draws below stay inside these ranges and needn't reach their ends.
Inputs may be any that keep to these rules, and one draw needn't show every extreme that they name: `migrant_count`: entry j of a region counts the parcels it sends to the region at offset o_j along the loop of regions; it equals the count that region sends back at offset -o_j. Some pair of regions reaches 128; regions near a few busy ones send far more. `send_rows`: the first migrant_count entries of each peer slot are distinct local parcels of the region, disjoint over all slots; the remaining entries are 0. `arrival_slot`: over all peer slots, the first migrant_count entries name each parcel that the same region lists in send_rows exactly once; the remaining entries are 0.
All inputs are finite; a program needn't handle non-finite values.
Results may differ from the reference program's by a relative error of at most 0.0003.
Values may be sent and summed in bfloat16 or wider, within the bound.
No kernel may reach another device: no remote copies, remote signals or barrier semaphores. Data moves between devices by JAX's collectives and lax.ppermute only.
A program may use at most 128 MiB of HBM per device.

```python
import math
import jax
import jax.numpy as jnp
from jax import lax

S = 150
R = 256
BLK = 128
K = 3
HOP = 4
CAP = 128
P_DEV = 8192
NB = 64
BCAP = 16
PARCELS = 1048576
BLOCKS = 8192
N_REGION = 128


def peer_offsets_drawn():
    return [column - HOP if column < HOP else column - HOP + 1 for column in range(2 * HOP)]


def shuffle_one(key_region):
    return jax.random.permutation(key_region, P_DEV).astype(jnp.int32)


def migration_plan(key):
    regions = N_REGION
    base_key = jax.random.fold_in(key, 7)
    key_busy, key_load, key_peak, key_shuffle, key_rotate = jax.random.split(base_key, 5)
    busy_region = jax.random.randint(key_busy, (regions,), 0, 8) == 0
    load_bits = jax.random.randint(key_load, (regions, HOP), 0, 1 << 20)
    small_cap = max(1, CAP // 4)
    edge_counts = []
    for distance in range(1, HOP + 1):
        either_busy = busy_region | jnp.roll(busy_region, -distance)
        edge_limit = jnp.where(either_busy, CAP, small_cap)
        edge_counts.append(load_bits[:, distance - 1] % edge_limit + 1)
    upward = jnp.stack(edge_counts, axis=1).astype(jnp.int32)
    peak_region = jax.random.randint(key_peak, (), 0, regions)
    upward = upward.at[peak_region, 0].set(CAP)
    columns = []
    for offset in peer_offsets_drawn():
        if offset > 0:
            columns.append(upward[:, offset - 1])
        else:
            columns.append(jnp.roll(upward[:, -offset - 1], -offset))
    counts = jnp.stack(columns, axis=1).astype(jnp.int32)
    starts = jnp.cumsum(counts, axis=1) - counts
    total_out = jnp.sum(counts, axis=1)
    shuffles = jax.vmap(shuffle_one)(jax.random.split(key_shuffle, regions))
    rotation = jax.random.randint(key_rotate, (regions,), 0, 1 << 20) % total_out
    lane_index = jnp.arange(CAP, dtype=jnp.int32)
    live_lane = lane_index[None, None, :] < counts[:, :, None]
    position = starts[:, :, None] + lane_index[None, None, :]
    sent_rows = jnp.take_along_axis(shuffles, position.reshape(regions, -1), axis=1).reshape(regions, 2 * HOP, CAP)
    sent_rows = jnp.where(live_lane, sent_rows, 0).astype(jnp.int32)
    arrive_position = (position + rotation[:, None, None]) % total_out[:, None, None]
    arrive_rows = jnp.take_along_axis(shuffles, arrive_position.reshape(regions, -1), axis=1).reshape(regions, 2 * HOP, CAP)
    arrive_rows = jnp.where(live_lane, arrive_rows, 0).astype(jnp.int32)
    return (counts, sent_rows, arrive_rows)


def draw_send_rows(key, part):
    return migration_plan(key)[1]


def draw_migrant_count(key, part):
    return migration_plan(key)[0]


def draw_arrival_slot(key, part):
    return migration_plan(key)[2]


def with_ends(entries, stream_key, low, largest):
    longest = entries.shape.index(max(entries.shape))
    spots = []
    for shift in (0, 1):
        where = [jax.random.randint(jax.random.fold_in(stream_key, axis), (), 0, length) for axis, length in enumerate(entries.shape)]
        where[longest] = (where[longest] + shift) % entries.shape[longest]
        spots.append(tuple(where))
    return entries.at[spots[0]].set(low).at[spots[1]].set(largest)


def levels(own_key, dims, cuts, smallest, high):
    factor_of = 1.0
    for dim, parts in cuts:
        draws = jax.random.uniform(jax.random.fold_in(jax.random.fold_in(own_key, 6), dim), (parts,), jnp.float32, smallest / len(cuts), high / len(cuts))
        factor_of = factor_of * jnp.repeat(jnp.exp(draws), dims[dim] // parts).reshape((-1,) + (1,) * (len(dims) - 1 - dim))
    return factor_of


def setup_inputs(seed: int = 0) -> dict:
    key_of = jax.random.split(jax.random.key(seed), 14)
    mixing_ratio = jnp.clip(jnp.exp(math.log(5.0) - 4.609084 * jax.random.uniform(key_of[0], (S, PARCELS), jnp.float32) ** levels(key_of[0], (S, PARCELS), ((1, 128),), -0.2, 0.2)), 0.049804688, 5.0).astype(jnp.bfloat16)
    send_rows = draw_send_rows(jax.random.fold_in(key_of[13], 71), 0)
    migrant_count = draw_migrant_count(jax.random.fold_in(key_of[13], 71), 0)
    arrival_slot = draw_arrival_slot(jax.random.fold_in(key_of[13], 71), 0)
    halo_blocks = with_ends(jax.random.randint(key_of[4], (N_REGION, 2, BCAP), 0, NB), jax.random.fold_in(key_of[4], 1), 0, NB - 1).astype(jnp.int32)
    neighbour_block = with_ends(jax.random.randint(key_of[5], (BLOCKS, K), 0, NB + 2 * BCAP), jax.random.fold_in(key_of[5], 1), 0, (NB + 2 * BCAP) - 1).astype(jnp.int32)
    mix_weight = jnp.clip(0.0078125 * jax.random.uniform(key_of[6], (BLOCKS, K + 1, BLK, BLK), jnp.float32) ** levels(key_of[6], (BLOCKS, K + 1, BLK, BLK), ((0, 128),), -0.2, 0.2), 0.0, 0.0078125).astype(jnp.bfloat16)
    inverse_temp = jnp.clip(jax.random.uniform(key_of[7], (PARCELS,), jnp.float32, -1.0, 1.0) * levels(key_of[7], (PARCELS,), ((0, 128),), -0.4, 0.0), -1.0, 1.0)
    reactant_order = jnp.clip(jax.random.uniform(key_of[8], (R, S), jnp.float32, 0.0, 0.05), 0.0, 0.05)
    log_prefactor = jnp.clip(jax.random.uniform(key_of[9], (R,), jnp.float32, -1.0, 1.0), -1.0, 1.0)
    activation_energy = jnp.clip(jax.random.uniform(key_of[10], (R,), jnp.float32, 0.2, 1.5), 0.2, 1.5)
    production = jnp.clip(jax.random.uniform(key_of[11], (S, R), jnp.float32, 0.0, 0.0078125), 0.0, 0.0078125)
    loss_coefficient = jnp.clip(jax.random.uniform(key_of[12], (S, R), jnp.float32, 0.0, 0.0078125), 0.0, 0.0078125)
    return {"mixing_ratio": mixing_ratio, "send_rows": send_rows, "migrant_count": migrant_count, "arrival_slot": arrival_slot, "halo_blocks": halo_blocks, "neighbour_block": neighbour_block, "mix_weight": mix_weight, "inverse_temp": inverse_temp, "reactant_order": reactant_order, "log_prefactor": log_prefactor, "activation_energy": activation_energy, "production": production, "loss_coefficient": loss_coefficient}


def peer_offsets():
    return [column - HOP if column < HOP else column - HOP + 1 for column in range(2 * HOP)]


def pick_rows(region_shard, row_list):
    return jnp.take(region_shard, row_list.reshape(-1), axis=1).reshape(S, 2 * HOP, CAP)


def pick_blocks(block_rows, block_list):
    return jnp.take(block_rows, block_list, axis=1)


def place_arrivals(region_shard, arrived, counts, slot_list):
    lane_index = jnp.arange(CAP, dtype=jnp.int32)
    live_lane = lane_index[None, :] < counts[:, None]
    target = jnp.where(live_lane, slot_list, P_DEV).astype(jnp.int32)
    return region_shard.at[:, target.reshape(-1)].set(arrived.reshape(S, -1), mode="drop")


def reference(mixing_ratio, send_rows, migrant_count, arrival_slot, halo_blocks, neighbour_block, mix_weight, inverse_temp, reactant_order, log_prefactor, activation_energy, production, loss_coefficient):
    regions = N_REGION
    offsets = peer_offsets()
    peer_count = len(offsets)
    shards = mixing_ratio.reshape(S, regions, P_DEV).transpose(1, 0, 2)
    outgoing = jax.vmap(pick_rows)(shards, send_rows)
    received = jnp.stack([jnp.roll(outgoing[:, :, peer_count - 1 - column, :], -offsets[column], axis=0) for column in range(peer_count)], axis=2)
    migrated = jax.vmap(place_arrivals)(shards, received, migrant_count, arrival_slot)
    blocks = migrated.reshape(regions, S, NB, BLK)
    to_lower = jax.vmap(pick_blocks)(blocks, halo_blocks[:, 0])
    to_upper = jax.vmap(pick_blocks)(blocks, halo_blocks[:, 1])
    from_lower = jnp.roll(to_upper, 1, axis=0)
    from_upper = jnp.roll(to_lower, -1, axis=0)
    tables = jnp.concatenate([blocks, from_lower, from_upper], axis=2)
    neighbours = neighbour_block.reshape(regions, NB, K)
    weights = mix_weight.reshape(regions, NB, K + 1, BLK, BLK)
    temp_rows = inverse_temp.reshape(regions, P_DEV)

    def one_region(region_items):
        block_table, neighbour, weight, temp_row = region_items
        own_blocks = block_table[:, :NB].astype(jnp.float32)
        gathered = jnp.take(block_table, neighbour, axis=1).astype(jnp.float32)
        weight_f = weight.astype(jnp.float32)
        mixed_ratio = jnp.einsum("sbp,bpq->sbq", own_blocks, weight_f[:, 0], precision=lax.Precision.HIGHEST)
        mixed_ratio = mixed_ratio + jnp.einsum("sbkp,bkpq->sbq", gathered, weight_f[:, 1:], precision=lax.Precision.HIGHEST)
        mixed_ratio = mixed_ratio.reshape(S, P_DEV)
        log_ratio = jnp.log(mixed_ratio)
        exponent = jnp.dot(reactant_order, log_ratio, precision=lax.Precision.HIGHEST)
        reaction_rate = jnp.exp(log_prefactor[:, None] - activation_energy[:, None] * temp_row[None, :] + exponent)
        gained = jnp.dot(production, reaction_rate, precision=lax.Precision.HIGHEST)
        lost_mass = jnp.dot(loss_coefficient, reaction_rate, precision=lax.Precision.HIGHEST)
        return (mixed_ratio + gained) / (1.0 + lost_mass / mixed_ratio)

    results = lax.map(one_region, (tables, neighbours, weights, temp_rows))
    return results.transpose(1, 0, 2).reshape(S, regions * P_DEV)
```

```python
import functools

import jax
import jax.numpy as jnp
from jax import lax
from jax.experimental import pallas as pl
from jax.experimental.pallas import tpu as pltpu
from jax.sharding import PartitionSpec as P

HOP = 4
TILE_BLOCKS = 4


def from_behind(block, axis, distance):
    devices = range(lax.axis_size(axis))
    route = [((i - distance) % len(devices), i) for i in devices]
    return lax.ppermute(block, axis, route)


def peer_offsets():
    return [column - HOP if column < HOP else column - HOP + 1 for column in range(2 * HOP)]


def migrate(mixing_ratio, send_rows, migrant_count, arrival_slot):
    species, parcels = mixing_ratio.shape
    capacity = send_rows.shape[-1]
    offsets = peer_offsets()
    peer_count = len(offsets)
    outgoing = jnp.take(mixing_ratio, send_rows[0].reshape(-1), axis=1).reshape(
        species, peer_count, capacity
    )
    arrived = []
    for column in range(peer_count):
        opposite = peer_count - 1 - column
        arrived.append(from_behind(outgoing[:, opposite, :], "region", -offsets[column]))
    received = jnp.stack(arrived, axis=1)
    lane_index = jnp.arange(capacity, dtype=jnp.int32)
    live_lane = lane_index[None, :] < migrant_count[0][:, None]
    target_slot = jnp.where(live_lane, arrival_slot[0], parcels)
    return mixing_ratio.at[:, target_slot.reshape(-1)].set(
        received.reshape(species, -1), mode="drop"
    )


def block_table(migrated, halo_blocks, block_size):
    species, parcels = migrated.shape
    blocks = migrated.reshape(species, parcels // block_size, block_size)
    to_lower = jnp.take(blocks, halo_blocks[0, 0], axis=1)
    to_upper = jnp.take(blocks, halo_blocks[0, 1], axis=1)
    from_lower = from_behind(to_upper, "region", 1)
    from_upper = from_behind(to_lower, "region", -1)
    return jnp.concatenate(
        [
            migrated,
            from_lower.reshape(species, -1),
            from_upper.reshape(species, -1),
        ],
        axis=1,
    )


def split3(x):
    high = x.astype(jnp.bfloat16)
    low = (x - high.astype(jnp.float32)).astype(jnp.bfloat16)
    return high, low


def dot3(a_high, a_low, b_high, b_low):
    f32 = jnp.float32
    total = jnp.dot(a_high, b_high, preferred_element_type=f32)
    total = total + jnp.dot(a_high, b_low, preferred_element_type=f32)
    return total + jnp.dot(a_low, b_high, preferred_element_type=f32)


def mix_react_kernel(tile_blocks, neighbours, block_size, nb_ref, own_ref, *refs):
    count = tile_blocks * neighbours
    picked = refs[:count]
    (
        weight_ref,
        temp_ref,
        order_high,
        order_low,
        prefactor_ref,
        energy_ref,
        prod_high,
        prod_low,
        loss_high,
        loss_low,
        out_ref,
        mixed_ref,
    ) = refs[count:]
    f32 = jnp.float32
    for t in range(tile_blocks):
        lanes = slice(t * block_size, (t + 1) * block_size)
        acc = jnp.dot(own_ref[:, lanes], weight_ref[t, 0], preferred_element_type=f32)
        for k in range(neighbours):
            acc = acc + jnp.dot(
                picked[t * neighbours + k][...], weight_ref[t, k + 1], preferred_element_type=f32
            )
        mixed_ref[:, lanes] = acc
    mixed = mixed_ref[...]
    log_high, log_low = split3(jnp.log(mixed))
    exponent = dot3(order_high[...], order_low[...], log_high, log_low)
    rate = jnp.exp(prefactor_ref[...] - energy_ref[...] * temp_ref[...] + exponent)
    rate_high, rate_low = split3(rate)
    gained = dot3(prod_high[...], prod_low[...], rate_high, rate_low)
    lost_mass = dot3(loss_high[...], loss_low[...], rate_high, rate_low)
    out_ref[...] = (mixed + gained) / (1.0 + lost_mass / mixed)


def mix_react(
    table,
    neighbour_block,
    mix_weight,
    inverse_temp,
    reactant_order,
    log_prefactor,
    activation_energy,
    production,
    loss_coefficient,
):
    species = table.shape[0]
    count_blocks, _, block_size, _ = mix_weight.shape
    neighbours = neighbour_block.shape[1]
    reactions = reactant_order.shape[0]
    tile_blocks = TILE_BLOCKS
    width = tile_blocks * block_size
    steps = count_blocks // tile_blocks

    def picked_spec(t, k):
        return pl.BlockSpec(
            (species, block_size),
            lambda i, nb: (0, nb[(i * tile_blocks + t) * neighbours + k]),
        )

    def whole(shape):
        return pl.BlockSpec(shape, lambda i, nb: (0,) * len(shape))

    order_high, order_low = split3(reactant_order)
    prod_high, prod_low = split3(production)
    loss_high, loss_low = split3(loss_coefficient)
    in_specs = (
        [pl.BlockSpec((species, width), lambda i, nb: (0, i))]
        + [picked_spec(t, k) for t in range(tile_blocks) for k in range(neighbours)]
        + [
            pl.BlockSpec((tile_blocks,) + mix_weight.shape[1:], lambda i, nb: (i, 0, 0, 0)),
            pl.BlockSpec((1, width), lambda i, nb: (0, i)),
            whole(reactant_order.shape),
            whole(reactant_order.shape),
            whole((reactions, 1)),
            whole((reactions, 1)),
            whole(production.shape),
            whole(production.shape),
            whole(loss_coefficient.shape),
            whole(loss_coefficient.shape),
        ]
    )
    grid_spec = pltpu.PrefetchScalarGridSpec(
        num_scalar_prefetch=1,
        grid=(steps,),
        in_specs=in_specs,
        out_specs=pl.BlockSpec((species, width), lambda i, nb: (0, i)),
        scratch_shapes=[pltpu.VMEM((species, width), jnp.float32)],
    )
    kernel = functools.partial(mix_react_kernel, tile_blocks, neighbours, block_size)
    return pl.pallas_call(
        kernel,
        grid_spec=grid_spec,
        out_shape=jax.ShapeDtypeStruct((species, count_blocks * block_size), jnp.float32),
        compiler_params=pltpu.CompilerParams(dimension_semantics=("arbitrary",)),
    )(
        neighbour_block.reshape(-1),
        table,
        *([table] * (tile_blocks * neighbours)),
        mix_weight,
        inverse_temp.reshape(1, -1),
        order_high,
        order_low,
        log_prefactor.reshape(-1, 1),
        activation_energy.reshape(-1, 1),
        prod_high,
        prod_low,
        loss_high,
        loss_low,
    )


def shards(
    mixing_ratio,
    send_rows,
    migrant_count,
    arrival_slot,
    halo_blocks,
    neighbour_block,
    mix_weight,
    inverse_temp,
    reactant_order,
    log_prefactor,
    activation_energy,
    production,
    loss_coefficient,
):
    migrated = migrate(mixing_ratio, send_rows, migrant_count, arrival_slot)
    table = block_table(migrated, halo_blocks, mix_weight.shape[-1])
    return mix_react(
        table,
        neighbour_block,
        mix_weight,
        inverse_temp,
        reactant_order,
        log_prefactor,
        activation_energy,
        production,
        loss_coefficient,
    )


def solution(mesh):
    placed = (
        P(None, "region"),
        P("region", None, None),
        P("region", None),
        P("region", None, None),
        P("region", None, None),
        P("region", None),
        P("region", None, None, None),
        P("region"),
        P(),
        P(),
        P(),
        P(),
        P(),
    )
    return jax.shard_map(
        shards, mesh=mesh, in_specs=placed, out_specs=P(None, "region"), check_vma=False
    )
```

```python
import functools

import jax
import jax.numpy as jnp
from jax import lax
from jax.experimental import pallas as pl
from jax.experimental.pallas import tpu as pltpu
from jax.sharding import PartitionSpec as P

HOP = 4
TILE_BLOCKS = 4


def from_behind(block, axis, distance):
    devices = range(lax.axis_size(axis))
    route = [((i - distance) % len(devices), i) for i in devices]
    return lax.ppermute(block, axis, route)


def peer_offsets():
    return [column - HOP if column < HOP else column - HOP + 1 for column in range(2 * HOP)]


def one_hot(rows, size, axis):
    positions = lax.broadcasted_iota(jnp.int32, (size, rows.shape[0]), 0)
    if axis == 0:
        return (positions == rows[None, :]).astype(jnp.bfloat16)
    return (positions.T == rows[:, None]).astype(jnp.bfloat16)


def migrate(mixing_ratio, send_rows, migrant_count, arrival_slot):
    species, parcels = mixing_ratio.shape
    capacity = send_rows.shape[-1]
    offsets = peer_offsets()
    peer_count = len(offsets)
    f32 = jnp.float32
    pick = one_hot(send_rows[0].reshape(-1), parcels, 0)
    outgoing = jnp.dot(mixing_ratio, pick, preferred_element_type=f32).astype(jnp.bfloat16)
    outgoing = outgoing.reshape(species, peer_count, capacity)
    arrived = []
    for column in range(peer_count):
        opposite = peer_count - 1 - column
        arrived.append(from_behind(outgoing[:, opposite, :], "region", -offsets[column]))
    received = jnp.stack(arrived, axis=1).reshape(species, -1)
    lane_index = jnp.arange(capacity, dtype=jnp.int32)
    live_lane = lane_index[None, :] < migrant_count[0][:, None]
    target_slot = jnp.where(live_lane, arrival_slot[0], parcels).reshape(-1)
    place = one_hot(target_slot, parcels, 1)
    marked = jnp.concatenate([received, jnp.ones((1, received.shape[1]), received.dtype)], axis=0)
    placed = jnp.dot(marked, place, preferred_element_type=f32)
    hit = placed[species:] > 0.5
    return jnp.where(hit, placed[:species].astype(jnp.bfloat16), mixing_ratio)


def block_table(migrated, halo_blocks, block_size):
    species, parcels = migrated.shape
    blocks = migrated.reshape(species, parcels // block_size, block_size)
    to_lower = jnp.take(blocks, halo_blocks[0, 0], axis=1)
    to_upper = jnp.take(blocks, halo_blocks[0, 1], axis=1)
    from_lower = from_behind(to_upper, "region", 1)
    from_upper = from_behind(to_lower, "region", -1)
    return jnp.concatenate(
        [
            migrated,
            from_lower.reshape(species, -1),
            from_upper.reshape(species, -1),
        ],
        axis=1,
    )


def split3(x):
    high = x.astype(jnp.bfloat16)
    low = (x - high.astype(jnp.float32)).astype(jnp.bfloat16)
    return high, low


def dot3(a_high, a_low, b_high, b_low):
    f32 = jnp.float32
    total = jnp.dot(a_high, b_high, preferred_element_type=f32)
    total = total + jnp.dot(a_high, b_low, preferred_element_type=f32)
    return total + jnp.dot(a_low, b_high, preferred_element_type=f32)


def mix_react_kernel(tile_blocks, neighbours, block_size, nb_ref, own_ref, *refs):
    count = tile_blocks * neighbours
    picked = refs[:count]
    (
        weight_ref,
        temp_ref,
        order_ref,
        rate_terms_ref,
        prod_ref,
        loss_ref,
        out_ref,
        mixed_ref,
        order_split,
        prod_split,
        loss_split,
    ) = refs[count:]
    f32 = jnp.float32

    @pl.when(pl.program_id(0) == 0)
    def _():
        for source, target in ((order_ref, order_split), (prod_ref, prod_split), (loss_ref, loss_split)):
            high, low = split3(source[...])
            target[0] = high
            target[1] = low

    for t in range(tile_blocks):
        lanes = slice(t * block_size, (t + 1) * block_size)
        acc = jnp.dot(own_ref[:, lanes], weight_ref[t, 0], preferred_element_type=f32)
        for k in range(neighbours):
            acc = acc + jnp.dot(
                picked[t * neighbours + k][...], weight_ref[t, k + 1], preferred_element_type=f32
            )
        mixed_ref[:, lanes] = acc
    mixed = mixed_ref[...]
    log_high, log_low = split3(jnp.log(mixed))
    exponent = dot3(order_split[0], order_split[1], log_high, log_low)
    prefactor = rate_terms_ref[:, 0:1]
    energy = rate_terms_ref[:, 1:2]
    rate = jnp.exp(prefactor - energy * temp_ref[...] + exponent)
    rate_high, rate_low = split3(rate)
    gained = dot3(prod_split[0], prod_split[1], rate_high, rate_low)
    lost_mass = dot3(loss_split[0], loss_split[1], rate_high, rate_low)
    out_ref[...] = (mixed + gained) / (1.0 + lost_mass / mixed)


def mix_react(
    table,
    neighbour_block,
    mix_weight,
    inverse_temp,
    reactant_order,
    log_prefactor,
    activation_energy,
    production,
    loss_coefficient,
):
    species = table.shape[0]
    count_blocks, _, block_size, _ = mix_weight.shape
    neighbours = neighbour_block.shape[1]
    reactions = reactant_order.shape[0]
    tile_blocks = TILE_BLOCKS
    width = tile_blocks * block_size
    steps = count_blocks // tile_blocks

    def picked_spec(t, k):
        return pl.BlockSpec(
            (species, block_size),
            lambda i, nb: (0, nb[i * tile_blocks + t, k]),
        )

    def whole(shape):
        return pl.BlockSpec(shape, lambda i, nb: (0,) * len(shape))

    in_specs = (
        [pl.BlockSpec((species, width), lambda i, nb: (0, i))]
        + [picked_spec(t, k) for t in range(tile_blocks) for k in range(neighbours)]
        + [
            pl.BlockSpec((tile_blocks,) + mix_weight.shape[1:], lambda i, nb: (i, 0, 0, 0)),
            pl.BlockSpec((1, width), lambda i, nb: (0, i)),
            whole(reactant_order.shape),
            whole((reactions, 2)),
            whole(production.shape),
            whole(loss_coefficient.shape),
        ]
    )
    bf16 = jnp.bfloat16
    grid_spec = pltpu.PrefetchScalarGridSpec(
        num_scalar_prefetch=1,
        grid=(steps,),
        in_specs=in_specs,
        out_specs=pl.BlockSpec((species, width), lambda i, nb: (0, i)),
        scratch_shapes=[
            pltpu.VMEM((species, width), jnp.float32),
            pltpu.VMEM((2,) + reactant_order.shape, bf16),
            pltpu.VMEM((2,) + production.shape, bf16),
            pltpu.VMEM((2,) + loss_coefficient.shape, bf16),
        ],
    )
    kernel = functools.partial(mix_react_kernel, tile_blocks, neighbours, block_size)
    return pl.pallas_call(
        kernel,
        grid_spec=grid_spec,
        out_shape=jax.ShapeDtypeStruct((species, count_blocks * block_size), jnp.float32),
        compiler_params=pltpu.CompilerParams(dimension_semantics=("arbitrary",)),
    )(
        neighbour_block,
        table,
        *([table] * (tile_blocks * neighbours)),
        mix_weight,
        inverse_temp.reshape(1, -1),
        reactant_order,
        jnp.stack([log_prefactor, activation_energy], axis=1),
        production,
        loss_coefficient,
    )


def shards(
    mixing_ratio,
    send_rows,
    migrant_count,
    arrival_slot,
    halo_blocks,
    neighbour_block,
    mix_weight,
    inverse_temp,
    reactant_order,
    log_prefactor,
    activation_energy,
    production,
    loss_coefficient,
):
    migrated = migrate(mixing_ratio, send_rows, migrant_count, arrival_slot)
    table = block_table(migrated, halo_blocks, mix_weight.shape[-1])
    return mix_react(
        table,
        neighbour_block,
        mix_weight,
        inverse_temp,
        reactant_order,
        log_prefactor,
        activation_energy,
        production,
        loss_coefficient,
    )


def solution(mesh):
    placed = (
        P(None, "region"),
        P("region", None, None),
        P("region", None),
        P("region", None, None),
        P("region", None, None),
        P("region", None),
        P("region", None, None, None),
        P("region"),
        P(),
        P(),
        P(),
        P(),
        P(),
    )
    return jax.shard_map(
        shards, mesh=mesh, in_specs=placed, out_specs=P(None, "region"), check_vma=False
    )
```

```python
import functools

import jax
import jax.numpy as jnp
from jax import lax
from jax.experimental import pallas as pl
from jax.experimental.pallas import tpu as pltpu
from jax.sharding import PartitionSpec as P

HOP = 4
TILE_BLOCKS = 4


def from_behind(block, axis, distance):
    devices = range(lax.axis_size(axis))
    route = [((i - distance) % len(devices), i) for i in devices]
    return lax.ppermute(block, axis, route)


def peer_offsets():
    return [column - HOP if column < HOP else column - HOP + 1 for column in range(2 * HOP)]


def one_hot(rows, size, axis):
    positions = lax.broadcasted_iota(jnp.int32, (size, rows.shape[0]), 0)
    if axis == 0:
        return (positions == rows[None, :]).astype(jnp.bfloat16)
    return (positions.T == rows[:, None]).astype(jnp.bfloat16)


def migrate(mixing_ratio, send_rows, migrant_count, arrival_slot):
    species, parcels = mixing_ratio.shape
    capacity = send_rows.shape[-1]
    offsets = peer_offsets()
    peer_count = len(offsets)
    f32 = jnp.float32
    pick = one_hot(send_rows[0].reshape(-1), parcels, 0)
    outgoing = jnp.dot(mixing_ratio, pick, preferred_element_type=f32).astype(jnp.bfloat16)
    outgoing = outgoing.reshape(species, peer_count, capacity)
    arrived = []
    for column in range(peer_count):
        opposite = peer_count - 1 - column
        arrived.append(from_behind(outgoing[:, opposite, :], "region", -offsets[column]))
    received = jnp.stack(arrived, axis=1).reshape(species, -1)
    lane_index = jnp.arange(capacity, dtype=jnp.int32)
    live_lane = lane_index[None, :] < migrant_count[0][:, None]
    target_slot = jnp.where(live_lane, arrival_slot[0], parcels).reshape(-1)
    place = one_hot(target_slot, parcels, 1)
    marked = jnp.concatenate([received, jnp.ones((1, received.shape[1]), received.dtype)], axis=0)
    placed = jnp.dot(marked, place, preferred_element_type=f32)
    hit = placed[species:] > 0.5
    return jnp.where(hit, placed[:species].astype(jnp.bfloat16), mixing_ratio)


def halo_kernel(block_size, halo_ref, migrated_hbm, out_hbm, sems):
    sides, listed = halo_ref.shape
    copies = []
    for side in range(sides):
        for j in range(listed):
            start = pl.multiple_of(halo_ref[side, j] * block_size, block_size)
            copy = pltpu.make_async_copy(
                migrated_hbm.at[:, pl.ds(start, block_size)],
                out_hbm.at[side, :, pl.ds(j * block_size, block_size)],
                sems.at[side, j],
            )
            copy.start()
            copies.append(copy)
    for copy in copies:
        copy.wait()


def halo_exchange(migrated, halo_blocks, block_size):
    species = migrated.shape[0]
    sides, listed = halo_blocks.shape[1:]
    grid_spec = pltpu.PrefetchScalarGridSpec(
        num_scalar_prefetch=1,
        grid=(1,),
        in_specs=[pl.BlockSpec(memory_space=pl.ANY)],
        out_specs=pl.BlockSpec(memory_space=pl.ANY),
        scratch_shapes=[pltpu.SemaphoreType.DMA((sides, listed))],
    )
    listed_blocks = pl.pallas_call(
        functools.partial(halo_kernel, block_size),
        grid_spec=grid_spec,
        out_shape=jax.ShapeDtypeStruct((sides, species, listed * block_size), migrated.dtype),
    )(halo_blocks[0], migrated)
    from_lower = from_behind(listed_blocks[1], "region", 1)
    from_upper = from_behind(listed_blocks[0], "region", -1)
    return from_lower, from_upper


def split3(x):
    high = x.astype(jnp.bfloat16)
    low = (x - high.astype(jnp.float32)).astype(jnp.bfloat16)
    return high, low


def dot3(a_high, a_low, b_high, b_low):
    f32 = jnp.float32
    total = jnp.dot(a_high, b_high, preferred_element_type=f32)
    total = total + jnp.dot(a_high, b_low, preferred_element_type=f32)
    return total + jnp.dot(a_low, b_high, preferred_element_type=f32)


def mix_react_kernel(
    tile_blocks,
    neighbours,
    block_size,
    nb_ref,
    own_ref,
    weight_ref,
    temp_ref,
    order_ref,
    rate_terms_ref,
    prod_ref,
    loss_ref,
    migrated_hbm,
    lower_hbm,
    upper_hbm,
    out_ref,
    picked,
    sems,
    mixed_ref,
    order_split,
    prod_split,
    loss_split,
):
    f32 = jnp.float32
    step = pl.program_id(0)
    steps = pl.num_programs(0)
    own_count = migrated_hbm.shape[1] // block_size
    halo_count = lower_hbm.shape[1] // block_size

    def fetch(at, slot, start):
        for t in range(tile_blocks):
            for k in range(neighbours):
                index = nb_ref[at * tile_blocks + t, k]
                target = picked.at[slot, t * neighbours + k]
                sem = sems.at[slot, t * neighbours + k]
                if not start:
                    pltpu.make_async_copy(
                        migrated_hbm.at[:, pl.ds(0, block_size)], target, sem
                    ).wait()
                    continue
                sources = (
                    (migrated_hbm, index, index < own_count),
                    (lower_hbm, index - own_count,
                     (index >= own_count) & (index < own_count + halo_count)),
                    (upper_hbm, index - own_count - halo_count,
                     index >= own_count + halo_count),
                )
                for source, local, chosen in sources:
                    limit = source.shape[1] // block_size - 1
                    local = jnp.minimum(jnp.maximum(local, 0), limit)

                    @pl.when(chosen)
                    def _():
                        begin = pl.multiple_of(local * block_size, block_size)
                        pltpu.make_async_copy(
                            source.at[:, pl.ds(begin, block_size)], target, sem
                        ).start()

    @pl.when(step == 0)
    def _():
        fetch(0, 0, True)
        for source, target in ((order_ref, order_split), (prod_ref, prod_split), (loss_ref, loss_split)):
            high, low = split3(source[...])
            target[0] = high
            target[1] = low

    slot = step % 2

    @pl.when(step + 1 < steps)
    def _():
        fetch(step + 1, 1 - slot, True)

    fetch(step, slot, False)

    for t in range(tile_blocks):
        lanes = slice(t * block_size, (t + 1) * block_size)
        acc = jnp.dot(own_ref[:, lanes], weight_ref[t, 0], preferred_element_type=f32)
        for k in range(neighbours):
            acc = acc + jnp.dot(
                picked[slot, t * neighbours + k], weight_ref[t, k + 1], preferred_element_type=f32
            )
        mixed_ref[:, lanes] = acc
    mixed = mixed_ref[...]
    log_high, log_low = split3(jnp.log(mixed))
    exponent = dot3(order_split[0], order_split[1], log_high, log_low)
    prefactor = rate_terms_ref[:, 0:1]
    energy = rate_terms_ref[:, 1:2]
    rate = jnp.exp(prefactor - energy * temp_ref[...] + exponent)
    rate_high, rate_low = split3(rate)
    gained = dot3(prod_split[0], prod_split[1], rate_high, rate_low)
    lost_mass = dot3(loss_split[0], loss_split[1], rate_high, rate_low)
    out_ref[...] = (mixed + gained) / (1.0 + lost_mass / mixed)


def mix_react(
    migrated,
    from_lower,
    from_upper,
    neighbour_block,
    mix_weight,
    inverse_temp,
    reactant_order,
    log_prefactor,
    activation_energy,
    production,
    loss_coefficient,
):
    species = migrated.shape[0]
    count_blocks, _, block_size, _ = mix_weight.shape
    neighbours = neighbour_block.shape[1]
    reactions = reactant_order.shape[0]
    tile_blocks = TILE_BLOCKS
    width = tile_blocks * block_size
    steps = count_blocks // tile_blocks

    def whole(shape):
        return pl.BlockSpec(shape, lambda i, nb: (0,) * len(shape))

    in_specs = [
        pl.BlockSpec((species, width), lambda i, nb: (0, i)),
        pl.BlockSpec((tile_blocks,) + mix_weight.shape[1:], lambda i, nb: (i, 0, 0, 0)),
        pl.BlockSpec((1, width), lambda i, nb: (0, i)),
        whole(reactant_order.shape),
        whole((reactions, 2)),
        whole(production.shape),
        whole(loss_coefficient.shape),
        pl.BlockSpec(memory_space=pl.ANY),
        pl.BlockSpec(memory_space=pl.ANY),
        pl.BlockSpec(memory_space=pl.ANY),
    ]
    bf16 = jnp.bfloat16
    grid_spec = pltpu.PrefetchScalarGridSpec(
        num_scalar_prefetch=1,
        grid=(steps,),
        in_specs=in_specs,
        out_specs=pl.BlockSpec((species, width), lambda i, nb: (0, i)),
        scratch_shapes=[
            pltpu.VMEM((2, tile_blocks * neighbours, species, block_size), bf16),
            pltpu.SemaphoreType.DMA((2, tile_blocks * neighbours)),
            pltpu.VMEM((species, width), jnp.float32),
            pltpu.VMEM((2,) + reactant_order.shape, bf16),
            pltpu.VMEM((2,) + production.shape, bf16),
            pltpu.VMEM((2,) + loss_coefficient.shape, bf16),
        ],
    )
    kernel = functools.partial(mix_react_kernel, tile_blocks, neighbours, block_size)
    return pl.pallas_call(
        kernel,
        grid_spec=grid_spec,
        out_shape=jax.ShapeDtypeStruct((species, count_blocks * block_size), jnp.float32),
        compiler_params=pltpu.CompilerParams(dimension_semantics=("arbitrary",)),
    )(
        neighbour_block,
        migrated,
        mix_weight,
        inverse_temp.reshape(1, -1),
        reactant_order,
        jnp.stack([log_prefactor, activation_energy], axis=1),
        production,
        loss_coefficient,
        migrated,
        from_lower,
        from_upper,
    )


def shards(
    mixing_ratio,
    send_rows,
    migrant_count,
    arrival_slot,
    halo_blocks,
    neighbour_block,
    mix_weight,
    inverse_temp,
    reactant_order,
    log_prefactor,
    activation_energy,
    production,
    loss_coefficient,
):
    migrated = migrate(mixing_ratio, send_rows, migrant_count, arrival_slot)
    from_lower, from_upper = halo_exchange(migrated, halo_blocks, mix_weight.shape[-1])
    return mix_react(
        migrated,
        from_lower,
        from_upper,
        neighbour_block,
        mix_weight,
        inverse_temp,
        reactant_order,
        log_prefactor,
        activation_energy,
        production,
        loss_coefficient,
    )


def solution(mesh):
    placed = (
        P(None, "region"),
        P("region", None, None),
        P("region", None),
        P("region", None, None),
        P("region", None, None),
        P("region", None),
        P("region", None, None, None),
        P("region"),
        P(),
        P(),
        P(),
        P(),
        P(),
    )
    return jax.shard_map(
        shards, mesh=mesh, in_specs=placed, out_specs=P(None, "region"), check_vma=False
    )
```

```python
import functools

import jax
import jax.numpy as jnp
from jax import lax
from jax.experimental import pallas as pl
from jax.experimental.pallas import tpu as pltpu
from jax.sharding import PartitionSpec as P

HOP = 4
TILE_BLOCKS = 4


def from_behind(block, axis, distance):
    devices = range(lax.axis_size(axis))
    route = [((i - distance) % len(devices), i) for i in devices]
    return lax.ppermute(block, axis, route)


def peer_offsets():
    return [column - HOP if column < HOP else column - HOP + 1 for column in range(2 * HOP)]


def one_hot(rows, size, axis):
    positions = lax.broadcasted_iota(jnp.int32, (size, rows.shape[0]), 0)
    if axis == 0:
        return (positions == rows[None, :]).astype(jnp.bfloat16)
    return (positions.T == rows[:, None]).astype(jnp.bfloat16)


def migrate(mixing_ratio, send_rows, migrant_count, arrival_slot):
    species, parcels = mixing_ratio.shape
    capacity = send_rows.shape[-1]
    offsets = peer_offsets()
    peer_count = len(offsets)
    f32 = jnp.float32
    pick = one_hot(send_rows[0].reshape(-1), parcels, 0)
    outgoing = jnp.dot(mixing_ratio, pick, preferred_element_type=f32).astype(jnp.bfloat16)
    outgoing = outgoing.reshape(species, peer_count, capacity)
    arrived = []
    for column in range(peer_count):
        opposite = peer_count - 1 - column
        arrived.append(from_behind(outgoing[:, opposite, :], "region", -offsets[column]))
    received = jnp.stack(arrived, axis=1).reshape(species, -1)
    lane_index = jnp.arange(capacity, dtype=jnp.int32)
    live_lane = lane_index[None, :] < migrant_count[0][:, None]
    target_slot = jnp.where(live_lane, arrival_slot[0], parcels).reshape(-1)
    place = one_hot(target_slot, parcels, 1)
    marked = jnp.concatenate([received, jnp.ones((1, received.shape[1]), received.dtype)], axis=0)
    placed = jnp.dot(marked, place, preferred_element_type=f32)
    hit = placed[species:] > 0.5
    return jnp.where(hit, placed[:species].astype(jnp.bfloat16), mixing_ratio)


def halo_kernel(block_size, halo_ref, migrated_hbm, out_hbm, sems):
    sides, listed = halo_ref.shape
    copies = []
    for side in range(sides):
        for j in range(listed):
            start = pl.multiple_of(halo_ref[side, j] * block_size, block_size)
            copy = pltpu.make_async_copy(
                migrated_hbm.at[:, pl.ds(start, block_size)],
                out_hbm.at[side, :, pl.ds(j * block_size, block_size)],
                sems.at[side, j],
            )
            copy.start()
            copies.append(copy)
    for copy in copies:
        copy.wait()


def halo_exchange(migrated, halo_blocks, block_size):
    species = migrated.shape[0]
    sides, listed = halo_blocks.shape[1:]
    grid_spec = pltpu.PrefetchScalarGridSpec(
        num_scalar_prefetch=1,
        grid=(1,),
        in_specs=[pl.BlockSpec(memory_space=pl.ANY)],
        out_specs=pl.BlockSpec(
            (sides, species, listed * block_size), lambda i, halo: (0, 0, 0)
        ),
        scratch_shapes=[pltpu.SemaphoreType.DMA((sides, listed))],
    )
    listed_blocks = pl.pallas_call(
        functools.partial(halo_kernel, block_size),
        grid_spec=grid_spec,
        out_shape=jax.ShapeDtypeStruct((sides, species, listed * block_size), migrated.dtype),
    )(halo_blocks[0], migrated)
    from_lower = from_behind(listed_blocks[1], "region", 1)
    from_upper = from_behind(listed_blocks[0], "region", -1)
    return from_lower, from_upper


def split3(x):
    high = x.astype(jnp.bfloat16)
    low = (x - high.astype(jnp.float32)).astype(jnp.bfloat16)
    return high, low


def dot3(a_high, a_low, b_high, b_low):
    f32 = jnp.float32
    total = jnp.dot(a_high, b_high, preferred_element_type=f32)
    total = total + jnp.dot(a_high, b_low, preferred_element_type=f32)
    return total + jnp.dot(a_low, b_high, preferred_element_type=f32)


def mix_react_kernel(
    tile_blocks,
    neighbours,
    block_size,
    nb_ref,
    own_ref,
    weight_ref,
    temp_ref,
    order_ref,
    rate_terms_ref,
    prod_ref,
    loss_ref,
    migrated_hbm,
    lower_hbm,
    upper_hbm,
    out_ref,
    picked,
    sems,
    mixed_ref,
    order_split,
    prod_split,
    loss_split,
):
    f32 = jnp.float32
    step = pl.program_id(0)
    steps = pl.num_programs(0)
    own_count = migrated_hbm.shape[1] // block_size
    halo_count = lower_hbm.shape[1] // block_size

    def fetch(at, slot, start):
        for t in range(tile_blocks):
            for k in range(neighbours):
                index = nb_ref[at * tile_blocks + t, k]
                target = picked.at[slot, t * neighbours + k]
                sem = sems.at[slot, t * neighbours + k]
                if not start:
                    pltpu.make_async_copy(
                        migrated_hbm.at[:, pl.ds(0, block_size)], target, sem
                    ).wait()
                    continue
                sources = (
                    (migrated_hbm, index, index < own_count),
                    (lower_hbm, index - own_count,
                     (index >= own_count) & (index < own_count + halo_count)),
                    (upper_hbm, index - own_count - halo_count,
                     index >= own_count + halo_count),
                )
                for source, local, chosen in sources:
                    limit = source.shape[1] // block_size - 1
                    local = jnp.minimum(jnp.maximum(local, 0), limit)

                    @pl.when(chosen)
                    def _():
                        begin = pl.multiple_of(local * block_size, block_size)
                        pltpu.make_async_copy(
                            source.at[:, pl.ds(begin, block_size)], target, sem
                        ).start()

    @pl.when(step == 0)
    def _():
        fetch(0, 0, True)
        for source, target in ((order_ref, order_split), (prod_ref, prod_split), (loss_ref, loss_split)):
            high, low = split3(source[...])
            target[0] = high
            target[1] = low

    slot = step % 2

    @pl.when(step + 1 < steps)
    def _():
        fetch(step + 1, 1 - slot, True)

    fetch(step, slot, False)

    for t in range(tile_blocks):
        lanes = slice(t * block_size, (t + 1) * block_size)
        acc = jnp.dot(own_ref[:, lanes], weight_ref[t, 0], preferred_element_type=f32)
        for k in range(neighbours):
            acc = acc + jnp.dot(
                picked[slot, t * neighbours + k], weight_ref[t, k + 1], preferred_element_type=f32
            )
        mixed_ref[:, lanes] = acc
    mixed = mixed_ref[...]
    log_high, log_low = split3(jnp.log(mixed))
    exponent = dot3(order_split[0], order_split[1], log_high, log_low)
    prefactor = rate_terms_ref[:, 0:1]
    energy = rate_terms_ref[:, 1:2]
    rate = jnp.exp(prefactor - energy * temp_ref[...] + exponent)
    rate_high, rate_low = split3(rate)
    gained = dot3(prod_split[0], prod_split[1], rate_high, rate_low)
    lost_mass = dot3(loss_split[0], loss_split[1], rate_high, rate_low)
    out_ref[...] = (mixed + gained) / (1.0 + lost_mass / mixed)


def mix_react(
    migrated,
    from_lower,
    from_upper,
    neighbour_block,
    mix_weight,
    inverse_temp,
    reactant_order,
    log_prefactor,
    activation_energy,
    production,
    loss_coefficient,
):
    species = migrated.shape[0]
    count_blocks, _, block_size, _ = mix_weight.shape
    neighbours = neighbour_block.shape[1]
    reactions = reactant_order.shape[0]
    tile_blocks = TILE_BLOCKS
    width = tile_blocks * block_size
    steps = count_blocks // tile_blocks

    def whole(shape):
        return pl.BlockSpec(shape, lambda i, nb: (0,) * len(shape))

    in_specs = [
        pl.BlockSpec((species, width), lambda i, nb: (0, i)),
        pl.BlockSpec((tile_blocks,) + mix_weight.shape[1:], lambda i, nb: (i, 0, 0, 0)),
        pl.BlockSpec((1, width), lambda i, nb: (0, i)),
        whole(reactant_order.shape),
        whole((reactions, 2)),
        whole(production.shape),
        whole(loss_coefficient.shape),
        pl.BlockSpec(memory_space=pl.ANY),
        pl.BlockSpec(memory_space=pl.ANY),
        pl.BlockSpec(memory_space=pl.ANY),
    ]
    bf16 = jnp.bfloat16
    grid_spec = pltpu.PrefetchScalarGridSpec(
        num_scalar_prefetch=1,
        grid=(steps,),
        in_specs=in_specs,
        out_specs=pl.BlockSpec((species, width), lambda i, nb: (0, i)),
        scratch_shapes=[
            pltpu.VMEM((2, tile_blocks * neighbours, species, block_size), bf16),
            pltpu.SemaphoreType.DMA((2, tile_blocks * neighbours)),
            pltpu.VMEM((species, width), jnp.float32),
            pltpu.VMEM((2,) + reactant_order.shape, bf16),
            pltpu.VMEM((2,) + production.shape, bf16),
            pltpu.VMEM((2,) + loss_coefficient.shape, bf16),
        ],
    )
    kernel = functools.partial(mix_react_kernel, tile_blocks, neighbours, block_size)
    return pl.pallas_call(
        kernel,
        grid_spec=grid_spec,
        out_shape=jax.ShapeDtypeStruct((species, count_blocks * block_size), jnp.float32),
        compiler_params=pltpu.CompilerParams(dimension_semantics=("arbitrary",)),
    )(
        neighbour_block,
        migrated,
        mix_weight,
        inverse_temp.reshape(1, -1),
        reactant_order,
        jnp.stack([log_prefactor, activation_energy], axis=1),
        production,
        loss_coefficient,
        migrated,
        from_lower,
        from_upper,
    )


def shards(
    mixing_ratio,
    send_rows,
    migrant_count,
    arrival_slot,
    halo_blocks,
    neighbour_block,
    mix_weight,
    inverse_temp,
    reactant_order,
    log_prefactor,
    activation_energy,
    production,
    loss_coefficient,
):
    migrated = migrate(mixing_ratio, send_rows, migrant_count, arrival_slot)
    from_lower, from_upper = halo_exchange(migrated, halo_blocks, mix_weight.shape[-1])
    return mix_react(
        migrated,
        from_lower,
        from_upper,
        neighbour_block,
        mix_weight,
        inverse_temp,
        reactant_order,
        log_prefactor,
        activation_energy,
        production,
        loss_coefficient,
    )


def solution(mesh):
    placed = (
        P(None, "region"),
        P("region", None, None),
        P("region", None),
        P("region", None, None),
        P("region", None, None),
        P("region", None),
        P("region", None, None, None),
        P("region"),
        P(),
        P(),
        P(),
        P(),
        P(),
    )
    return jax.shard_map(
        shards, mesh=mesh, in_specs=placed, out_specs=P(None, "region"), check_vma=False
    )
```

```python
import functools

import jax
import jax.numpy as jnp
from jax import lax
from jax.experimental import pallas as pl
from jax.experimental.pallas import tpu as pltpu
from jax.sharding import PartitionSpec as P

HOP = 4
TILE_BLOCKS = 8
PAD_ROWS = 160


def from_behind(block, axis, distance):
    devices = range(lax.axis_size(axis))
    route = [((i - distance) % len(devices), i) for i in devices]
    return lax.ppermute(block, axis, route)


def peer_offsets():
    return [column - HOP if column < HOP else column - HOP + 1 for column in range(2 * HOP)]


def one_hot(rows, size, axis):
    positions = lax.broadcasted_iota(jnp.int32, (size, rows.shape[0]), 0)
    if axis == 0:
        return (positions == rows[None, :]).astype(jnp.bfloat16)
    return (positions.T == rows[:, None]).astype(jnp.bfloat16)


def migrate(mixing_ratio, send_rows, migrant_count, arrival_slot):
    species, parcels = mixing_ratio.shape
    capacity = send_rows.shape[-1]
    offsets = peer_offsets()
    peer_count = len(offsets)
    f32 = jnp.float32
    pick = one_hot(send_rows[0].reshape(-1), parcels, 0)
    outgoing = jnp.dot(mixing_ratio, pick, preferred_element_type=f32).astype(jnp.bfloat16)
    outgoing = outgoing.reshape(species, peer_count, capacity)
    arrived = []
    for column in range(peer_count):
        opposite = peer_count - 1 - column
        arrived.append(from_behind(outgoing[:, opposite, :], "region", -offsets[column]))
    received = jnp.stack(arrived, axis=1).reshape(species, -1)
    lane_index = jnp.arange(capacity, dtype=jnp.int32)
    live_lane = lane_index[None, :] < migrant_count[0][:, None]
    target_slot = jnp.where(live_lane, arrival_slot[0], parcels).reshape(-1)
    place = one_hot(target_slot, parcels, 1)
    marked = jnp.concatenate([received, jnp.ones((1, received.shape[1]), received.dtype)], axis=0)
    placed = jnp.dot(marked, place, preferred_element_type=f32)
    hit = placed[species:] > 0.5
    return jnp.where(hit, placed[:species].astype(jnp.bfloat16), mixing_ratio)


def halo_kernel(block_size, halo_ref, migrated_hbm, lower_ref, upper_ref, sems):
    sides, listed = halo_ref.shape
    outs = (lower_ref, upper_ref)
    copies = []
    for side in range(sides):
        for j in range(listed):
            start = pl.multiple_of(halo_ref[side, j] * block_size, block_size)
            copy = pltpu.make_async_copy(
                migrated_hbm.at[:, pl.ds(start, block_size)],
                outs[side].at[:, pl.ds(j * block_size, block_size)],
                sems.at[side, j],
            )
            copy.start()
            copies.append(copy)
    for copy in copies:
        copy.wait()


def halo_exchange(migrated, halo_blocks, block_size):
    species = migrated.shape[0]
    sides, listed = halo_blocks.shape[1:]
    grid_spec = pltpu.PrefetchScalarGridSpec(
        num_scalar_prefetch=1,
        grid=(1,),
        in_specs=[pl.BlockSpec(memory_space=pl.ANY)],
        out_specs=[
            pl.BlockSpec((species, listed * block_size), lambda i, halo: (0, 0))
        ] * sides,
        scratch_shapes=[pltpu.SemaphoreType.DMA((sides, listed))],
    )
    listed_blocks = pl.pallas_call(
        functools.partial(halo_kernel, block_size),
        grid_spec=grid_spec,
        out_shape=[jax.ShapeDtypeStruct((species, listed * block_size), migrated.dtype)] * sides,
    )(halo_blocks[0], migrated)
    from_lower = from_behind(listed_blocks[1], "region", 1)
    from_upper = from_behind(listed_blocks[0], "region", -1)
    return from_lower, from_upper


def split3(x):
    high = x.astype(jnp.bfloat16)
    low = (x - high.astype(jnp.float32)).astype(jnp.bfloat16)
    return high, low


def dot3(a_high, a_low, b_high, b_low):
    f32 = jnp.float32
    total = jnp.dot(a_high, b_high, preferred_element_type=f32)
    total = total + jnp.dot(a_high, b_low, preferred_element_type=f32)
    return total + jnp.dot(a_low, b_high, preferred_element_type=f32)


def mix_react_kernel(
    tile_blocks,
    neighbours,
    block_size,
    nb_ref,
    own_ref,
    weight_ref,
    temp_ref,
    order_ref,
    rate_terms_ref,
    prod_ref,
    loss_ref,
    migrated_hbm,
    lower_hbm,
    upper_hbm,
    out_ref,
    picked,
    sems,
    mixed_ref,
    order_split,
    gain_split,
    gain_high,
):
    f32 = jnp.float32
    step = pl.program_id(0)
    steps = pl.num_programs(0)
    own_count = migrated_hbm.shape[1] // block_size
    halo_count = lower_hbm.shape[1] // block_size

    def fetch(at, slot, start):
        for t in range(tile_blocks):
            for k in range(neighbours):
                index = nb_ref[at * tile_blocks + t, k]
                target = picked.at[slot, t * neighbours + k]
                sem = sems.at[slot, t * neighbours + k]
                if not start:
                    pltpu.make_async_copy(
                        migrated_hbm.at[:, pl.ds(0, block_size)], target, sem
                    ).wait()
                    continue
                sources = (
                    (migrated_hbm, index, index < own_count),
                    (lower_hbm, index - own_count,
                     (index >= own_count) & (index < own_count + halo_count)),
                    (upper_hbm, index - own_count - halo_count,
                     index >= own_count + halo_count),
                )
                for source, local, chosen in sources:
                    limit = source.shape[1] // block_size - 1
                    local = jnp.minimum(jnp.maximum(local, 0), limit)

                    @pl.when(chosen)
                    def _():
                        begin = pl.multiple_of(local * block_size, block_size)
                        pltpu.make_async_copy(
                            source.at[:, pl.ds(begin, block_size)], target, sem
                        ).start()

    @pl.when(step == 0)
    def _():
        fetch(0, 0, True)
        order_high, order_low = split3(order_ref[...])
        reactions = order_high.shape[0]
        order_split[0:reactions] = order_high
        order_split[reactions:] = order_low
        gain_split[...] = jnp.zeros_like(gain_split)
        rows = prod_ref.shape[0]
        for part, source in enumerate((prod_ref, loss_ref)):
            high, low = split3(source[...])
            gain_split[pl.ds(2 * part * PAD_ROWS, rows)] = high
            gain_split[pl.ds((2 * part + 1) * PAD_ROWS, rows)] = low
            gain_high[pl.ds(part * PAD_ROWS, rows)] = high
        gain_high[...] = jnp.where(
            lax.broadcasted_iota(jnp.int32, gain_high.shape, 0) % PAD_ROWS < rows,
            gain_high[...],
            jnp.zeros_like(gain_high),
        )

    slot = step % 2

    @pl.when(step + 1 < steps)
    def _():
        fetch(step + 1, 1 - slot, True)

    fetch(step, slot, False)

    for t in range(tile_blocks):
        lanes = slice(t * block_size, (t + 1) * block_size)
        stacked = jnp.concatenate(
            [own_ref[:, lanes]] + [picked[slot, t * neighbours + k] for k in range(neighbours)],
            axis=1,
        )
        weight = weight_ref[t].reshape((neighbours + 1) * block_size, block_size)
        mixed_ref[:, lanes] = jnp.dot(stacked, weight, preferred_element_type=f32)
    mixed = mixed_ref[...]
    species = mixed.shape[0]
    log_high, log_low = split3(jnp.log(mixed))
    reactions = order_split.shape[0] // 2
    both = jnp.dot(order_split[...], log_high, preferred_element_type=f32)
    exponent = both[:reactions] + both[reactions:]
    exponent = exponent + jnp.dot(order_split[0:reactions], log_low, preferred_element_type=f32)
    prefactor = rate_terms_ref[:, 0:1]
    energy = rate_terms_ref[:, 1:2]
    rate = jnp.exp(prefactor - energy * temp_ref[...] + exponent)
    rate_high, rate_low = split3(rate)
    by_high = jnp.dot(gain_split[...], rate_high, preferred_element_type=f32)
    by_low = jnp.dot(gain_high[...], rate_low, preferred_element_type=f32)
    gained = by_high[0:species] + by_high[PAD_ROWS:PAD_ROWS + species] + by_low[0:species]
    lost_mass = (
        by_high[2 * PAD_ROWS:2 * PAD_ROWS + species]
        + by_high[3 * PAD_ROWS:3 * PAD_ROWS + species]
        + by_low[PAD_ROWS:PAD_ROWS + species]
    )
    out_ref[...] = (mixed + gained) / (1.0 + lost_mass / mixed)


def mix_react(
    migrated,
    from_lower,
    from_upper,
    neighbour_block,
    mix_weight,
    inverse_temp,
    reactant_order,
    log_prefactor,
    activation_energy,
    production,
    loss_coefficient,
):
    species = migrated.shape[0]
    count_blocks, _, block_size, _ = mix_weight.shape
    neighbours = neighbour_block.shape[1]
    reactions = reactant_order.shape[0]
    tile_blocks = TILE_BLOCKS
    width = tile_blocks * block_size
    steps = count_blocks // tile_blocks

    def whole(shape):
        return pl.BlockSpec(shape, lambda i, nb: (0,) * len(shape))

    in_specs = [
        pl.BlockSpec((species, width), lambda i, nb: (0, i)),
        pl.BlockSpec((tile_blocks,) + mix_weight.shape[1:], lambda i, nb: (i, 0, 0, 0)),
        pl.BlockSpec((1, width), lambda i, nb: (0, i)),
        whole(reactant_order.shape),
        whole((reactions, 2)),
        whole(production.shape),
        whole(loss_coefficient.shape),
        pl.BlockSpec(memory_space=pl.ANY),
        pl.BlockSpec(memory_space=pl.ANY),
        pl.BlockSpec(memory_space=pl.ANY),
    ]
    bf16 = jnp.bfloat16
    grid_spec = pltpu.PrefetchScalarGridSpec(
        num_scalar_prefetch=1,
        grid=(steps,),
        in_specs=in_specs,
        out_specs=pl.BlockSpec((species, width), lambda i, nb: (0, i)),
        scratch_shapes=[
            pltpu.VMEM((2, tile_blocks * neighbours, species, block_size), bf16),
            pltpu.SemaphoreType.DMA((2, tile_blocks * neighbours)),
            pltpu.VMEM((species, width), jnp.float32),
            pltpu.VMEM((2 * reactions, species), bf16),
            pltpu.VMEM((4 * PAD_ROWS, reactions), bf16),
            pltpu.VMEM((2 * PAD_ROWS, reactions), bf16),
        ],
    )
    kernel = functools.partial(mix_react_kernel, tile_blocks, neighbours, block_size)
    return pl.pallas_call(
        kernel,
        grid_spec=grid_spec,
        out_shape=jax.ShapeDtypeStruct((species, count_blocks * block_size), jnp.float32),
        compiler_params=pltpu.CompilerParams(dimension_semantics=("arbitrary",)),
    )(
        neighbour_block,
        migrated,
        mix_weight,
        inverse_temp.reshape(1, -1),
        reactant_order,
        jnp.stack([log_prefactor, activation_energy], axis=1),
        production,
        loss_coefficient,
        migrated,
        from_lower,
        from_upper,
    )


def shards(
    mixing_ratio,
    send_rows,
    migrant_count,
    arrival_slot,
    halo_blocks,
    neighbour_block,
    mix_weight,
    inverse_temp,
    reactant_order,
    log_prefactor,
    activation_energy,
    production,
    loss_coefficient,
):
    migrated = migrate(mixing_ratio, send_rows, migrant_count, arrival_slot)
    from_lower, from_upper = halo_exchange(migrated, halo_blocks, mix_weight.shape[-1])
    return mix_react(
        migrated,
        from_lower,
        from_upper,
        neighbour_block,
        mix_weight,
        inverse_temp,
        reactant_order,
        log_prefactor,
        activation_energy,
        production,
        loss_coefficient,
    )


def solution(mesh):
    placed = (
        P(None, "region"),
        P("region", None, None),
        P("region", None),
        P("region", None, None),
        P("region", None, None),
        P("region", None),
        P("region", None, None, None),
        P("region"),
        P(),
        P(),
        P(),
        P(),
        P(),
    )
    return jax.shard_map(
        shards, mesh=mesh, in_specs=placed, out_specs=P(None, "region"), check_vma=False
    )
```

```python
import functools

import jax
import jax.numpy as jnp
from jax import lax
from jax.experimental import pallas as pl
from jax.experimental.pallas import tpu as pltpu
from jax.sharding import PartitionSpec as P

HOP = 4
TILE_BLOCKS = 8
PAD_ROWS = 160


def from_behind(block, axis, distance):
    devices = range(lax.axis_size(axis))
    route = [((i - distance) % len(devices), i) for i in devices]
    return lax.ppermute(block, axis, route)


def peer_offsets():
    return [column - HOP if column < HOP else column - HOP + 1 for column in range(2 * HOP)]


def pick_kernel(chunk, mixing_ref, rows_ref, out_ref):
    species, parcels = mixing_ref.shape
    wanted = rows_ref[...]
    total = jnp.zeros(out_ref.shape, jnp.float32)
    for part in range(parcels // chunk):
        position = lax.broadcasted_iota(jnp.int32, (chunk, wanted.shape[1]), 0) + part * chunk
        pick = (position == wanted).astype(jnp.bfloat16)
        total = total + jnp.dot(
            mixing_ref[:, part * chunk:(part + 1) * chunk], pick, preferred_element_type=jnp.float32
        )
    out_ref[...] = total.astype(out_ref.dtype)


def place_kernel(chunk, block_size, halo_ref, mixing_ref, received_ref, slots_ref,
                 migrated_ref, lower_ref, upper_ref, sems):
    species, parcels = mixing_ref.shape
    slots = slots_ref[...]
    received = received_ref[...]
    marks = jnp.ones((8, slots.shape[1]), jnp.bfloat16)
    contract = (((1,), (1,)), ((), ()))
    for part in range(parcels // chunk):
        lanes = slice(part * chunk, (part + 1) * chunk)
        position = lax.broadcasted_iota(jnp.int32, (chunk, slots.shape[1]), 0) + part * chunk
        place = (position == slots).astype(jnp.bfloat16)
        placed = lax.dot_general(received, place, contract, preferred_element_type=jnp.float32)
        hit = lax.dot_general(marks, place, contract, preferred_element_type=jnp.float32)[0:1]
        migrated_ref[:, lanes] = jnp.where(
            hit > 0.5, placed.astype(migrated_ref.dtype), mixing_ref[:, lanes]
        )
    sides, listed = halo_ref.shape
    outs = (lower_ref, upper_ref)
    copies = []
    for side in range(sides):
        for j in range(listed):
            start = pl.multiple_of(halo_ref[side, j] * block_size, block_size)
            copy = pltpu.make_async_copy(
                migrated_ref.at[:, pl.ds(start, block_size)],
                outs[side].at[:, pl.ds(j * block_size, block_size)],
                sems.at[side, j],
            )
            copy.start()
            copies.append(copy)
    for copy in copies:
        copy.wait()


def vmem_whole(shape):
    return pl.BlockSpec(shape, lambda *_: (0,) * len(shape))


def migrate(mixing_ratio, send_rows, migrant_count, arrival_slot, halo_blocks, block_size):
    species, parcels = mixing_ratio.shape
    capacity = send_rows.shape[-1]
    offsets = peer_offsets()
    peer_count = len(offsets)
    chunk = 1024
    wanted = send_rows[0].reshape(1, -1)
    outgoing = pl.pallas_call(
        functools.partial(pick_kernel, chunk),
        grid=(1,),
        in_specs=[vmem_whole(mixing_ratio.shape), vmem_whole(wanted.shape)],
        out_specs=vmem_whole((species, wanted.shape[1])),
        out_shape=jax.ShapeDtypeStruct((species, wanted.shape[1]), mixing_ratio.dtype),
    )(mixing_ratio, wanted)
    outgoing = outgoing.reshape(species, peer_count, capacity)
    arrived = []
    for column in range(peer_count):
        opposite = peer_count - 1 - column
        arrived.append(from_behind(outgoing[:, opposite, :], "region", -offsets[column]))
    received = jnp.stack(arrived, axis=1).reshape(species, -1)
    lane_index = jnp.arange(capacity, dtype=jnp.int32)
    live_lane = lane_index[None, :] < migrant_count[0][:, None]
    slots = jnp.where(live_lane, arrival_slot[0], parcels).reshape(1, -1)
    sides, listed = halo_blocks.shape[1:]
    halo_shape = (species, listed * block_size)
    grid_spec = pltpu.PrefetchScalarGridSpec(
        num_scalar_prefetch=1,
        grid=(1,),
        in_specs=[vmem_whole(mixing_ratio.shape), vmem_whole(received.shape), vmem_whole(slots.shape)],
        out_specs=[vmem_whole(mixing_ratio.shape), vmem_whole(halo_shape), vmem_whole(halo_shape)],
        scratch_shapes=[pltpu.SemaphoreType.DMA((sides, listed))],
    )
    migrated, to_lower, to_upper = pl.pallas_call(
        functools.partial(place_kernel, chunk, block_size),
        grid_spec=grid_spec,
        out_shape=[
            jax.ShapeDtypeStruct(mixing_ratio.shape, mixing_ratio.dtype),
            jax.ShapeDtypeStruct(halo_shape, mixing_ratio.dtype),
            jax.ShapeDtypeStruct(halo_shape, mixing_ratio.dtype),
        ],
    )(halo_blocks[0], mixing_ratio, received, slots)
    from_lower = from_behind(to_upper, "region", 1)
    from_upper = from_behind(to_lower, "region", -1)
    return migrated, from_lower, from_upper


def split3(x):
    high = x.astype(jnp.bfloat16)
    low = (x - high.astype(jnp.float32)).astype(jnp.bfloat16)
    return high, low


def dot3(a_high, a_low, b_high, b_low):
    f32 = jnp.float32
    total = jnp.dot(a_high, b_high, preferred_element_type=f32)
    total = total + jnp.dot(a_high, b_low, preferred_element_type=f32)
    return total + jnp.dot(a_low, b_high, preferred_element_type=f32)


def mix_react_kernel(
    tile_blocks,
    neighbours,
    block_size,
    nb_ref,
    own_ref,
    weight_ref,
    temp_ref,
    order_ref,
    rate_terms_ref,
    prod_ref,
    loss_ref,
    migrated_hbm,
    lower_hbm,
    upper_hbm,
    out_ref,
    picked,
    sems,
    mixed_ref,
    order_split,
    gain_split,
    gain_high,
):
    f32 = jnp.float32
    step = pl.program_id(0)
    steps = pl.num_programs(0)
    own_count = migrated_hbm.shape[1] // block_size
    halo_count = lower_hbm.shape[1] // block_size

    def fetch(at, slot, start):
        for t in range(tile_blocks):
            for k in range(neighbours):
                index = nb_ref[at * tile_blocks + t, k]
                target = picked.at[slot, t * neighbours + k]
                sem = sems.at[slot, t * neighbours + k]
                if not start:
                    pltpu.make_async_copy(
                        migrated_hbm.at[:, pl.ds(0, block_size)], target, sem
                    ).wait()
                    continue
                sources = (
                    (migrated_hbm, index, index < own_count),
                    (lower_hbm, index - own_count,
                     (index >= own_count) & (index < own_count + halo_count)),
                    (upper_hbm, index - own_count - halo_count,
                     index >= own_count + halo_count),
                )
                for source, local, chosen in sources:
                    limit = source.shape[1] // block_size - 1
                    local = jnp.minimum(jnp.maximum(local, 0), limit)

                    @pl.when(chosen)
                    def _():
                        begin = pl.multiple_of(local * block_size, block_size)
                        pltpu.make_async_copy(
                            source.at[:, pl.ds(begin, block_size)], target, sem
                        ).start()

    @pl.when(step == 0)
    def _():
        fetch(0, 0, True)
        order_high, order_low = split3(order_ref[...])
        reactions = order_high.shape[0]
        order_split[0:reactions] = order_high
        order_split[reactions:] = order_low
        gain_split[...] = jnp.zeros_like(gain_split)
        rows = prod_ref.shape[0]
        for part, source in enumerate((prod_ref, loss_ref)):
            high, low = split3(source[...])
            gain_split[pl.ds(2 * part * PAD_ROWS, rows)] = high
            gain_split[pl.ds((2 * part + 1) * PAD_ROWS, rows)] = low
            gain_high[pl.ds(part * PAD_ROWS, rows)] = high
        gain_high[...] = jnp.where(
            lax.broadcasted_iota(jnp.int32, gain_high.shape, 0) % PAD_ROWS < rows,
            gain_high[...],
            jnp.zeros_like(gain_high),
        )

    slot = step % 2

    @pl.when(step + 1 < steps)
    def _():
        fetch(step + 1, 1 - slot, True)

    fetch(step, slot, False)

    for t in range(tile_blocks):
        lanes = slice(t * block_size, (t + 1) * block_size)
        stacked = jnp.concatenate(
            [own_ref[:, lanes]] + [picked[slot, t * neighbours + k] for k in range(neighbours)],
            axis=1,
        )
        weight = weight_ref[t].reshape((neighbours + 1) * block_size, block_size)
        mixed_ref[:, lanes] = jnp.dot(stacked, weight, preferred_element_type=f32)
    mixed = mixed_ref[...]
    species = mixed.shape[0]
    log_high, log_low = split3(jnp.log(mixed))
    reactions = order_split.shape[0] // 2
    both = jnp.dot(order_split[...], log_high, preferred_element_type=f32)
    exponent = both[:reactions] + both[reactions:]
    exponent = exponent + jnp.dot(order_split[0:reactions], log_low, preferred_element_type=f32)
    prefactor = rate_terms_ref[:, 0:1]
    energy = rate_terms_ref[:, 1:2]
    rate = jnp.exp(prefactor - energy * temp_ref[...] + exponent)
    rate_high, rate_low = split3(rate)
    by_high = jnp.dot(gain_split[...], rate_high, preferred_element_type=f32)
    by_low = jnp.dot(gain_high[...], rate_low, preferred_element_type=f32)
    gained = by_high[0:species] + by_high[PAD_ROWS:PAD_ROWS + species] + by_low[0:species]
    lost_mass = (
        by_high[2 * PAD_ROWS:2 * PAD_ROWS + species]
        + by_high[3 * PAD_ROWS:3 * PAD_ROWS + species]
        + by_low[PAD_ROWS:PAD_ROWS + species]
    )
    out_ref[...] = (mixed + gained) / (1.0 + lost_mass / mixed)


def mix_react(
    migrated,
    from_lower,
    from_upper,
    neighbour_block,
    mix_weight,
    inverse_temp,
    reactant_order,
    log_prefactor,
    activation_energy,
    production,
    loss_coefficient,
):
    species = migrated.shape[0]
    count_blocks, _, block_size, _ = mix_weight.shape
    neighbours = neighbour_block.shape[1]
    reactions = reactant_order.shape[0]
    tile_blocks = TILE_BLOCKS
    width = tile_blocks * block_size
    steps = count_blocks // tile_blocks

    def whole(shape):
        return pl.BlockSpec(shape, lambda i, nb: (0,) * len(shape))

    in_specs = [
        pl.BlockSpec((species, width), lambda i, nb: (0, i)),
        pl.BlockSpec((tile_blocks,) + mix_weight.shape[1:], lambda i, nb: (i, 0, 0, 0)),
        pl.BlockSpec((1, width), lambda i, nb: (0, i)),
        whole(reactant_order.shape),
        whole((reactions, 2)),
        whole(production.shape),
        whole(loss_coefficient.shape),
        pl.BlockSpec(memory_space=pl.ANY),
        pl.BlockSpec(memory_space=pl.ANY),
        pl.BlockSpec(memory_space=pl.ANY),
    ]
    bf16 = jnp.bfloat16
    grid_spec = pltpu.PrefetchScalarGridSpec(
        num_scalar_prefetch=1,
        grid=(steps,),
        in_specs=in_specs,
        out_specs=pl.BlockSpec((species, width), lambda i, nb: (0, i)),
        scratch_shapes=[
            pltpu.VMEM((2, tile_blocks * neighbours, species, block_size), bf16),
            pltpu.SemaphoreType.DMA((2, tile_blocks * neighbours)),
            pltpu.VMEM((species, width), jnp.float32),
            pltpu.VMEM((2 * reactions, species), bf16),
            pltpu.VMEM((4 * PAD_ROWS, reactions), bf16),
            pltpu.VMEM((2 * PAD_ROWS, reactions), bf16),
        ],
    )
    kernel = functools.partial(mix_react_kernel, tile_blocks, neighbours, block_size)
    return pl.pallas_call(
        kernel,
        grid_spec=grid_spec,
        out_shape=jax.ShapeDtypeStruct((species, count_blocks * block_size), jnp.float32),
        compiler_params=pltpu.CompilerParams(dimension_semantics=("arbitrary",)),
    )(
        neighbour_block,
        migrated,
        mix_weight,
        inverse_temp.reshape(1, -1),
        reactant_order,
        jnp.stack([log_prefactor, activation_energy], axis=1),
        production,
        loss_coefficient,
        migrated,
        from_lower,
        from_upper,
    )


def shards(
    mixing_ratio,
    send_rows,
    migrant_count,
    arrival_slot,
    halo_blocks,
    neighbour_block,
    mix_weight,
    inverse_temp,
    reactant_order,
    log_prefactor,
    activation_energy,
    production,
    loss_coefficient,
):
    migrated, from_lower, from_upper = migrate(
        mixing_ratio, send_rows, migrant_count, arrival_slot, halo_blocks, mix_weight.shape[-1]
    )
    return mix_react(
        migrated,
        from_lower,
        from_upper,
        neighbour_block,
        mix_weight,
        inverse_temp,
        reactant_order,
        log_prefactor,
        activation_energy,
        production,
        loss_coefficient,
    )


def solution(mesh):
    placed = (
        P(None, "region"),
        P("region", None, None),
        P("region", None),
        P("region", None, None),
        P("region", None, None),
        P("region", None),
        P("region", None, None, None),
        P("region"),
        P(),
        P(),
        P(),
        P(),
        P(),
    )
    return jax.shard_map(
        shards, mesh=mesh, in_specs=placed, out_specs=P(None, "region"), check_vma=False
    )
```

```python
import functools

import jax
import jax.numpy as jnp
from jax import lax
from jax.experimental import pallas as pl
from jax.experimental.pallas import tpu as pltpu
from jax.sharding import PartitionSpec as P

HOP = 4
TILE_BLOCKS = 8
PAD_ROWS = 160


def from_behind(block, axis, distance):
    devices = range(lax.axis_size(axis))
    route = [((i - distance) % len(devices), i) for i in devices]
    return lax.ppermute(block, axis, route)


def peer_offsets():
    return [column - HOP if column < HOP else column - HOP + 1 for column in range(2 * HOP)]


def pick_kernel(chunk, mixing_ref, rows_ref, out_ref):
    species, parcels = mixing_ref.shape
    wanted = rows_ref[...]
    total = jnp.zeros(out_ref.shape, jnp.float32)
    for part in range(parcels // chunk):
        position = lax.broadcasted_iota(jnp.int32, (chunk, wanted.shape[1]), 0) + part * chunk
        pick = (position == wanted).astype(jnp.bfloat16)
        total = total + jnp.dot(
            mixing_ref[:, part * chunk:(part + 1) * chunk], pick, preferred_element_type=jnp.float32
        )
    out_ref[...] = total.astype(out_ref.dtype)


def place_kernel(chunk, block_size, halo_ref, mixing_ref, received_ref, slots_ref,
                 migrated_ref, lower_ref, upper_ref, sems):
    species, parcels = mixing_ref.shape
    slots = slots_ref[...]
    received = received_ref[...]
    marks = jnp.ones((8, slots.shape[0]), jnp.bfloat16)
    for part in range(parcels // chunk):
        lanes = slice(part * chunk, (part + 1) * chunk)
        position = lax.broadcasted_iota(jnp.int32, (slots.shape[0], chunk), 1) + part * chunk
        place = (position == slots).astype(jnp.bfloat16)
        placed = jnp.dot(received, place, preferred_element_type=jnp.float32)
        hit = jnp.dot(marks, place, preferred_element_type=jnp.float32)[0:1]
        migrated_ref[:, lanes] = jnp.where(
            hit > 0.5, placed.astype(migrated_ref.dtype), mixing_ref[:, lanes]
        )
    sides, listed = halo_ref.shape
    outs = (lower_ref, upper_ref)
    copies = []
    for side in range(sides):
        for j in range(listed):
            start = pl.multiple_of(halo_ref[side, j] * block_size, block_size)
            copy = pltpu.make_async_copy(
                migrated_ref.at[:, pl.ds(start, block_size)],
                outs[side].at[:, pl.ds(j * block_size, block_size)],
                sems.at[side, j],
            )
            copy.start()
            copies.append(copy)
    for copy in copies:
        copy.wait()


def vmem_whole(shape):
    return pl.BlockSpec(shape, lambda *_: (0,) * len(shape))


def migrate(mixing_ratio, send_rows, migrant_count, arrival_slot, halo_blocks, block_size):
    species, parcels = mixing_ratio.shape
    capacity = send_rows.shape[-1]
    offsets = peer_offsets()
    peer_count = len(offsets)
    chunk = 1024
    wanted = send_rows[0].reshape(1, -1)
    outgoing = pl.pallas_call(
        functools.partial(pick_kernel, chunk),
        grid=(1,),
        in_specs=[vmem_whole(mixing_ratio.shape), vmem_whole(wanted.shape)],
        out_specs=vmem_whole((species, wanted.shape[1])),
        out_shape=jax.ShapeDtypeStruct((species, wanted.shape[1]), mixing_ratio.dtype),
    )(mixing_ratio, wanted)
    outgoing = outgoing.reshape(species, peer_count, capacity)
    arrived = []
    for column in range(peer_count):
        opposite = peer_count - 1 - column
        arrived.append(from_behind(outgoing[:, opposite, :], "region", -offsets[column]))
    received = jnp.stack(arrived, axis=1).reshape(species, -1)
    lane_index = jnp.arange(capacity, dtype=jnp.int32)
    live_lane = lane_index[None, :] < migrant_count[0][:, None]
    slots = jnp.where(live_lane, arrival_slot[0], parcels).reshape(-1, 1)
    sides, listed = halo_blocks.shape[1:]
    halo_shape = (species, listed * block_size)
    grid_spec = pltpu.PrefetchScalarGridSpec(
        num_scalar_prefetch=1,
        grid=(1,),
        in_specs=[vmem_whole(mixing_ratio.shape), vmem_whole(received.shape), vmem_whole(slots.shape)],
        out_specs=[vmem_whole(mixing_ratio.shape), vmem_whole(halo_shape), vmem_whole(halo_shape)],
        scratch_shapes=[pltpu.SemaphoreType.DMA((sides, listed))],
    )
    migrated, to_lower, to_upper = pl.pallas_call(
        functools.partial(place_kernel, chunk, block_size),
        grid_spec=grid_spec,
        out_shape=[
            jax.ShapeDtypeStruct(mixing_ratio.shape, mixing_ratio.dtype),
            jax.ShapeDtypeStruct(halo_shape, mixing_ratio.dtype),
            jax.ShapeDtypeStruct(halo_shape, mixing_ratio.dtype),
        ],
    )(halo_blocks[0], mixing_ratio, received, slots)
    from_lower = from_behind(to_upper, "region", 1)
    from_upper = from_behind(to_lower, "region", -1)
    return migrated, from_lower, from_upper


def split3(x):
    high = x.astype(jnp.bfloat16)
    low = (x - high.astype(jnp.float32)).astype(jnp.bfloat16)
    return high, low


def dot3(a_high, a_low, b_high, b_low):
    f32 = jnp.float32
    total = jnp.dot(a_high, b_high, preferred_element_type=f32)
    total = total + jnp.dot(a_high, b_low, preferred_element_type=f32)
    return total + jnp.dot(a_low, b_high, preferred_element_type=f32)


def mix_react_kernel(
    tile_blocks,
    neighbours,
    block_size,
    nb_ref,
    own_ref,
    weight_ref,
    temp_ref,
    order_ref,
    rate_terms_ref,
    prod_ref,
    loss_ref,
    migrated_hbm,
    lower_hbm,
    upper_hbm,
    out_ref,
    picked,
    sems,
    mixed_ref,
    order_split,
    gain_split,
    gain_high,
):
    f32 = jnp.float32
    step = pl.program_id(0)
    steps = pl.num_programs(0)
    own_count = migrated_hbm.shape[1] // block_size
    halo_count = lower_hbm.shape[1] // block_size

    def fetch(at, slot, start):
        for t in range(tile_blocks):
            for k in range(neighbours):
                index = nb_ref[at * tile_blocks + t, k]
                target = picked.at[slot, t * neighbours + k]
                sem = sems.at[slot, t * neighbours + k]
                if not start:
                    pltpu.make_async_copy(
                        migrated_hbm.at[:, pl.ds(0, block_size)], target, sem
                    ).wait()
                    continue
                sources = (
                    (migrated_hbm, index, index < own_count),
                    (lower_hbm, index - own_count,
                     (index >= own_count) & (index < own_count + halo_count)),
                    (upper_hbm, index - own_count - halo_count,
                     index >= own_count + halo_count),
                )
                for source, local, chosen in sources:
                    limit = source.shape[1] // block_size - 1
                    local = jnp.minimum(jnp.maximum(local, 0), limit)

                    @pl.when(chosen)
                    def _():
                        begin = pl.multiple_of(local * block_size, block_size)
                        pltpu.make_async_copy(
                            source.at[:, pl.ds(begin, block_size)], target, sem
                        ).start()

    @pl.when(step == 0)
    def _():
        fetch(0, 0, True)
        order_high, order_low = split3(order_ref[...])
        reactions = order_high.shape[0]
        order_split[0:reactions] = order_high
        order_split[reactions:] = order_low
        gain_split[...] = jnp.zeros_like(gain_split)
        rows = prod_ref.shape[0]
        for part, source in enumerate((prod_ref, loss_ref)):
            high, low = split3(source[...])
            gain_split[pl.ds(2 * part * PAD_ROWS, rows)] = high
            gain_split[pl.ds((2 * part + 1) * PAD_ROWS, rows)] = low
            gain_high[pl.ds(part * PAD_ROWS, rows)] = high
        gain_high[...] = jnp.where(
            lax.broadcasted_iota(jnp.int32, gain_high.shape, 0) % PAD_ROWS < rows,
            gain_high[...],
            jnp.zeros_like(gain_high),
        )

    slot = step % 2

    @pl.when(step + 1 < steps)
    def _():
        fetch(step + 1, 1 - slot, True)

    fetch(step, slot, False)

    for t in range(tile_blocks):
        lanes = slice(t * block_size, (t + 1) * block_size)
        stacked = jnp.concatenate(
            [own_ref[:, lanes]] + [picked[slot, t * neighbours + k] for k in range(neighbours)],
            axis=1,
        )
        weight = weight_ref[t].reshape((neighbours + 1) * block_size, block_size)
        mixed_ref[:, lanes] = jnp.dot(stacked, weight, preferred_element_type=f32)
    mixed = mixed_ref[...]
    species = mixed.shape[0]
    log_high, log_low = split3(jnp.log(mixed))
    reactions = order_split.shape[0] // 2
    both = jnp.dot(order_split[...], log_high, preferred_element_type=f32)
    exponent = both[:reactions] + both[reactions:]
    exponent = exponent + jnp.dot(order_split[0:reactions], log_low, preferred_element_type=f32)
    prefactor = rate_terms_ref[:, 0:1]
    energy = rate_terms_ref[:, 1:2]
    rate = jnp.exp(prefactor - energy * temp_ref[...] + exponent)
    rate_high, rate_low = split3(rate)
    by_high = jnp.dot(gain_split[...], rate_high, preferred_element_type=f32)
    by_low = jnp.dot(gain_high[...], rate_low, preferred_element_type=f32)
    gained = by_high[0:species] + by_high[PAD_ROWS:PAD_ROWS + species] + by_low[0:species]
    lost_mass = (
        by_high[2 * PAD_ROWS:2 * PAD_ROWS + species]
        + by_high[3 * PAD_ROWS:3 * PAD_ROWS + species]
        + by_low[PAD_ROWS:PAD_ROWS + species]
    )
    out_ref[...] = (mixed + gained) / (1.0 + lost_mass / mixed)


def mix_react(
    migrated,
    from_lower,
    from_upper,
    neighbour_block,
    mix_weight,
    inverse_temp,
    reactant_order,
    log_prefactor,
    activation_energy,
    production,
    loss_coefficient,
):
    species = migrated.shape[0]
    count_blocks, _, block_size, _ = mix_weight.shape
    neighbours = neighbour_block.shape[1]
    reactions = reactant_order.shape[0]
    tile_blocks = TILE_BLOCKS
    width = tile_blocks * block_size
    steps = count_blocks // tile_blocks

    def whole(shape):
        return pl.BlockSpec(shape, lambda i, nb: (0,) * len(shape))

    in_specs = [
        pl.BlockSpec((species, width), lambda i, nb: (0, i)),
        pl.BlockSpec((tile_blocks,) + mix_weight.shape[1:], lambda i, nb: (i, 0, 0, 0)),
        pl.BlockSpec((1, width), lambda i, nb: (0, i)),
        whole(reactant_order.shape),
        whole((reactions, 2)),
        whole(production.shape),
        whole(loss_coefficient.shape),
        pl.BlockSpec(memory_space=pl.ANY),
        pl.BlockSpec(memory_space=pl.ANY),
        pl.BlockSpec(memory_space=pl.ANY),
    ]
    bf16 = jnp.bfloat16
    grid_spec = pltpu.PrefetchScalarGridSpec(
        num_scalar_prefetch=1,
        grid=(steps,),
        in_specs=in_specs,
        out_specs=pl.BlockSpec((species, width), lambda i, nb: (0, i)),
        scratch_shapes=[
            pltpu.VMEM((2, tile_blocks * neighbours, species, block_size), bf16),
            pltpu.SemaphoreType.DMA((2, tile_blocks * neighbours)),
            pltpu.VMEM((species, width), jnp.float32),
            pltpu.VMEM((2 * reactions, species), bf16),
            pltpu.VMEM((4 * PAD_ROWS, reactions), bf16),
            pltpu.VMEM((2 * PAD_ROWS, reactions), bf16),
        ],
    )
    kernel = functools.partial(mix_react_kernel, tile_blocks, neighbours, block_size)
    return pl.pallas_call(
        kernel,
        grid_spec=grid_spec,
        out_shape=jax.ShapeDtypeStruct((species, count_blocks * block_size), jnp.float32),
        compiler_params=pltpu.CompilerParams(dimension_semantics=("arbitrary",)),
    )(
        neighbour_block,
        migrated,
        mix_weight,
        inverse_temp.reshape(1, -1),
        reactant_order,
        jnp.stack([log_prefactor, activation_energy], axis=1),
        production,
        loss_coefficient,
        migrated,
        from_lower,
        from_upper,
    )


def shards(
    mixing_ratio,
    send_rows,
    migrant_count,
    arrival_slot,
    halo_blocks,
    neighbour_block,
    mix_weight,
    inverse_temp,
    reactant_order,
    log_prefactor,
    activation_energy,
    production,
    loss_coefficient,
):
    migrated, from_lower, from_upper = migrate(
        mixing_ratio, send_rows, migrant_count, arrival_slot, halo_blocks, mix_weight.shape[-1]
    )
    return mix_react(
        migrated,
        from_lower,
        from_upper,
        neighbour_block,
        mix_weight,
        inverse_temp,
        reactant_order,
        log_prefactor,
        activation_energy,
        production,
        loss_coefficient,
    )


def solution(mesh):
    placed = (
        P(None, "region"),
        P("region", None, None),
        P("region", None),
        P("region", None, None),
        P("region", None, None),
        P("region", None),
        P("region", None, None, None),
        P("region"),
        P(),
        P(),
        P(),
        P(),
        P(),
    )
    return jax.shard_map(
        shards, mesh=mesh, in_specs=placed, out_specs=P(None, "region"), check_vma=False
    )
```

```python
import functools

import jax
import jax.numpy as jnp
from jax import lax
from jax.experimental import pallas as pl
from jax.experimental.pallas import tpu as pltpu
from jax.sharding import PartitionSpec as P

HOP = 4
TILE_BLOCKS = 8
PAD_ROWS = 160


def from_behind(block, axis, distance):
    devices = range(lax.axis_size(axis))
    route = [((i - distance) % len(devices), i) for i in devices]
    return lax.ppermute(block, axis, route)


def peer_offsets():
    return [column - HOP if column < HOP else column - HOP + 1 for column in range(2 * HOP)]


def pick_kernel(chunk, mixing_ref, rows_ref, *out_refs):
    species, parcels = mixing_ref.shape
    wanted = rows_ref[...]
    total = jnp.zeros((species, wanted.shape[1]), jnp.float32)
    for part in range(parcels // chunk):
        position = lax.broadcasted_iota(jnp.int32, (chunk, wanted.shape[1]), 0) + part * chunk
        pick = (position == wanted).astype(jnp.bfloat16)
        total = total + jnp.dot(
            mixing_ref[:, part * chunk:(part + 1) * chunk], pick, preferred_element_type=jnp.float32
        )
    width = out_refs[0].shape[1]
    for column, out_ref in enumerate(out_refs):
        out_ref[...] = total[:, column * width:(column + 1) * width].astype(out_ref.dtype)


def place_kernel(chunk, block_size, peer_count, halo_ref, mixing_ref, *refs):
    received_refs = refs[:peer_count]
    slots_ref, migrated_ref, lower_ref, upper_ref, sems = refs[peer_count:]
    species, parcels = mixing_ref.shape
    slots = slots_ref[...]
    received = jnp.concatenate([ref[...] for ref in received_refs], axis=1)
    pad = (-species) % 16 or 16
    marked = jnp.concatenate([received, jnp.ones((pad, slots.shape[0]), received.dtype)], axis=0)
    for part in range(parcels // chunk):
        lanes = slice(part * chunk, (part + 1) * chunk)
        position = lax.broadcasted_iota(jnp.int32, (slots.shape[0], chunk), 1) + part * chunk
        place = (position == slots).astype(jnp.bfloat16)
        placed = jnp.dot(marked, place, preferred_element_type=jnp.float32)
        hit = placed[species:species + 1]
        migrated_ref[:, lanes] = jnp.where(
            hit > 0.5, placed[:species].astype(migrated_ref.dtype), mixing_ref[:, lanes]
        )
    sides, listed = halo_ref.shape
    outs = (lower_ref, upper_ref)
    copies = []
    for side in range(sides):
        for j in range(listed):
            start = pl.multiple_of(halo_ref[side, j] * block_size, block_size)
            copy = pltpu.make_async_copy(
                migrated_ref.at[:, pl.ds(start, block_size)],
                outs[side].at[:, pl.ds(j * block_size, block_size)],
                sems.at[side, j],
            )
            copy.start()
            copies.append(copy)
    for copy in copies:
        copy.wait()


def vmem_whole(shape):
    return pl.BlockSpec(shape, lambda *_: (0,) * len(shape))


def migrate(mixing_ratio, send_rows, migrant_count, arrival_slot, halo_blocks, block_size):
    species, parcels = mixing_ratio.shape
    capacity = send_rows.shape[-1]
    offsets = peer_offsets()
    peer_count = len(offsets)
    chunk = 1024
    wanted = send_rows[0].reshape(1, -1)
    outgoing = pl.pallas_call(
        functools.partial(pick_kernel, chunk),
        grid=(1,),
        in_specs=[vmem_whole(mixing_ratio.shape), vmem_whole(wanted.shape)],
        out_specs=[vmem_whole((species, capacity))] * peer_count,
        out_shape=[jax.ShapeDtypeStruct((species, capacity), mixing_ratio.dtype)] * peer_count,
    )(mixing_ratio, wanted)
    arrived = []
    for column in range(peer_count):
        opposite = peer_count - 1 - column
        arrived.append(from_behind(outgoing[opposite], "region", -offsets[column]))
    lane_index = jnp.arange(capacity, dtype=jnp.int32)
    live_lane = lane_index[None, :] < migrant_count[0][:, None]
    slots = jnp.where(live_lane, arrival_slot[0], parcels).reshape(-1, 1)
    sides, listed = halo_blocks.shape[1:]
    halo_shape = (species, listed * block_size)
    grid_spec = pltpu.PrefetchScalarGridSpec(
        num_scalar_prefetch=1,
        grid=(1,),
        in_specs=[vmem_whole(mixing_ratio.shape)]
        + [vmem_whole((species, capacity))] * peer_count
        + [vmem_whole(slots.shape)],
        out_specs=[vmem_whole(mixing_ratio.shape), vmem_whole(halo_shape), vmem_whole(halo_shape)],
        scratch_shapes=[pltpu.SemaphoreType.DMA((sides, listed))],
    )
    migrated, to_lower, to_upper = pl.pallas_call(
        functools.partial(place_kernel, chunk, block_size, peer_count),
        grid_spec=grid_spec,
        out_shape=[
            jax.ShapeDtypeStruct(mixing_ratio.shape, mixing_ratio.dtype),
            jax.ShapeDtypeStruct(halo_shape, mixing_ratio.dtype),
            jax.ShapeDtypeStruct(halo_shape, mixing_ratio.dtype),
        ],
    )(halo_blocks[0], mixing_ratio, *arrived, slots)
    from_lower = from_behind(to_upper, "region", 1)
    from_upper = from_behind(to_lower, "region", -1)
    return migrated, from_lower, from_upper


def split3(x):
    high = x.astype(jnp.bfloat16)
    low = (x - high.astype(jnp.float32)).astype(jnp.bfloat16)
    return high, low


def dot3(a_high, a_low, b_high, b_low):
    f32 = jnp.float32
    total = jnp.dot(a_high, b_high, preferred_element_type=f32)
    total = total + jnp.dot(a_high, b_low, preferred_element_type=f32)
    return total + jnp.dot(a_low, b_high, preferred_element_type=f32)


def mix_react_kernel(
    tile_blocks,
    neighbours,
    block_size,
    nb_ref,
    own_ref,
    weight_ref,
    temp_ref,
    order_ref,
    rate_terms_ref,
    prod_ref,
    loss_ref,
    migrated_hbm,
    lower_hbm,
    upper_hbm,
    out_ref,
    picked,
    sems,
    mixed_ref,
    order_split,
    gain_split,
    gain_high,
):
    f32 = jnp.float32
    step = pl.program_id(0)
    steps = pl.num_programs(0)
    own_count = migrated_hbm.shape[1] // block_size
    halo_count = lower_hbm.shape[1] // block_size

    def fetch(at, slot, start):
        for t in range(tile_blocks):
            for k in range(neighbours):
                index = nb_ref[at * tile_blocks + t, k]
                target = picked.at[slot, t * neighbours + k]
                sem = sems.at[slot, t * neighbours + k]
                if not start:
                    pltpu.make_async_copy(
                        migrated_hbm.at[:, pl.ds(0, block_size)], target, sem
                    ).wait()
                    continue
                sources = (
                    (migrated_hbm, index, index < own_count),
                    (lower_hbm, index - own_count,
                     (index >= own_count) & (index < own_count + halo_count)),
                    (upper_hbm, index - own_count - halo_count,
                     index >= own_count + halo_count),
                )
                for source, local, chosen in sources:
                    limit = source.shape[1] // block_size - 1
                    local = jnp.minimum(jnp.maximum(local, 0), limit)

                    @pl.when(chosen)
                    def _():
                        begin = pl.multiple_of(local * block_size, block_size)
                        pltpu.make_async_copy(
                            source.at[:, pl.ds(begin, block_size)], target, sem
                        ).start()

    @pl.when(step == 0)
    def _():
        fetch(0, 0, True)
        order_high, order_low = split3(order_ref[...])
        reactions = order_high.shape[0]
        order_split[0:reactions] = order_high
        order_split[reactions:] = order_low
        gain_split[...] = jnp.zeros_like(gain_split)
        rows = prod_ref.shape[0]
        for part, source in enumerate((prod_ref, loss_ref)):
            high, low = split3(source[...])
            gain_split[pl.ds(2 * part * PAD_ROWS, rows)] = high
            gain_split[pl.ds((2 * part + 1) * PAD_ROWS, rows)] = low
            gain_high[pl.ds(part * PAD_ROWS, rows)] = high
        gain_high[...] = jnp.where(
            lax.broadcasted_iota(jnp.int32, gain_high.shape, 0) % PAD_ROWS < rows,
            gain_high[...],
            jnp.zeros_like(gain_high),
        )

    slot = step % 2

    @pl.when(step + 1 < steps)
    def _():
        fetch(step + 1, 1 - slot, True)

    fetch(step, slot, False)

    for t in range(tile_blocks):
        lanes = slice(t * block_size, (t + 1) * block_size)
        stacked = jnp.concatenate(
            [own_ref[:, lanes]] + [picked[slot, t * neighbours + k] for k in range(neighbours)],
            axis=1,
        )
        weight = weight_ref[t].reshape((neighbours + 1) * block_size, block_size)
        mixed_ref[:, lanes] = jnp.dot(stacked, weight, preferred_element_type=f32)
    mixed = mixed_ref[...]
    species = mixed.shape[0]
    log_high, log_low = split3(jnp.log(mixed))
    reactions = order_split.shape[0] // 2
    both = jnp.dot(order_split[...], log_high, preferred_element_type=f32)
    exponent = both[:reactions] + both[reactions:]
    exponent = exponent + jnp.dot(order_split[0:reactions], log_low, preferred_element_type=f32)
    prefactor = rate_terms_ref[:, 0:1]
    energy = rate_terms_ref[:, 1:2]
    rate = jnp.exp(prefactor - energy * temp_ref[...] + exponent)
    rate_high, rate_low = split3(rate)
    by_high = jnp.dot(gain_split[...], rate_high, preferred_element_type=f32)
    by_low = jnp.dot(gain_high[...], rate_low, preferred_element_type=f32)
    gained = by_high[0:species] + by_high[PAD_ROWS:PAD_ROWS + species] + by_low[0:species]
    lost_mass = (
        by_high[2 * PAD_ROWS:2 * PAD_ROWS + species]
        + by_high[3 * PAD_ROWS:3 * PAD_ROWS + species]
        + by_low[PAD_ROWS:PAD_ROWS + species]
    )
    out_ref[...] = (mixed + gained) / (1.0 + lost_mass / mixed)


def mix_react(
    migrated,
    from_lower,
    from_upper,
    neighbour_block,
    mix_weight,
    inverse_temp,
    reactant_order,
    log_prefactor,
    activation_energy,
    production,
    loss_coefficient,
):
    species = migrated.shape[0]
    count_blocks, _, block_size, _ = mix_weight.shape
    neighbours = neighbour_block.shape[1]
    reactions = reactant_order.shape[0]
    tile_blocks = TILE_BLOCKS
    width = tile_blocks * block_size
    steps = count_blocks // tile_blocks

    def whole(shape):
        return pl.BlockSpec(shape, lambda i, nb: (0,) * len(shape))

    in_specs = [
        pl.BlockSpec((species, width), lambda i, nb: (0, i)),
        pl.BlockSpec((tile_blocks,) + mix_weight.shape[1:], lambda i, nb: (i, 0, 0, 0)),
        pl.BlockSpec((1, width), lambda i, nb: (0, i)),
        whole(reactant_order.shape),
        whole((reactions, 2)),
        whole(production.shape),
        whole(loss_coefficient.shape),
        pl.BlockSpec(memory_space=pl.ANY),
        pl.BlockSpec(memory_space=pl.ANY),
        pl.BlockSpec(memory_space=pl.ANY),
    ]
    bf16 = jnp.bfloat16
    grid_spec = pltpu.PrefetchScalarGridSpec(
        num_scalar_prefetch=1,
        grid=(steps,),
        in_specs=in_specs,
        out_specs=pl.BlockSpec((species, width), lambda i, nb: (0, i)),
        scratch_shapes=[
            pltpu.VMEM((2, tile_blocks * neighbours, species, block_size), bf16),
            pltpu.SemaphoreType.DMA((2, tile_blocks * neighbours)),
            pltpu.VMEM((species, width), jnp.float32),
            pltpu.VMEM((2 * reactions, species), bf16),
            pltpu.VMEM((4 * PAD_ROWS, reactions), bf16),
            pltpu.VMEM((2 * PAD_ROWS, reactions), bf16),
        ],
    )
    kernel = functools.partial(mix_react_kernel, tile_blocks, neighbours, block_size)
    return pl.pallas_call(
        kernel,
        grid_spec=grid_spec,
        out_shape=jax.ShapeDtypeStruct((species, count_blocks * block_size), jnp.float32),
        compiler_params=pltpu.CompilerParams(dimension_semantics=("arbitrary",)),
    )(
        neighbour_block,
        migrated,
        mix_weight,
        inverse_temp.reshape(1, -1),
        reactant_order,
        jnp.stack([log_prefactor, activation_energy], axis=1),
        production,
        loss_coefficient,
        migrated,
        from_lower,
        from_upper,
    )


def shards(
    mixing_ratio,
    send_rows,
    migrant_count,
    arrival_slot,
    halo_blocks,
    neighbour_block,
    mix_weight,
    inverse_temp,
    reactant_order,
    log_prefactor,
    activation_energy,
    production,
    loss_coefficient,
):
    migrated, from_lower, from_upper = migrate(
        mixing_ratio, send_rows, migrant_count, arrival_slot, halo_blocks, mix_weight.shape[-1]
    )
    return mix_react(
        migrated,
        from_lower,
        from_upper,
        neighbour_block,
        mix_weight,
        inverse_temp,
        reactant_order,
        log_prefactor,
        activation_energy,
        production,
        loss_coefficient,
    )


def solution(mesh):
    placed = (
        P(None, "region"),
        P("region", None, None),
        P("region", None),
        P("region", None, None),
        P("region", None, None),
        P("region", None),
        P("region", None, None, None),
        P("region"),
        P(),
        P(),
        P(),
        P(),
        P(),
    )
    return jax.shard_map(
        shards, mesh=mesh, in_specs=placed, out_specs=P(None, "region"), check_vma=False
    )
```

```python
import functools

import jax
import jax.numpy as jnp
from jax import lax
from jax.experimental import pallas as pl
from jax.experimental.pallas import tpu as pltpu
from jax.sharding import PartitionSpec as P

HOP = 4
TILE_BLOCKS = 8
PAD_ROWS = 160


def from_behind(block, axis, distance):
    devices = range(lax.axis_size(axis))
    route = [((i - distance) % len(devices), i) for i in devices]
    return lax.ppermute(block, axis, route)


def peer_offsets():
    return [column - HOP if column < HOP else column - HOP + 1 for column in range(2 * HOP)]


def pick_kernel(chunk, mixing_ref, rows_ref, *out_refs):
    species, parcels = mixing_ref.shape
    wanted = rows_ref[...]
    total = jnp.zeros((species, wanted.shape[1]), jnp.float32)
    position = lax.broadcasted_iota(jnp.int32, (chunk, wanted.shape[1]), 0)
    for part in range(parcels // chunk):
        pick = (position == wanted - part * chunk).astype(jnp.bfloat16)
        total = total + jnp.dot(
            mixing_ref[:, part * chunk:(part + 1) * chunk], pick, preferred_element_type=jnp.float32
        )
    width = out_refs[0].shape[1]
    for column, out_ref in enumerate(out_refs):
        out_ref[...] = total[:, column * width:(column + 1) * width].astype(out_ref.dtype)


def place_kernel(chunk, block_size, peer_count, halo_ref, mixing_ref, *refs):
    received_refs = refs[:peer_count]
    slots_ref, migrated_ref, lower_ref, upper_ref, sems = refs[peer_count:]
    species, parcels = mixing_ref.shape
    slots = slots_ref[...]
    received = jnp.concatenate([ref[...] for ref in received_refs], axis=1)
    pad = (-species) % 16 or 16
    marked = jnp.concatenate([received, jnp.ones((pad, slots.shape[0]), received.dtype)], axis=0)
    position = lax.broadcasted_iota(jnp.int32, (slots.shape[0], chunk), 1)
    for part in range(parcels // chunk):
        lanes = slice(part * chunk, (part + 1) * chunk)
        place = (position == slots - part * chunk).astype(jnp.bfloat16)
        placed = jnp.dot(marked, place, preferred_element_type=jnp.float32)
        hit = placed[species:species + 1]
        migrated_ref[:, lanes] = jnp.where(
            hit > 0.5, placed[:species].astype(migrated_ref.dtype), mixing_ref[:, lanes]
        )
    sides, listed = halo_ref.shape
    outs = (lower_ref, upper_ref)
    copies = []
    for side in range(sides):
        for j in range(listed):
            start = pl.multiple_of(halo_ref[side, j] * block_size, block_size)
            copy = pltpu.make_async_copy(
                migrated_ref.at[:, pl.ds(start, block_size)],
                outs[side].at[:, pl.ds(j * block_size, block_size)],
                sems.at[side, j],
            )
            copy.start()
            copies.append(copy)
    for copy in copies:
        copy.wait()


def vmem_whole(shape):
    return pl.BlockSpec(shape, lambda *_: (0,) * len(shape))


def migrate(mixing_ratio, send_rows, migrant_count, arrival_slot, halo_blocks, block_size):
    species, parcels = mixing_ratio.shape
    capacity = send_rows.shape[-1]
    offsets = peer_offsets()
    peer_count = len(offsets)
    chunk = 1024
    wanted = send_rows[0].reshape(1, -1)
    outgoing = pl.pallas_call(
        functools.partial(pick_kernel, chunk),
        grid=(1,),
        in_specs=[vmem_whole(mixing_ratio.shape), vmem_whole(wanted.shape)],
        out_specs=[vmem_whole((species, capacity))] * peer_count,
        out_shape=[jax.ShapeDtypeStruct((species, capacity), mixing_ratio.dtype)] * peer_count,
    )(mixing_ratio, wanted)
    arrived = []
    for column in range(peer_count):
        opposite = peer_count - 1 - column
        arrived.append(from_behind(outgoing[opposite], "region", -offsets[column]))
    lane_index = jnp.arange(capacity, dtype=jnp.int32)
    live_lane = lane_index[None, :] < migrant_count[0][:, None]
    slots = jnp.where(live_lane, arrival_slot[0], parcels).reshape(-1, 1)
    sides, listed = halo_blocks.shape[1:]
    halo_shape = (species, listed * block_size)
    grid_spec = pltpu.PrefetchScalarGridSpec(
        num_scalar_prefetch=1,
        grid=(1,),
        in_specs=[vmem_whole(mixing_ratio.shape)]
        + [vmem_whole((species, capacity))] * peer_count
        + [vmem_whole(slots.shape)],
        out_specs=[vmem_whole(mixing_ratio.shape), vmem_whole(halo_shape), vmem_whole(halo_shape)],
        scratch_shapes=[pltpu.SemaphoreType.DMA((sides, listed))],
    )
    migrated, to_lower, to_upper = pl.pallas_call(
        functools.partial(place_kernel, chunk, block_size, peer_count),
        grid_spec=grid_spec,
        out_shape=[
            jax.ShapeDtypeStruct(mixing_ratio.shape, mixing_ratio.dtype),
            jax.ShapeDtypeStruct(halo_shape, mixing_ratio.dtype),
            jax.ShapeDtypeStruct(halo_shape, mixing_ratio.dtype),
        ],
    )(halo_blocks[0], mixing_ratio, *arrived, slots)
    from_lower = from_behind(to_upper, "region", 1)
    from_upper = from_behind(to_lower, "region", -1)
    return migrated, from_lower, from_upper


def split3(x):
    high = x.astype(jnp.bfloat16)
    low = (x - high.astype(jnp.float32)).astype(jnp.bfloat16)
    return high, low


def dot3(a_high, a_low, b_high, b_low):
    f32 = jnp.float32
    total = jnp.dot(a_high, b_high, preferred_element_type=f32)
    total = total + jnp.dot(a_high, b_low, preferred_element_type=f32)
    return total + jnp.dot(a_low, b_high, preferred_element_type=f32)


def mix_react_kernel(
    tile_blocks,
    neighbours,
    block_size,
    nb_ref,
    own_ref,
    weight_ref,
    temp_ref,
    order_ref,
    rate_terms_ref,
    prod_ref,
    loss_ref,
    migrated_hbm,
    lower_hbm,
    upper_hbm,
    out_ref,
    picked,
    sems,
    mixed_ref,
    order_split,
    gain_split,
    gain_high,
):
    f32 = jnp.float32
    step = pl.program_id(0)
    steps = pl.num_programs(0)
    own_count = migrated_hbm.shape[1] // block_size
    halo_count = lower_hbm.shape[1] // block_size

    def fetch(at, slot, start):
        for t in range(tile_blocks):
            for k in range(neighbours):
                index = nb_ref[at * tile_blocks + t, k]
                target = picked.at[slot, t * neighbours + k]
                sem = sems.at[slot, t * neighbours + k]
                if not start:
                    pltpu.make_async_copy(
                        migrated_hbm.at[:, pl.ds(0, block_size)], target, sem
                    ).wait()
                    continue
                sources = (
                    (migrated_hbm, index, index < own_count),
                    (lower_hbm, index - own_count,
                     (index >= own_count) & (index < own_count + halo_count)),
                    (upper_hbm, index - own_count - halo_count,
                     index >= own_count + halo_count),
                )
                for source, local, chosen in sources:
                    limit = source.shape[1] // block_size - 1
                    local = jnp.minimum(jnp.maximum(local, 0), limit)

                    @pl.when(chosen)
                    def _():
                        begin = pl.multiple_of(local * block_size, block_size)
                        pltpu.make_async_copy(
                            source.at[:, pl.ds(begin, block_size)], target, sem
                        ).start()

    @pl.when(step == 0)
    def _():
        fetch(0, 0, True)
        order_high, order_low = split3(order_ref[...])
        reactions = order_high.shape[0]
        order_split[0:reactions] = order_high
        order_split[reactions:] = order_low
        gain_split[...] = jnp.zeros_like(gain_split)
        rows = prod_ref.shape[0]
        for part, source in enumerate((prod_ref, loss_ref)):
            high, low = split3(source[...])
            gain_split[pl.ds(2 * part * PAD_ROWS, rows)] = high
            gain_split[pl.ds((2 * part + 1) * PAD_ROWS, rows)] = low
            gain_high[pl.ds(part * PAD_ROWS, rows)] = high
        gain_high[...] = jnp.where(
            lax.broadcasted_iota(jnp.int32, gain_high.shape, 0) % PAD_ROWS < rows,
            gain_high[...],
            jnp.zeros_like(gain_high),
        )

    slot = step % 2

    @pl.when(step + 1 < steps)
    def _():
        fetch(step + 1, 1 - slot, True)

    fetch(step, slot, False)

    for t in range(tile_blocks):
        lanes = slice(t * block_size, (t + 1) * block_size)
        stacked = jnp.concatenate(
            [own_ref[:, lanes]] + [picked[slot, t * neighbours + k] for k in range(neighbours)],
            axis=1,
        )
        weight = weight_ref[t].reshape((neighbours + 1) * block_size, block_size)
        mixed_ref[:, lanes] = jnp.dot(stacked, weight, preferred_element_type=f32)
    mixed = mixed_ref[...]
    species = mixed.shape[0]
    log_high, log_low = split3(jnp.log(mixed))
    reactions = order_split.shape[0] // 2
    both = jnp.dot(order_split[...], log_high, preferred_element_type=f32)
    exponent = both[:reactions] + both[reactions:]
    exponent = exponent + jnp.dot(order_split[0:reactions], log_low, preferred_element_type=f32)
    prefactor = rate_terms_ref[:, 0:1]
    energy = rate_terms_ref[:, 1:2]
    rate = jnp.exp(prefactor - energy * temp_ref[...] + exponent)
    rate_high, rate_low = split3(rate)
    by_high = jnp.dot(gain_split[...], rate_high, preferred_element_type=f32)
    by_low = jnp.dot(gain_high[...], rate_low, preferred_element_type=f32)
    gained = by_high[0:species] + by_high[PAD_ROWS:PAD_ROWS + species] + by_low[0:species]
    lost_mass = (
        by_high[2 * PAD_ROWS:2 * PAD_ROWS + species]
        + by_high[3 * PAD_ROWS:3 * PAD_ROWS + species]
        + by_low[PAD_ROWS:PAD_ROWS + species]
    )
    out_ref[...] = (mixed + gained) / (1.0 + lost_mass / mixed)


def mix_react(
    migrated,
    from_lower,
    from_upper,
    neighbour_block,
    mix_weight,
    inverse_temp,
    reactant_order,
    log_prefactor,
    activation_energy,
    production,
    loss_coefficient,
):
    species = migrated.shape[0]
    count_blocks, _, block_size, _ = mix_weight.shape
    neighbours = neighbour_block.shape[1]
    reactions = reactant_order.shape[0]
    tile_blocks = TILE_BLOCKS
    width = tile_blocks * block_size
    steps = count_blocks // tile_blocks

    def whole(shape):
        return pl.BlockSpec(shape, lambda i, nb: (0,) * len(shape))

    in_specs = [
        pl.BlockSpec((species, width), lambda i, nb: (0, i)),
        pl.BlockSpec((tile_blocks,) + mix_weight.shape[1:], lambda i, nb: (i, 0, 0, 0)),
        pl.BlockSpec((1, width), lambda i, nb: (0, i)),
        whole(reactant_order.shape),
        whole((reactions, 2)),
        whole(production.shape),
        whole(loss_coefficient.shape),
        pl.BlockSpec(memory_space=pl.ANY),
        pl.BlockSpec(memory_space=pl.ANY),
        pl.BlockSpec(memory_space=pl.ANY),
    ]
    bf16 = jnp.bfloat16
    grid_spec = pltpu.PrefetchScalarGridSpec(
        num_scalar_prefetch=1,
        grid=(steps,),
        in_specs=in_specs,
        out_specs=pl.BlockSpec((species, width), lambda i, nb: (0, i)),
        scratch_shapes=[
            pltpu.VMEM((2, tile_blocks * neighbours, species, block_size), bf16),
            pltpu.SemaphoreType.DMA((2, tile_blocks * neighbours)),
            pltpu.VMEM((species, width), jnp.float32),
            pltpu.VMEM((2 * reactions, species), bf16),
            pltpu.VMEM((4 * PAD_ROWS, reactions), bf16),
            pltpu.VMEM((2 * PAD_ROWS, reactions), bf16),
        ],
    )
    kernel = functools.partial(mix_react_kernel, tile_blocks, neighbours, block_size)
    return pl.pallas_call(
        kernel,
        grid_spec=grid_spec,
        out_shape=jax.ShapeDtypeStruct((species, count_blocks * block_size), jnp.float32),
        compiler_params=pltpu.CompilerParams(dimension_semantics=("arbitrary",)),
    )(
        neighbour_block,
        migrated,
        mix_weight,
        inverse_temp.reshape(1, -1),
        reactant_order,
        jnp.stack([log_prefactor, activation_energy], axis=1),
        production,
        loss_coefficient,
        migrated,
        from_lower,
        from_upper,
    )


def shards(
    mixing_ratio,
    send_rows,
    migrant_count,
    arrival_slot,
    halo_blocks,
    neighbour_block,
    mix_weight,
    inverse_temp,
    reactant_order,
    log_prefactor,
    activation_energy,
    production,
    loss_coefficient,
):
    migrated, from_lower, from_upper = migrate(
        mixing_ratio, send_rows, migrant_count, arrival_slot, halo_blocks, mix_weight.shape[-1]
    )
    return mix_react(
        migrated,
        from_lower,
        from_upper,
        neighbour_block,
        mix_weight,
        inverse_temp,
        reactant_order,
        log_prefactor,
        activation_energy,
        production,
        loss_coefficient,
    )


def solution(mesh):
    placed = (
        P(None, "region"),
        P("region", None, None),
        P("region", None),
        P("region", None, None),
        P("region", None, None),
        P("region", None),
        P("region", None, None, None),
        P("region"),
        P(),
        P(),
        P(),
        P(),
        P(),
    )
    return jax.shard_map(
        shards, mesh=mesh, in_specs=placed, out_specs=P(None, "region"), check_vma=False
    )
```

```python
import functools

import jax
import jax.numpy as jnp
from jax import lax
from jax.experimental import pallas as pl
from jax.experimental.pallas import tpu as pltpu
from jax.sharding import PartitionSpec as P

HOP = 4
TILE_BLOCKS = 8
PAD_ROWS = 160


def from_behind(block, axis, distance):
    devices = range(lax.axis_size(axis))
    route = [((i - distance) % len(devices), i) for i in devices]
    return lax.ppermute(block, axis, route)


def peer_offsets():
    return [column - HOP if column < HOP else column - HOP + 1 for column in range(2 * HOP)]


def pick_kernel(chunk, mixing_ref, rows_ref, *out_refs):
    species, parcels = mixing_ref.shape
    wanted = rows_ref[...]
    total = jnp.zeros((species, wanted.shape[1]), jnp.float32)
    for part in range(parcels // chunk):
        position = lax.broadcasted_iota(jnp.int32, (chunk, wanted.shape[1]), 0) + part * chunk
        pick = (position == wanted).astype(jnp.bfloat16)
        total = total + jnp.dot(
            mixing_ref[:, part * chunk:(part + 1) * chunk], pick, preferred_element_type=jnp.float32
        )
    width = out_refs[0].shape[1]
    for column, out_ref in enumerate(out_refs):
        out_ref[...] = total[:, column * width:(column + 1) * width].astype(out_ref.dtype)


def marked_arrivals(received_refs, rows):
    received = jnp.concatenate([ref[...] for ref in received_refs], axis=1)
    species = received.shape[0]
    pad = (-species) % 16 or 16
    return jnp.concatenate([received, jnp.ones((pad, rows), received.dtype)], axis=0)


def place_kernel(chunk, peer_count, mixing_ref, *refs):
    received_refs = refs[:peer_count]
    slots_ref, migrated_ref = refs[peer_count:]
    species, parcels = mixing_ref.shape
    slots = slots_ref[...]
    marked = marked_arrivals(received_refs, slots.shape[0])
    for part in range(parcels // chunk):
        lanes = slice(part * chunk, (part + 1) * chunk)
        position = lax.broadcasted_iota(jnp.int32, (slots.shape[0], chunk), 1) + part * chunk
        place = (position == slots).astype(jnp.bfloat16)
        placed = jnp.dot(marked, place, preferred_element_type=jnp.float32)
        hit = placed[species:species + 1]
        migrated_ref[:, lanes] = jnp.where(
            hit > 0.5, placed[:species].astype(migrated_ref.dtype), mixing_ref[:, lanes]
        )


def halo_kernel(chunk, block_size, peer_count, halo_ref, mixing_ref, *refs):
    received_refs = refs[:peer_count]
    slots_ref, lower_ref, upper_ref, sems = refs[peer_count:]
    species = mixing_ref.shape[0]
    sides, listed = halo_ref.shape
    outs = (lower_ref, upper_ref)
    copies = []
    for side in range(sides):
        for j in range(listed):
            start = pl.multiple_of(halo_ref[side, j] * block_size, block_size)
            copy = pltpu.make_async_copy(
                mixing_ref.at[:, pl.ds(start, block_size)],
                outs[side].at[:, pl.ds(j * block_size, block_size)],
                sems.at[side, j],
            )
            copy.start()
            copies.append(copy)
    slots = slots_ref[...]
    marked = marked_arrivals(received_refs, slots.shape[0])
    lane = lax.broadcasted_iota(jnp.int32, (1, block_size), 1)
    per_chunk = chunk // block_size
    for copy in copies:
        copy.wait()
    for side in range(sides):
        for part in range(listed // per_chunk):
            first = part * per_chunk
            where_to = jnp.concatenate(
                [lane + halo_ref[side, j] * block_size for j in range(first, first + per_chunk)],
                axis=1,
            )
            place = (where_to == slots).astype(jnp.bfloat16)
            placed = jnp.dot(marked, place, preferred_element_type=jnp.float32)
            hit = placed[species:species + 1]
            lanes = slice(first * block_size, (first + per_chunk) * block_size)
            outs[side][:, lanes] = jnp.where(
                hit > 0.5, placed[:species].astype(outs[side].dtype), outs[side][:, lanes]
            )


def vmem_whole(shape):
    return pl.BlockSpec(shape, lambda *_: (0,) * len(shape))


def migrate(mixing_ratio, send_rows, migrant_count, arrival_slot, halo_blocks, block_size):
    species, parcels = mixing_ratio.shape
    capacity = send_rows.shape[-1]
    offsets = peer_offsets()
    peer_count = len(offsets)
    chunk = 1024
    wanted = send_rows[0].reshape(1, -1)
    outgoing = pl.pallas_call(
        functools.partial(pick_kernel, chunk),
        grid=(1,),
        in_specs=[vmem_whole(mixing_ratio.shape), vmem_whole(wanted.shape)],
        out_specs=[vmem_whole((species, capacity))] * peer_count,
        out_shape=[jax.ShapeDtypeStruct((species, capacity), mixing_ratio.dtype)] * peer_count,
    )(mixing_ratio, wanted)
    arrived = []
    for column in range(peer_count):
        opposite = peer_count - 1 - column
        arrived.append(from_behind(outgoing[opposite], "region", -offsets[column]))
    lane_index = jnp.arange(capacity, dtype=jnp.int32)
    live_lane = lane_index[None, :] < migrant_count[0][:, None]
    slots = jnp.where(live_lane, arrival_slot[0], parcels).reshape(-1, 1)
    sides, listed = halo_blocks.shape[1:]
    halo_shape = (species, listed * block_size)
    grid_spec = pltpu.PrefetchScalarGridSpec(
        num_scalar_prefetch=1,
        grid=(1,),
        in_specs=[vmem_whole(mixing_ratio.shape)]
        + [vmem_whole((species, capacity))] * peer_count
        + [vmem_whole(slots.shape)],
        out_specs=[vmem_whole(halo_shape), vmem_whole(halo_shape)],
        scratch_shapes=[pltpu.SemaphoreType.DMA((sides, listed))],
    )
    to_lower, to_upper = pl.pallas_call(
        functools.partial(halo_kernel, chunk, block_size, peer_count),
        grid_spec=grid_spec,
        out_shape=[jax.ShapeDtypeStruct(halo_shape, mixing_ratio.dtype)] * sides,
    )(halo_blocks[0], mixing_ratio, *arrived, slots)
    migrated = pl.pallas_call(
        functools.partial(place_kernel, chunk, peer_count),
        grid=(1,),
        in_specs=[vmem_whole(mixing_ratio.shape)]
        + [vmem_whole((species, capacity))] * peer_count
        + [vmem_whole(slots.shape)],
        out_specs=vmem_whole(mixing_ratio.shape),
        out_shape=jax.ShapeDtypeStruct(mixing_ratio.shape, mixing_ratio.dtype),
    )(mixing_ratio, *arrived, slots)
    from_lower = from_behind(to_upper, "region", 1)
    from_upper = from_behind(to_lower, "region", -1)
    return migrated, from_lower, from_upper


def split3(x):
    high = x.astype(jnp.bfloat16)
    low = (x - high.astype(jnp.float32)).astype(jnp.bfloat16)
    return high, low


def dot3(a_high, a_low, b_high, b_low):
    f32 = jnp.float32
    total = jnp.dot(a_high, b_high, preferred_element_type=f32)
    total = total + jnp.dot(a_high, b_low, preferred_element_type=f32)
    return total + jnp.dot(a_low, b_high, preferred_element_type=f32)


def mix_react_kernel(
    tile_blocks,
    neighbours,
    block_size,
    nb_ref,
    own_ref,
    weight_ref,
    temp_ref,
    order_ref,
    rate_terms_ref,
    prod_ref,
    loss_ref,
    migrated_hbm,
    lower_hbm,
    upper_hbm,
    out_ref,
    picked,
    sems,
    mixed_ref,
    order_split,
    gain_split,
    gain_high,
):
    f32 = jnp.float32
    step = pl.program_id(0)
    steps = pl.num_programs(0)
    own_count = migrated_hbm.shape[1] // block_size
    halo_count = lower_hbm.shape[1] // block_size

    def fetch(at, slot, start):
        for t in range(tile_blocks):
            for k in range(neighbours):
                index = nb_ref[at * tile_blocks + t, k]
                target = picked.at[slot, t * neighbours + k]
                sem = sems.at[slot, t * neighbours + k]
                if not start:
                    pltpu.make_async_copy(
                        migrated_hbm.at[:, pl.ds(0, block_size)], target, sem
                    ).wait()
                    continue
                sources = (
                    (migrated_hbm, index, index < own_count),
                    (lower_hbm, index - own_count,
                     (index >= own_count) & (index < own_count + halo_count)),
                    (upper_hbm, index - own_count - halo_count,
                     index >= own_count + halo_count),
                )
                for source, local, chosen in sources:
                    limit = source.shape[1] // block_size - 1
                    local = jnp.minimum(jnp.maximum(local, 0), limit)

                    @pl.when(chosen)
                    def _():
                        begin = pl.multiple_of(local * block_size, block_size)
                        pltpu.make_async_copy(
                            source.at[:, pl.ds(begin, block_size)], target, sem
                        ).start()

    @pl.when(step == 0)
    def _():
        fetch(0, 0, True)
        order_high, order_low = split3(order_ref[...])
        reactions = order_high.shape[0]
        order_split[0:reactions] = order_high
        order_split[reactions:] = order_low
        gain_split[...] = jnp.zeros_like(gain_split)
        rows = prod_ref.shape[0]
        for part, source in enumerate((prod_ref, loss_ref)):
            high, low = split3(source[...])
            gain_split[pl.ds(2 * part * PAD_ROWS, rows)] = high
            gain_split[pl.ds((2 * part + 1) * PAD_ROWS, rows)] = low
            gain_high[pl.ds(part * PAD_ROWS, rows)] = high
        gain_high[...] = jnp.where(
            lax.broadcasted_iota(jnp.int32, gain_high.shape, 0) % PAD_ROWS < rows,
            gain_high[...],
            jnp.zeros_like(gain_high),
        )

    slot = step % 2

    @pl.when(step + 1 < steps)
    def _():
        fetch(step + 1, 1 - slot, True)

    fetch(step, slot, False)

    for t in range(tile_blocks):
        lanes = slice(t * block_size, (t + 1) * block_size)
        stacked = jnp.concatenate(
            [own_ref[:, lanes]] + [picked[slot, t * neighbours + k] for k in range(neighbours)],
            axis=1,
        )
        weight = weight_ref[t].reshape((neighbours + 1) * block_size, block_size)
        mixed_ref[:, lanes] = jnp.dot(stacked, weight, preferred_element_type=f32)
    mixed = mixed_ref[...]
    species = mixed.shape[0]
    log_high, log_low = split3(jnp.log(mixed))
    reactions = order_split.shape[0] // 2
    both = jnp.dot(order_split[...], log_high, preferred_element_type=f32)
    exponent = both[:reactions] + both[reactions:]
    exponent = exponent + jnp.dot(order_split[0:reactions], log_low, preferred_element_type=f32)
    prefactor = rate_terms_ref[:, 0:1]
    energy = rate_terms_ref[:, 1:2]
    rate = jnp.exp(prefactor - energy * temp_ref[...] + exponent)
    rate_high, rate_low = split3(rate)
    by_high = jnp.dot(gain_split[...], rate_high, preferred_element_type=f32)
    by_low = jnp.dot(gain_high[...], rate_low, preferred_element_type=f32)
    gained = by_high[0:species] + by_high[PAD_ROWS:PAD_ROWS + species] + by_low[0:species]
    lost_mass = (
        by_high[2 * PAD_ROWS:2 * PAD_ROWS + species]
        + by_high[3 * PAD_ROWS:3 * PAD_ROWS + species]
        + by_low[PAD_ROWS:PAD_ROWS + species]
    )
    out_ref[...] = (mixed + gained) / (1.0 + lost_mass / mixed)


def mix_react(
    migrated,
    from_lower,
    from_upper,
    neighbour_block,
    mix_weight,
    inverse_temp,
    reactant_order,
    log_prefactor,
    activation_energy,
    production,
    loss_coefficient,
):
    species = migrated.shape[0]
    count_blocks, _, block_size, _ = mix_weight.shape
    neighbours = neighbour_block.shape[1]
    reactions = reactant_order.shape[0]
    tile_blocks = TILE_BLOCKS
    width = tile_blocks * block_size
    steps = count_blocks // tile_blocks

    def whole(shape):
        return pl.BlockSpec(shape, lambda i, nb: (0,) * len(shape))

    in_specs = [
        pl.BlockSpec((species, width), lambda i, nb: (0, i)),
        pl.BlockSpec((tile_blocks,) + mix_weight.shape[1:], lambda i, nb: (i, 0, 0, 0)),
        pl.BlockSpec((1, width), lambda i, nb: (0, i)),
        whole(reactant_order.shape),
        whole((reactions, 2)),
        whole(production.shape),
        whole(loss_coefficient.shape),
        pl.BlockSpec(memory_space=pl.ANY),
        pl.BlockSpec(memory_space=pl.ANY),
        pl.BlockSpec(memory_space=pl.ANY),
    ]
    bf16 = jnp.bfloat16
    grid_spec = pltpu.PrefetchScalarGridSpec(
        num_scalar_prefetch=1,
        grid=(steps,),
        in_specs=in_specs,
        out_specs=pl.BlockSpec((species, width), lambda i, nb: (0, i)),
        scratch_shapes=[
            pltpu.VMEM((2, tile_blocks * neighbours, species, block_size), bf16),
            pltpu.SemaphoreType.DMA((2, tile_blocks * neighbours)),
            pltpu.VMEM((species, width), jnp.float32),
            pltpu.VMEM((2 * reactions, species), bf16),
            pltpu.VMEM((4 * PAD_ROWS, reactions), bf16),
            pltpu.VMEM((2 * PAD_ROWS, reactions), bf16),
        ],
    )
    kernel = functools.partial(mix_react_kernel, tile_blocks, neighbours, block_size)
    return pl.pallas_call(
        kernel,
        grid_spec=grid_spec,
        out_shape=jax.ShapeDtypeStruct((species, count_blocks * block_size), jnp.float32),
        compiler_params=pltpu.CompilerParams(dimension_semantics=("arbitrary",)),
    )(
        neighbour_block,
        migrated,
        mix_weight,
        inverse_temp.reshape(1, -1),
        reactant_order,
        jnp.stack([log_prefactor, activation_energy], axis=1),
        production,
        loss_coefficient,
        migrated,
        from_lower,
        from_upper,
    )


def shards(
    mixing_ratio,
    send_rows,
    migrant_count,
    arrival_slot,
    halo_blocks,
    neighbour_block,
    mix_weight,
    inverse_temp,
    reactant_order,
    log_prefactor,
    activation_energy,
    production,
    loss_coefficient,
):
    migrated, from_lower, from_upper = migrate(
        mixing_ratio, send_rows, migrant_count, arrival_slot, halo_blocks, mix_weight.shape[-1]
    )
    return mix_react(
        migrated,
        from_lower,
        from_upper,
        neighbour_block,
        mix_weight,
        inverse_temp,
        reactant_order,
        log_prefactor,
        activation_energy,
        production,
        loss_coefficient,
    )


def solution(mesh):
    placed = (
        P(None, "region"),
        P("region", None, None),
        P("region", None),
        P("region", None, None),
        P("region", None, None),
        P("region", None),
        P("region", None, None, None),
        P("region"),
        P(),
        P(),
        P(),
        P(),
        P(),
    )
    return jax.shard_map(
        shards, mesh=mesh, in_specs=placed, out_specs=P(None, "region"), check_vma=False
    )
```

```python
import functools

import jax
import jax.numpy as jnp
from jax import lax
from jax.experimental import pallas as pl
from jax.experimental.pallas import tpu as pltpu
from jax.sharding import PartitionSpec as P

HOP = 4
TILE_BLOCKS = 8
PAD_ROWS = 160


def from_behind(block, axis, distance):
    devices = range(lax.axis_size(axis))
    route = [((i - distance) % len(devices), i) for i in devices]
    return lax.ppermute(block, axis, route)


def peer_offsets():
    return [column - HOP if column < HOP else column - HOP + 1 for column in range(2 * HOP)]


def pick_kernel(chunk, mixing_ref, rows_ref, *out_refs):
    species, parcels = mixing_ref.shape
    wanted = rows_ref[...]
    total = jnp.zeros((species, wanted.shape[1]), jnp.float32)
    for part in range(parcels // chunk):
        position = lax.broadcasted_iota(jnp.int32, (chunk, wanted.shape[1]), 0) + part * chunk
        pick = (position == wanted).astype(jnp.bfloat16)
        total = total + jnp.dot(
            mixing_ref[:, part * chunk:(part + 1) * chunk], pick, preferred_element_type=jnp.float32
        )
    width = out_refs[0].shape[1]
    for column, out_ref in enumerate(out_refs):
        out_ref[...] = total[:, column * width:(column + 1) * width].astype(out_ref.dtype)


def marked_arrivals(received_refs, rows):
    received = jnp.concatenate([ref[...] for ref in received_refs], axis=1)
    species = received.shape[0]
    pad = (-species) % 16 or 16
    return jnp.concatenate([received, jnp.ones((pad, rows), received.dtype)], axis=0)


def place_kernel(chunk, peer_count, mixing_ref, *refs):
    received_refs = refs[:peer_count]
    slots_ref, migrated_ref = refs[peer_count:]
    species, parcels = mixing_ref.shape
    slots = slots_ref[...]
    marked = marked_arrivals(received_refs, slots.shape[0])
    for part in range(parcels // chunk):
        lanes = slice(part * chunk, (part + 1) * chunk)
        position = lax.broadcasted_iota(jnp.int32, (slots.shape[0], chunk), 1) + part * chunk
        place = (position == slots).astype(jnp.bfloat16)
        placed = jnp.dot(marked, place, preferred_element_type=jnp.float32)
        hit = placed[species:species + 1]
        migrated_ref[:, lanes] = jnp.where(
            hit > 0.5, placed[:species].astype(migrated_ref.dtype), mixing_ref[:, lanes]
        )


def halo_kernel(chunk, block_size, peer_count, halo_ref, mixing_ref, *refs):
    received_refs = refs[:peer_count]
    slots_ref, lower_ref, upper_ref, sems = refs[peer_count:]
    species = mixing_ref.shape[0]
    sides, listed = halo_ref.shape
    outs = (lower_ref, upper_ref)
    copies = []
    for side in range(sides):
        for j in range(listed):
            start = pl.multiple_of(halo_ref[side, j] * block_size, block_size)
            copy = pltpu.make_async_copy(
                mixing_ref.at[:, pl.ds(start, block_size)],
                outs[side].at[:, pl.ds(j * block_size, block_size)],
                sems.at[side, j],
            )
            copy.start()
            copies.append(copy)
    slots = slots_ref[...]
    marked = marked_arrivals(received_refs, slots.shape[0])
    lane = lax.broadcasted_iota(jnp.int32, (1, block_size), 1)
    per_chunk = chunk // block_size
    for copy in copies:
        copy.wait()
    for side in range(sides):
        for part in range(listed // per_chunk):
            first = part * per_chunk
            where_to = jnp.concatenate(
                [lane + halo_ref[side, j] * block_size for j in range(first, first + per_chunk)],
                axis=1,
            )
            place = (where_to == slots).astype(jnp.bfloat16)
            placed = jnp.dot(marked, place, preferred_element_type=jnp.float32)
            hit = placed[species:species + 1]
            lanes = slice(first * block_size, (first + per_chunk) * block_size)
            outs[side][:, lanes] = jnp.where(
                hit > 0.5, placed[:species].astype(outs[side].dtype), outs[side][:, lanes]
            )


def vmem_whole(shape):
    return pl.BlockSpec(shape, lambda *_: (0,) * len(shape))


def migrate(mixing_ratio, send_rows, migrant_count, arrival_slot, halo_blocks, block_size):
    species, parcels = mixing_ratio.shape
    capacity = send_rows.shape[-1]
    offsets = peer_offsets()
    peer_count = len(offsets)
    chunk = 1024
    wanted = send_rows[0].reshape(1, -1)
    outgoing = pl.pallas_call(
        functools.partial(pick_kernel, chunk),
        grid=(1,),
        in_specs=[vmem_whole(mixing_ratio.shape), vmem_whole(wanted.shape)],
        out_specs=[vmem_whole((species, capacity))] * peer_count,
        out_shape=[jax.ShapeDtypeStruct((species, capacity), mixing_ratio.dtype)] * peer_count,
    )(mixing_ratio, wanted)
    arrived = []
    for column in range(peer_count):
        opposite = peer_count - 1 - column
        arrived.append(from_behind(outgoing[opposite], "region", -offsets[column]))
    lane_index = jnp.arange(capacity, dtype=jnp.int32)
    live_lane = lane_index[None, :] < migrant_count[0][:, None]
    slots = jnp.where(live_lane, arrival_slot[0], parcels).reshape(-1, 1)
    sides, listed = halo_blocks.shape[1:]
    halo_shape = (species, listed * block_size)
    grid_spec = pltpu.PrefetchScalarGridSpec(
        num_scalar_prefetch=1,
        grid=(1,),
        in_specs=[pl.BlockSpec(memory_space=pl.ANY)]
        + [vmem_whole((species, capacity))] * peer_count
        + [vmem_whole(slots.shape)],
        out_specs=[vmem_whole(halo_shape), vmem_whole(halo_shape)],
        scratch_shapes=[pltpu.SemaphoreType.DMA((sides, listed))],
    )
    to_lower, to_upper = pl.pallas_call(
        functools.partial(halo_kernel, chunk, block_size, peer_count),
        grid_spec=grid_spec,
        out_shape=[jax.ShapeDtypeStruct(halo_shape, mixing_ratio.dtype)] * sides,
    )(halo_blocks[0], mixing_ratio, *arrived, slots)
    migrated = pl.pallas_call(
        functools.partial(place_kernel, chunk, peer_count),
        grid=(1,),
        in_specs=[vmem_whole(mixing_ratio.shape)]
        + [vmem_whole((species, capacity))] * peer_count
        + [vmem_whole(slots.shape)],
        out_specs=vmem_whole(mixing_ratio.shape),
        out_shape=jax.ShapeDtypeStruct(mixing_ratio.shape, mixing_ratio.dtype),
    )(mixing_ratio, *arrived, slots)
    from_lower = from_behind(to_upper, "region", 1)
    from_upper = from_behind(to_lower, "region", -1)
    return migrated, from_lower, from_upper


def split3(x):
    high = x.astype(jnp.bfloat16)
    low = (x - high.astype(jnp.float32)).astype(jnp.bfloat16)
    return high, low


def dot3(a_high, a_low, b_high, b_low):
    f32 = jnp.float32
    total = jnp.dot(a_high, b_high, preferred_element_type=f32)
    total = total + jnp.dot(a_high, b_low, preferred_element_type=f32)
    return total + jnp.dot(a_low, b_high, preferred_element_type=f32)


def mix_react_kernel(
    tile_blocks,
    neighbours,
    block_size,
    nb_ref,
    own_ref,
    weight_ref,
    temp_ref,
    order_ref,
    rate_terms_ref,
    prod_ref,
    loss_ref,
    migrated_hbm,
    lower_hbm,
    upper_hbm,
    out_ref,
    picked,
    sems,
    mixed_ref,
    order_split,
    gain_split,
    gain_high,
):
    f32 = jnp.float32
    step = pl.program_id(0)
    steps = pl.num_programs(0)
    own_count = migrated_hbm.shape[1] // block_size
    halo_count = lower_hbm.shape[1] // block_size

    def fetch(at, slot, start):
        for t in range(tile_blocks):
            for k in range(neighbours):
                index = nb_ref[at * tile_blocks + t, k]
                target = picked.at[slot, t * neighbours + k]
                sem = sems.at[slot, t * neighbours + k]
                if not start:
                    pltpu.make_async_copy(
                        migrated_hbm.at[:, pl.ds(0, block_size)], target, sem
                    ).wait()
                    continue
                sources = (
                    (migrated_hbm, index, index < own_count),
                    (lower_hbm, index - own_count,
                     (index >= own_count) & (index < own_count + halo_count)),
                    (upper_hbm, index - own_count - halo_count,
                     index >= own_count + halo_count),
                )
                for source, local, chosen in sources:
                    limit = source.shape[1] // block_size - 1
                    local = jnp.minimum(jnp.maximum(local, 0), limit)

                    @pl.when(chosen)
                    def _():
                        begin = pl.multiple_of(local * block_size, block_size)
                        pltpu.make_async_copy(
                            source.at[:, pl.ds(begin, block_size)], target, sem
                        ).start()

    @pl.when(step == 0)
    def _():
        fetch(0, 0, True)
        order_high, order_low = split3(order_ref[...])
        reactions = order_high.shape[0]
        order_split[0:reactions] = order_high
        order_split[reactions:] = order_low
        gain_split[...] = jnp.zeros_like(gain_split)
        rows = prod_ref.shape[0]
        for part, source in enumerate((prod_ref, loss_ref)):
            high, low = split3(source[...])
            gain_split[pl.ds(2 * part * PAD_ROWS, rows)] = high
            gain_split[pl.ds((2 * part + 1) * PAD_ROWS, rows)] = low
            gain_high[pl.ds(part * PAD_ROWS, rows)] = high
        gain_high[...] = jnp.where(
            lax.broadcasted_iota(jnp.int32, gain_high.shape, 0) % PAD_ROWS < rows,
            gain_high[...],
            jnp.zeros_like(gain_high),
        )

    slot = step % 2

    @pl.when(step + 1 < steps)
    def _():
        fetch(step + 1, 1 - slot, True)

    fetch(step, slot, False)

    for t in range(tile_blocks):
        lanes = slice(t * block_size, (t + 1) * block_size)
        stacked = jnp.concatenate(
            [own_ref[:, lanes]] + [picked[slot, t * neighbours + k] for k in range(neighbours)],
            axis=1,
        )
        weight = weight_ref[t].reshape((neighbours + 1) * block_size, block_size)
        mixed_ref[:, lanes] = jnp.dot(stacked, weight, preferred_element_type=f32)
    mixed = mixed_ref[...]
    species = mixed.shape[0]
    log_high, log_low = split3(jnp.log(mixed))
    reactions = order_split.shape[0] // 2
    both = jnp.dot(order_split[...], log_high, preferred_element_type=f32)
    exponent = both[:reactions] + both[reactions:]
    exponent = exponent + jnp.dot(order_split[0:reactions], log_low, preferred_element_type=f32)
    prefactor = rate_terms_ref[:, 0:1]
    energy = rate_terms_ref[:, 1:2]
    rate = jnp.exp(prefactor - energy * temp_ref[...] + exponent)
    rate_high, rate_low = split3(rate)
    by_high = jnp.dot(gain_split[...], rate_high, preferred_element_type=f32)
    by_low = jnp.dot(gain_high[...], rate_low, preferred_element_type=f32)
    gained = by_high[0:species] + by_high[PAD_ROWS:PAD_ROWS + species] + by_low[0:species]
    lost_mass = (
        by_high[2 * PAD_ROWS:2 * PAD_ROWS + species]
        + by_high[3 * PAD_ROWS:3 * PAD_ROWS + species]
        + by_low[PAD_ROWS:PAD_ROWS + species]
    )
    out_ref[...] = (mixed + gained) / (1.0 + lost_mass / mixed)


def mix_react(
    migrated,
    from_lower,
    from_upper,
    neighbour_block,
    mix_weight,
    inverse_temp,
    reactant_order,
    log_prefactor,
    activation_energy,
    production,
    loss_coefficient,
):
    species = migrated.shape[0]
    count_blocks, _, block_size, _ = mix_weight.shape
    neighbours = neighbour_block.shape[1]
    reactions = reactant_order.shape[0]
    tile_blocks = TILE_BLOCKS
    width = tile_blocks * block_size
    steps = count_blocks // tile_blocks

    def whole(shape):
        return pl.BlockSpec(shape, lambda i, nb: (0,) * len(shape))

    in_specs = [
        pl.BlockSpec((species, width), lambda i, nb: (0, i)),
        pl.BlockSpec((tile_blocks,) + mix_weight.shape[1:], lambda i, nb: (i, 0, 0, 0)),
        pl.BlockSpec((1, width), lambda i, nb: (0, i)),
        whole(reactant_order.shape),
        whole((reactions, 2)),
        whole(production.shape),
        whole(loss_coefficient.shape),
        pl.BlockSpec(memory_space=pl.ANY),
        pl.BlockSpec(memory_space=pl.ANY),
        pl.BlockSpec(memory_space=pl.ANY),
    ]
    bf16 = jnp.bfloat16
    grid_spec = pltpu.PrefetchScalarGridSpec(
        num_scalar_prefetch=1,
        grid=(steps,),
        in_specs=in_specs,
        out_specs=pl.BlockSpec((species, width), lambda i, nb: (0, i)),
        scratch_shapes=[
            pltpu.VMEM((2, tile_blocks * neighbours, species, block_size), bf16),
            pltpu.SemaphoreType.DMA((2, tile_blocks * neighbours)),
            pltpu.VMEM((species, width), jnp.float32),
            pltpu.VMEM((2 * reactions, species), bf16),
            pltpu.VMEM((4 * PAD_ROWS, reactions), bf16),
            pltpu.VMEM((2 * PAD_ROWS, reactions), bf16),
        ],
    )
    kernel = functools.partial(mix_react_kernel, tile_blocks, neighbours, block_size)
    return pl.pallas_call(
        kernel,
        grid_spec=grid_spec,
        out_shape=jax.ShapeDtypeStruct((species, count_blocks * block_size), jnp.float32),
        compiler_params=pltpu.CompilerParams(dimension_semantics=("arbitrary",)),
    )(
        neighbour_block,
        migrated,
        mix_weight,
        inverse_temp.reshape(1, -1),
        reactant_order,
        jnp.stack([log_prefactor, activation_energy], axis=1),
        production,
        loss_coefficient,
        migrated,
        from_lower,
        from_upper,
    )


def shards(
    mixing_ratio,
    send_rows,
    migrant_count,
    arrival_slot,
    halo_blocks,
    neighbour_block,
    mix_weight,
    inverse_temp,
    reactant_order,
    log_prefactor,
    activation_energy,
    production,
    loss_coefficient,
):
    migrated, from_lower, from_upper = migrate(
        mixing_ratio, send_rows, migrant_count, arrival_slot, halo_blocks, mix_weight.shape[-1]
    )
    return mix_react(
        migrated,
        from_lower,
        from_upper,
        neighbour_block,
        mix_weight,
        inverse_temp,
        reactant_order,
        log_prefactor,
        activation_energy,
        production,
        loss_coefficient,
    )


def solution(mesh):
    placed = (
        P(None, "region"),
        P("region", None, None),
        P("region", None),
        P("region", None, None),
        P("region", None, None),
        P("region", None),
        P("region", None, None, None),
        P("region"),
        P(),
        P(),
        P(),
        P(),
        P(),
    )
    return jax.shard_map(
        shards, mesh=mesh, in_specs=placed, out_specs=P(None, "region"), check_vma=False
    )
```

```python
import functools

import jax
import jax.numpy as jnp
from jax import lax
from jax.experimental import pallas as pl
from jax.experimental.pallas import tpu as pltpu
from jax.sharding import PartitionSpec as P

HOP = 4
TILE_BLOCKS = 8
PAD_ROWS = 160


def from_behind(block, axis, distance):
    devices = range(lax.axis_size(axis))
    route = [((i - distance) % len(devices), i) for i in devices]
    return lax.ppermute(block, axis, route)


def peer_offsets():
    return [column - HOP if column < HOP else column - HOP + 1 for column in range(2 * HOP)]


def pick_kernel(chunk, mixing_ref, rows_ref, *out_refs):
    species, parcels = mixing_ref.shape
    wanted = rows_ref[...]
    total = jnp.zeros((species, wanted.shape[1]), jnp.float32)
    for part in range(parcels // chunk):
        position = lax.broadcasted_iota(jnp.int32, (chunk, wanted.shape[1]), 0) + part * chunk
        pick = (position == wanted).astype(jnp.bfloat16)
        total = total + jnp.dot(
            mixing_ref[:, part * chunk:(part + 1) * chunk], pick, preferred_element_type=jnp.float32
        )
    width = out_refs[0].shape[1]
    for column, out_ref in enumerate(out_refs):
        out_ref[...] = total[:, column * width:(column + 1) * width].astype(out_ref.dtype)


def marked_arrivals(received_refs, rows):
    received = jnp.concatenate([ref[...] for ref in received_refs], axis=1)
    species = received.shape[0]
    pad = (-species) % 16 or 16
    return jnp.concatenate([received, jnp.ones((pad, rows), received.dtype)], axis=0)


def place_kernel(chunk, peer_count, mixing_ref, *refs):
    received_refs = refs[:peer_count]
    slots_ref, migrated_ref = refs[peer_count:]
    species, parcels = mixing_ref.shape
    slots = slots_ref[...]
    marked = marked_arrivals(received_refs, slots.shape[0])
    for part in range(parcels // chunk):
        lanes = slice(part * chunk, (part + 1) * chunk)
        position = lax.broadcasted_iota(jnp.int32, (slots.shape[0], chunk), 1) + part * chunk
        place = (position == slots).astype(jnp.bfloat16)
        placed = jnp.dot(marked, place, preferred_element_type=jnp.float32)
        hit = placed[species:species + 1]
        migrated_ref[:, lanes] = jnp.where(
            hit > 0.5, placed[:species].astype(migrated_ref.dtype), mixing_ref[:, lanes]
        )


def halo_kernel(chunk, block_size, peer_count, halo_ref, mixing_ref, *refs):
    received_refs = refs[:peer_count]
    slots_ref, lower_ref, upper_ref, sems = refs[peer_count:]
    species = mixing_ref.shape[0]
    sides, listed = halo_ref.shape
    outs = (lower_ref, upper_ref)
    copies = []
    for side in range(sides):
        for j in range(listed):
            start = pl.multiple_of(halo_ref[side, j] * block_size, block_size)
            copy = pltpu.make_async_copy(
                mixing_ref.at[:, pl.ds(start, block_size)],
                outs[side].at[:, pl.ds(j * block_size, block_size)],
                sems.at[side, j],
            )
            copy.start()
            copies.append(copy)
    slots = slots_ref[...]
    marked = marked_arrivals(received_refs, slots.shape[0])
    lane = lax.broadcasted_iota(jnp.int32, (1, block_size), 1)
    per_chunk = chunk // block_size
    for copy in copies:
        copy.wait()
    for side in range(sides):
        for part in range(listed // per_chunk):
            first = part * per_chunk
            where_to = jnp.concatenate(
                [lane + halo_ref[side, j] * block_size for j in range(first, first + per_chunk)],
                axis=1,
            )
            place = (where_to == slots).astype(jnp.bfloat16)
            placed = jnp.dot(marked, place, preferred_element_type=jnp.float32)
            hit = placed[species:species + 1]
            lanes = slice(first * block_size, (first + per_chunk) * block_size)
            outs[side][:, lanes] = jnp.where(
                hit > 0.5, placed[:species].astype(outs[side].dtype), outs[side][:, lanes]
            )


def vmem_whole(shape):
    return pl.BlockSpec(shape, lambda *_: (0,) * len(shape))


def migrate(mixing_ratio, send_rows, migrant_count, arrival_slot, halo_blocks, block_size):
    species, parcels = mixing_ratio.shape
    capacity = send_rows.shape[-1]
    offsets = peer_offsets()
    peer_count = len(offsets)
    chunk = 1024
    wanted = send_rows[0].reshape(1, -1)
    outgoing = pl.pallas_call(
        functools.partial(pick_kernel, chunk),
        grid=(1,),
        in_specs=[vmem_whole(mixing_ratio.shape), vmem_whole(wanted.shape)],
        out_specs=[vmem_whole((species, capacity))] * peer_count,
        out_shape=[jax.ShapeDtypeStruct((species, capacity), mixing_ratio.dtype)] * peer_count,
    )(mixing_ratio, wanted)
    arrived = []
    for column in range(peer_count):
        opposite = peer_count - 1 - column
        arrived.append(from_behind(outgoing[opposite], "region", -offsets[column]))
    lane_index = jnp.arange(capacity, dtype=jnp.int32)
    live_lane = lane_index[None, :] < migrant_count[0][:, None]
    slots = jnp.where(live_lane, arrival_slot[0], parcels).reshape(-1, 1)
    sides, listed = halo_blocks.shape[1:]
    halo_shape = (species, listed * block_size)
    grid_spec = pltpu.PrefetchScalarGridSpec(
        num_scalar_prefetch=1,
        grid=(1,),
        in_specs=[pl.BlockSpec(memory_space=pl.ANY)]
        + [vmem_whole((species, capacity))] * peer_count
        + [vmem_whole(slots.shape)],
        out_specs=[vmem_whole(halo_shape), vmem_whole(halo_shape)],
        scratch_shapes=[pltpu.SemaphoreType.DMA((sides, listed))],
    )
    to_lower, to_upper = pl.pallas_call(
        functools.partial(halo_kernel, chunk, block_size, peer_count),
        grid_spec=grid_spec,
        out_shape=[jax.ShapeDtypeStruct(halo_shape, mixing_ratio.dtype)] * sides,
    )(halo_blocks[0], mixing_ratio, *arrived, slots)
    migrated = pl.pallas_call(
        functools.partial(place_kernel, chunk, peer_count),
        grid=(1,),
        in_specs=[vmem_whole(mixing_ratio.shape)]
        + [vmem_whole((species, capacity))] * peer_count
        + [vmem_whole(slots.shape)],
        out_specs=vmem_whole(mixing_ratio.shape),
        out_shape=jax.ShapeDtypeStruct(mixing_ratio.shape, mixing_ratio.dtype),
    )(mixing_ratio, *arrived, slots)
    from_lower = from_behind(to_upper, "region", 1)
    from_upper = from_behind(to_lower, "region", -1)
    return migrated, from_lower, from_upper


def split3(x):
    high = x.astype(jnp.bfloat16)
    low = (x - high.astype(jnp.float32)).astype(jnp.bfloat16)
    return high, low


def dot3(a_high, a_low, b_high, b_low):
    f32 = jnp.float32
    total = jnp.dot(a_high, b_high, preferred_element_type=f32)
    total = total + jnp.dot(a_high, b_low, preferred_element_type=f32)
    return total + jnp.dot(a_low, b_high, preferred_element_type=f32)


def mix_react_kernel(
    tile_blocks,
    neighbours,
    block_size,
    nb_ref,
    own_ref,
    weight_ref,
    temp_ref,
    order_ref,
    prod_ref,
    loss_ref,
    migrated_hbm,
    lower_hbm,
    upper_hbm,
    out_ref,
    picked,
    sems,
    mixed_ref,
    terms_ref,
    order_split,
    gain_split,
    gain_high,
):
    f32 = jnp.float32
    step = pl.program_id(0)
    steps = pl.num_programs(0)
    own_count = migrated_hbm.shape[1] // block_size
    halo_count = lower_hbm.shape[1] // block_size

    def fetch(at, slot, start):
        for t in range(tile_blocks):
            for k in range(neighbours):
                index = nb_ref[at * tile_blocks + t, k]
                target = picked.at[slot, t * neighbours + k]
                sem = sems.at[slot, t * neighbours + k]
                if not start:
                    pltpu.make_async_copy(
                        migrated_hbm.at[:, pl.ds(0, block_size)], target, sem
                    ).wait()
                    continue
                sources = (
                    (migrated_hbm, index, index < own_count),
                    (lower_hbm, index - own_count,
                     (index >= own_count) & (index < own_count + halo_count)),
                    (upper_hbm, index - own_count - halo_count,
                     index >= own_count + halo_count),
                )
                for source, local, chosen in sources:
                    limit = source.shape[1] // block_size - 1
                    local = jnp.minimum(jnp.maximum(local, 0), limit)

                    @pl.when(chosen)
                    def _():
                        begin = pl.multiple_of(local * block_size, block_size)
                        pltpu.make_async_copy(
                            source.at[:, pl.ds(begin, block_size)], target, sem
                        ).start()

    @pl.when(step == 0)
    def _():
        fetch(0, 0, True)
        order_high, order_low = split3(order_ref[...].T)
        reactions = order_high.shape[0]
        order_split[0:reactions] = order_high
        order_split[reactions:] = order_low
        gain_split[...] = jnp.zeros_like(gain_split)
        rows = prod_ref.shape[0]
        for part, source in enumerate((prod_ref, loss_ref)):
            high, low = split3(source[...])
            gain_split[pl.ds(2 * part * PAD_ROWS, rows)] = high
            gain_split[pl.ds((2 * part + 1) * PAD_ROWS, rows)] = low
            gain_high[pl.ds(part * PAD_ROWS, rows)] = high
        gain_high[...] = jnp.where(
            lax.broadcasted_iota(jnp.int32, gain_high.shape, 0) % PAD_ROWS < rows,
            gain_high[...],
            jnp.zeros_like(gain_high),
        )

    slot = step % 2

    @pl.when(step + 1 < steps)
    def _():
        fetch(step + 1, 1 - slot, True)

    fetch(step, slot, False)

    for t in range(tile_blocks):
        lanes = slice(t * block_size, (t + 1) * block_size)
        stacked = jnp.concatenate(
            [own_ref[:, lanes]] + [picked[slot, t * neighbours + k] for k in range(neighbours)],
            axis=1,
        )
        weight = weight_ref[t].reshape((neighbours + 1) * block_size, block_size)
        mixed_ref[:, lanes] = jnp.dot(stacked, weight, preferred_element_type=f32)
    mixed = mixed_ref[...]
    species = mixed.shape[0]
    terms_ref[0:species] = jnp.log(mixed)
    terms_ref[species:species + 1] = jnp.ones((1, mixed.shape[1]), f32)
    terms_ref[species + 1:species + 2] = temp_ref[...]
    log_high, log_low = split3(terms_ref[...])
    reactions = order_split.shape[0] // 2
    both = jnp.dot(order_split[...], log_high, preferred_element_type=f32)
    exponent = both[:reactions] + both[reactions:]
    exponent = exponent + jnp.dot(order_split[0:reactions], log_low, preferred_element_type=f32)
    rate = jnp.exp(exponent)
    rate_high, rate_low = split3(rate)
    by_high = jnp.dot(gain_split[...], rate_high, preferred_element_type=f32)
    by_low = jnp.dot(gain_high[...], rate_low, preferred_element_type=f32)
    gained = by_high[0:species] + by_high[PAD_ROWS:PAD_ROWS + species] + by_low[0:species]
    lost_mass = (
        by_high[2 * PAD_ROWS:2 * PAD_ROWS + species]
        + by_high[3 * PAD_ROWS:3 * PAD_ROWS + species]
        + by_low[PAD_ROWS:PAD_ROWS + species]
    )
    out_ref[...] = (mixed + gained) / (1.0 + lost_mass / mixed)


def mix_react(
    migrated,
    from_lower,
    from_upper,
    neighbour_block,
    mix_weight,
    inverse_temp,
    reactant_order,
    log_prefactor,
    activation_energy,
    production,
    loss_coefficient,
):
    species = migrated.shape[0]
    count_blocks, _, block_size, _ = mix_weight.shape
    neighbours = neighbour_block.shape[1]
    reactions = reactant_order.shape[0]
    tile_blocks = TILE_BLOCKS
    width = tile_blocks * block_size
    steps = count_blocks // tile_blocks

    def whole(shape):
        return pl.BlockSpec(shape, lambda i, nb: (0,) * len(shape))

    in_specs = [
        pl.BlockSpec((species, width), lambda i, nb: (0, i)),
        pl.BlockSpec((tile_blocks,) + mix_weight.shape[1:], lambda i, nb: (i, 0, 0, 0)),
        pl.BlockSpec((1, width), lambda i, nb: (0, i)),
        whole((species + 2, reactions)),
        whole(production.shape),
        whole(loss_coefficient.shape),
        pl.BlockSpec(memory_space=pl.ANY),
        pl.BlockSpec(memory_space=pl.ANY),
        pl.BlockSpec(memory_space=pl.ANY),
    ]
    bf16 = jnp.bfloat16
    grid_spec = pltpu.PrefetchScalarGridSpec(
        num_scalar_prefetch=1,
        grid=(steps,),
        in_specs=in_specs,
        out_specs=pl.BlockSpec((species, width), lambda i, nb: (0, i)),
        scratch_shapes=[
            pltpu.VMEM((2, tile_blocks * neighbours, species, block_size), bf16),
            pltpu.SemaphoreType.DMA((2, tile_blocks * neighbours)),
            pltpu.VMEM((species, width), jnp.float32),
            pltpu.VMEM((species + 2, width), jnp.float32),
            pltpu.VMEM((2 * reactions, species + 2), bf16),
            pltpu.VMEM((4 * PAD_ROWS, reactions), bf16),
            pltpu.VMEM((2 * PAD_ROWS, reactions), bf16),
        ],
    )
    kernel = functools.partial(mix_react_kernel, tile_blocks, neighbours, block_size)
    return pl.pallas_call(
        kernel,
        grid_spec=grid_spec,
        out_shape=jax.ShapeDtypeStruct((species, count_blocks * block_size), jnp.float32),
        compiler_params=pltpu.CompilerParams(dimension_semantics=("arbitrary",)),
    )(
        neighbour_block,
        migrated,
        mix_weight,
        inverse_temp.reshape(1, -1),
        jnp.concatenate(
            [reactant_order.T, log_prefactor[None, :], -activation_energy[None, :]], axis=0
        ),
        production,
        loss_coefficient,
        migrated,
        from_lower,
        from_upper,
    )


def shards(
    mixing_ratio,
    send_rows,
    migrant_count,
    arrival_slot,
    halo_blocks,
    neighbour_block,
    mix_weight,
    inverse_temp,
    reactant_order,
    log_prefactor,
    activation_energy,
    production,
    loss_coefficient,
):
    migrated, from_lower, from_upper = migrate(
        mixing_ratio, send_rows, migrant_count, arrival_slot, halo_blocks, mix_weight.shape[-1]
    )
    return mix_react(
        migrated,
        from_lower,
        from_upper,
        neighbour_block,
        mix_weight,
        inverse_temp,
        reactant_order,
        log_prefactor,
        activation_energy,
        production,
        loss_coefficient,
    )


def solution(mesh):
    placed = (
        P(None, "region"),
        P("region", None, None),
        P("region", None),
        P("region", None, None),
        P("region", None, None),
        P("region", None),
        P("region", None, None, None),
        P("region"),
        P(),
        P(),
        P(),
        P(),
        P(),
    )
    return jax.shard_map(
        shards, mesh=mesh, in_specs=placed, out_specs=P(None, "region"), check_vma=False
    )
```

```python
import functools

import jax
import jax.numpy as jnp
from jax import lax
from jax.experimental import pallas as pl
from jax.experimental.pallas import tpu as pltpu
from jax.sharding import PartitionSpec as P

HOP = 4
TILE_BLOCKS = 8
PAD_ROWS = 160


def from_behind(block, axis, distance):
    devices = range(lax.axis_size(axis))
    route = [((i - distance) % len(devices), i) for i in devices]
    return lax.ppermute(block, axis, route)


def peer_offsets():
    return [column - HOP if column < HOP else column - HOP + 1 for column in range(2 * HOP)]


def pick_kernel(chunk, mixing_ref, rows_ref, *out_refs):
    species, parcels = mixing_ref.shape
    wanted = rows_ref[...]
    total = jnp.zeros((species, wanted.shape[1]), jnp.float32)
    for part in range(parcels // chunk):
        position = lax.broadcasted_iota(jnp.int32, (chunk, wanted.shape[1]), 0) + part * chunk
        pick = (position == wanted).astype(jnp.bfloat16)
        total = total + jnp.dot(
            mixing_ref[:, part * chunk:(part + 1) * chunk], pick, preferred_element_type=jnp.float32
        )
    width = out_refs[0].shape[1]
    for column, out_ref in enumerate(out_refs):
        out_ref[...] = total[:, column * width:(column + 1) * width].astype(out_ref.dtype)


def marked_arrivals(received_refs, rows):
    received = jnp.concatenate([ref[...] for ref in received_refs], axis=1)
    species = received.shape[0]
    pad = (-species) % 16 or 16
    return jnp.concatenate([received, jnp.ones((pad, rows), received.dtype)], axis=0)


def place_kernel(chunk, peer_count, mixing_ref, *refs):
    received_refs = refs[:peer_count]
    slots_ref, migrated_ref = refs[peer_count:]
    species, parcels = mixing_ref.shape
    slots = slots_ref[...]
    marked = marked_arrivals(received_refs, slots.shape[0])
    for part in range(parcels // chunk):
        lanes = slice(part * chunk, (part + 1) * chunk)
        position = lax.broadcasted_iota(jnp.int32, (slots.shape[0], chunk), 1) + part * chunk
        place = (position == slots).astype(jnp.bfloat16)
        placed = jnp.dot(marked, place, preferred_element_type=jnp.float32)
        hit = placed[species:species + 1]
        migrated_ref[:, lanes] = jnp.where(
            hit > 0.5, placed[:species].astype(migrated_ref.dtype), mixing_ref[:, lanes]
        )


def halo_kernel(chunk, block_size, peer_count, halo_ref, mixing_ref, *refs):
    received_refs = refs[:peer_count]
    slots_ref, lower_ref, upper_ref, sems = refs[peer_count:]
    species = mixing_ref.shape[0]
    sides, listed = halo_ref.shape
    outs = (lower_ref, upper_ref)
    copies = []
    for side in range(sides):
        for j in range(listed):
            start = pl.multiple_of(halo_ref[side, j] * block_size, block_size)
            copy = pltpu.make_async_copy(
                mixing_ref.at[:, pl.ds(start, block_size)],
                outs[side].at[:, pl.ds(j * block_size, block_size)],
                sems.at[side, j],
            )
            copy.start()
            copies.append(copy)
    slots = slots_ref[...]
    marked = marked_arrivals(received_refs, slots.shape[0])
    lane = lax.broadcasted_iota(jnp.int32, (1, block_size), 1)
    per_chunk = chunk // block_size
    for copy in copies:
        copy.wait()
    for side in range(sides):
        for part in range(listed // per_chunk):
            first = part * per_chunk
            where_to = jnp.concatenate(
                [lane + halo_ref[side, j] * block_size for j in range(first, first + per_chunk)],
                axis=1,
            )
            place = (where_to == slots).astype(jnp.bfloat16)
            placed = jnp.dot(marked, place, preferred_element_type=jnp.float32)
            hit = placed[species:species + 1]
            lanes = slice(first * block_size, (first + per_chunk) * block_size)
            outs[side][:, lanes] = jnp.where(
                hit > 0.5, placed[:species].astype(outs[side].dtype), outs[side][:, lanes]
            )


def vmem_whole(shape):
    return pl.BlockSpec(shape, lambda *_: (0,) * len(shape))


def migrate(mixing_ratio, send_rows, migrant_count, arrival_slot, halo_blocks, block_size):
    species, parcels = mixing_ratio.shape
    capacity = send_rows.shape[-1]
    offsets = peer_offsets()
    peer_count = len(offsets)
    chunk = 1024
    wanted = send_rows[0].reshape(1, -1)
    outgoing = pl.pallas_call(
        functools.partial(pick_kernel, chunk),
        grid=(1,),
        in_specs=[vmem_whole(mixing_ratio.shape), vmem_whole(wanted.shape)],
        out_specs=[vmem_whole((species, capacity))] * peer_count,
        out_shape=[jax.ShapeDtypeStruct((species, capacity), mixing_ratio.dtype)] * peer_count,
    )(mixing_ratio, wanted)
    arrived = []
    for column in range(peer_count):
        opposite = peer_count - 1 - column
        arrived.append(from_behind(outgoing[opposite], "region", -offsets[column]))
    lane_index = jnp.arange(capacity, dtype=jnp.int32)
    live_lane = lane_index[None, :] < migrant_count[0][:, None]
    slots = jnp.where(live_lane, arrival_slot[0], parcels).reshape(-1, 1)
    sides, listed = halo_blocks.shape[1:]
    halo_shape = (species, listed * block_size)
    grid_spec = pltpu.PrefetchScalarGridSpec(
        num_scalar_prefetch=1,
        grid=(1,),
        in_specs=[pl.BlockSpec(memory_space=pl.ANY)]
        + [vmem_whole((species, capacity))] * peer_count
        + [vmem_whole(slots.shape)],
        out_specs=[vmem_whole(halo_shape), vmem_whole(halo_shape)],
        scratch_shapes=[pltpu.SemaphoreType.DMA((sides, listed))],
    )
    to_lower, to_upper = pl.pallas_call(
        functools.partial(halo_kernel, chunk, block_size, peer_count),
        grid_spec=grid_spec,
        out_shape=[jax.ShapeDtypeStruct(halo_shape, mixing_ratio.dtype)] * sides,
    )(halo_blocks[0], mixing_ratio, *arrived, slots)
    migrated = pl.pallas_call(
        functools.partial(place_kernel, chunk, peer_count),
        grid=(1,),
        in_specs=[vmem_whole(mixing_ratio.shape)]
        + [vmem_whole((species, capacity))] * peer_count
        + [vmem_whole(slots.shape)],
        out_specs=vmem_whole(mixing_ratio.shape),
        out_shape=jax.ShapeDtypeStruct(mixing_ratio.shape, mixing_ratio.dtype),
    )(mixing_ratio, *arrived, slots)
    from_lower = from_behind(to_upper, "region", 1)
    from_upper = from_behind(to_lower, "region", -1)
    return migrated, from_lower, from_upper


def split3(x):
    high = x.astype(jnp.bfloat16)
    low = (x - high.astype(jnp.float32)).astype(jnp.bfloat16)
    return high, low


def dot3(a_high, a_low, b_high, b_low):
    f32 = jnp.float32
    total = jnp.dot(a_high, b_high, preferred_element_type=f32)
    total = total + jnp.dot(a_high, b_low, preferred_element_type=f32)
    return total + jnp.dot(a_low, b_high, preferred_element_type=f32)


def mix_react_kernel(
    tile_blocks,
    neighbours,
    block_size,
    nb_ref,
    own_ref,
    weight_ref,
    temp_ref,
    order_ref,
    prod_ref,
    loss_ref,
    migrated_hbm,
    lower_hbm,
    upper_hbm,
    out_ref,
    picked,
    sems,
    mixed_ref,
    terms_ref,
    order_split,
    gain_split,
    gain_high,
):
    f32 = jnp.float32
    step = pl.program_id(0)
    steps = pl.num_programs(0)
    own_count = migrated_hbm.shape[1] // block_size
    halo_count = lower_hbm.shape[1] // block_size

    def fetch(at, slot, start):
        for t in range(tile_blocks):
            for k in range(neighbours):
                index = nb_ref[k, at * tile_blocks + t]
                target = picked.at[slot, t * neighbours + k]
                sem = sems.at[slot, t * neighbours + k]
                if not start:
                    pltpu.make_async_copy(
                        migrated_hbm.at[:, pl.ds(0, block_size)], target, sem
                    ).wait()
                    continue
                sources = (
                    (migrated_hbm, index, index < own_count),
                    (lower_hbm, index - own_count,
                     (index >= own_count) & (index < own_count + halo_count)),
                    (upper_hbm, index - own_count - halo_count,
                     index >= own_count + halo_count),
                )
                for source, local, chosen in sources:
                    limit = source.shape[1] // block_size - 1
                    local = jnp.minimum(jnp.maximum(local, 0), limit)

                    @pl.when(chosen)
                    def _():
                        begin = pl.multiple_of(local * block_size, block_size)
                        pltpu.make_async_copy(
                            source.at[:, pl.ds(begin, block_size)], target, sem
                        ).start()

    @pl.when(step == 0)
    def _():
        fetch(0, 0, True)
        order_high, order_low = split3(order_ref[...].T)
        reactions = order_high.shape[0]
        order_split[0:reactions] = order_high
        order_split[reactions:] = order_low
        gain_split[...] = jnp.zeros_like(gain_split)
        rows = prod_ref.shape[0]
        for part, source in enumerate((prod_ref, loss_ref)):
            high, low = split3(source[...])
            gain_split[pl.ds(2 * part * PAD_ROWS, rows)] = high
            gain_split[pl.ds((2 * part + 1) * PAD_ROWS, rows)] = low
            gain_high[pl.ds(part * PAD_ROWS, rows)] = high
        gain_high[...] = jnp.where(
            lax.broadcasted_iota(jnp.int32, gain_high.shape, 0) % PAD_ROWS < rows,
            gain_high[...],
            jnp.zeros_like(gain_high),
        )

    slot = step % 2

    @pl.when(step + 1 < steps)
    def _():
        fetch(step + 1, 1 - slot, True)

    fetch(step, slot, False)

    for t in range(tile_blocks):
        lanes = slice(t * block_size, (t + 1) * block_size)
        stacked = jnp.concatenate(
            [own_ref[:, lanes]] + [picked[slot, t * neighbours + k] for k in range(neighbours)],
            axis=1,
        )
        weight = weight_ref[t].reshape((neighbours + 1) * block_size, block_size)
        mixed_ref[:, lanes] = jnp.dot(stacked, weight, preferred_element_type=f32)
    mixed = mixed_ref[...]
    species = mixed.shape[0]
    terms_ref[0:species] = jnp.log(mixed)
    terms_ref[species:species + 1] = jnp.ones((1, mixed.shape[1]), f32)
    terms_ref[species + 1:species + 2] = temp_ref[...]
    log_high, log_low = split3(terms_ref[...])
    reactions = order_split.shape[0] // 2
    both = jnp.dot(order_split[...], log_high, preferred_element_type=f32)
    exponent = both[:reactions] + both[reactions:]
    exponent = exponent + jnp.dot(order_split[0:reactions], log_low, preferred_element_type=f32)
    rate = jnp.exp(exponent)
    rate_high, rate_low = split3(rate)
    by_high = jnp.dot(gain_split[...], rate_high, preferred_element_type=f32)
    by_low = jnp.dot(gain_high[...], rate_low, preferred_element_type=f32)
    gained = by_high[0:species] + by_high[PAD_ROWS:PAD_ROWS + species] + by_low[0:species]
    lost_mass = (
        by_high[2 * PAD_ROWS:2 * PAD_ROWS + species]
        + by_high[3 * PAD_ROWS:3 * PAD_ROWS + species]
        + by_low[PAD_ROWS:PAD_ROWS + species]
    )
    out_ref[...] = (mixed + gained) / (1.0 + lost_mass / mixed)


def mix_react(
    migrated,
    from_lower,
    from_upper,
    neighbour_block,
    mix_weight,
    inverse_temp,
    reactant_order,
    log_prefactor,
    activation_energy,
    production,
    loss_coefficient,
):
    species = migrated.shape[0]
    count_blocks, _, block_size, _ = mix_weight.shape
    neighbours = neighbour_block.shape[1]
    reactions = reactant_order.shape[0]
    tile_blocks = TILE_BLOCKS
    width = tile_blocks * block_size
    steps = count_blocks // tile_blocks

    def whole(shape):
        return pl.BlockSpec(shape, lambda i, nb: (0,) * len(shape))

    in_specs = [
        pl.BlockSpec((species, width), lambda i, nb: (0, i)),
        pl.BlockSpec((tile_blocks,) + mix_weight.shape[1:], lambda i, nb: (i, 0, 0, 0)),
        pl.BlockSpec((1, width), lambda i, nb: (0, i)),
        whole((species + 2, reactions)),
        whole(production.shape),
        whole(loss_coefficient.shape),
        pl.BlockSpec(memory_space=pl.ANY),
        pl.BlockSpec(memory_space=pl.ANY),
        pl.BlockSpec(memory_space=pl.ANY),
    ]
    bf16 = jnp.bfloat16
    grid_spec = pltpu.PrefetchScalarGridSpec(
        num_scalar_prefetch=1,
        grid=(steps,),
        in_specs=in_specs,
        out_specs=pl.BlockSpec((species, width), lambda i, nb: (0, i)),
        scratch_shapes=[
            pltpu.VMEM((2, tile_blocks * neighbours, species, block_size), bf16),
            pltpu.SemaphoreType.DMA((2, tile_blocks * neighbours)),
            pltpu.VMEM((species, width), jnp.float32),
            pltpu.VMEM((species + 2, width), jnp.float32),
            pltpu.VMEM((2 * reactions, species + 2), bf16),
            pltpu.VMEM((4 * PAD_ROWS, reactions), bf16),
            pltpu.VMEM((2 * PAD_ROWS, reactions), bf16),
        ],
    )
    kernel = functools.partial(mix_react_kernel, tile_blocks, neighbours, block_size)
    return pl.pallas_call(
        kernel,
        grid_spec=grid_spec,
        out_shape=jax.ShapeDtypeStruct((species, count_blocks * block_size), jnp.float32),
        compiler_params=pltpu.CompilerParams(dimension_semantics=("arbitrary",)),
    )(
        neighbour_block.T,
        migrated,
        mix_weight,
        inverse_temp.reshape(1, -1),
        jnp.concatenate(
            [reactant_order.T, log_prefactor[None, :], -activation_energy[None, :]], axis=0
        ),
        production,
        loss_coefficient,
        migrated,
        from_lower,
        from_upper,
    )


def shards(
    mixing_ratio,
    send_rows,
    migrant_count,
    arrival_slot,
    halo_blocks,
    neighbour_block,
    mix_weight,
    inverse_temp,
    reactant_order,
    log_prefactor,
    activation_energy,
    production,
    loss_coefficient,
):
    migrated, from_lower, from_upper = migrate(
        mixing_ratio, send_rows, migrant_count, arrival_slot, halo_blocks, mix_weight.shape[-1]
    )
    return mix_react(
        migrated,
        from_lower,
        from_upper,
        neighbour_block,
        mix_weight,
        inverse_temp,
        reactant_order,
        log_prefactor,
        activation_energy,
        production,
        loss_coefficient,
    )


def solution(mesh):
    placed = (
        P(None, "region"),
        P("region", None, None),
        P("region", None),
        P("region", None, None),
        P("region", None, None),
        P("region", None),
        P("region", None, None, None),
        P("region"),
        P(),
        P(),
        P(),
        P(),
        P(),
    )
    return jax.shard_map(
        shards, mesh=mesh, in_specs=placed, out_specs=P(None, "region"), check_vma=False
    )
```

```python
import functools

import jax
import jax.numpy as jnp
from jax import lax
from jax.experimental import pallas as pl
from jax.experimental.pallas import tpu as pltpu
from jax.sharding import PartitionSpec as P

HOP = 4
TILE_BLOCKS = 8
PAD_ROWS = 160


def from_behind(block, axis, distance):
    devices = range(lax.axis_size(axis))
    route = [((i - distance) % len(devices), i) for i in devices]
    return lax.ppermute(block, axis, route)


def peer_offsets():
    return [column - HOP if column < HOP else column - HOP + 1 for column in range(2 * HOP)]


def pick_kernel(chunk, mixing_ref, rows_ref, *out_refs):
    species, parcels = mixing_ref.shape
    wanted = rows_ref[...]
    total = jnp.zeros((species, wanted.shape[1]), jnp.float32)
    for part in range(parcels // chunk):
        position = lax.broadcasted_iota(jnp.int32, (chunk, wanted.shape[1]), 0) + part * chunk
        pick = (position == wanted).astype(jnp.bfloat16)
        total = total + jnp.dot(
            mixing_ref[:, part * chunk:(part + 1) * chunk], pick, preferred_element_type=jnp.float32
        )
    width = out_refs[0].shape[1]
    for column, out_ref in enumerate(out_refs):
        out_ref[...] = total[:, column * width:(column + 1) * width].astype(out_ref.dtype)


def marked_arrivals(received_refs, rows):
    received = jnp.concatenate([ref[...] for ref in received_refs], axis=1)
    species = received.shape[0]
    pad = (-species) % 16 or 16
    return jnp.concatenate([received, jnp.ones((pad, rows), received.dtype)], axis=0)


def place_kernel(chunk, peer_count, mixing_ref, *refs):
    received_refs = refs[:peer_count]
    slots_ref, migrated_ref = refs[peer_count:]
    species, parcels = mixing_ref.shape
    slots = slots_ref[...]
    marked = marked_arrivals(received_refs, slots.shape[0])
    for part in range(parcels // chunk):
        lanes = slice(part * chunk, (part + 1) * chunk)
        position = lax.broadcasted_iota(jnp.int32, (slots.shape[0], chunk), 1) + part * chunk
        place = (position == slots).astype(jnp.bfloat16)
        placed = jnp.dot(marked, place, preferred_element_type=jnp.float32)
        hit = placed[species:species + 1]
        migrated_ref[:, lanes] = jnp.where(
            hit > 0.5, placed[:species].astype(migrated_ref.dtype), mixing_ref[:, lanes]
        )


def halo_kernel(chunk, block_size, peer_count, halo_ref, mixing_ref, *refs):
    received_refs = refs[:peer_count]
    slots_ref, lower_ref, upper_ref, sems = refs[peer_count:]
    species = mixing_ref.shape[0]
    sides, listed = halo_ref.shape
    outs = (lower_ref, upper_ref)
    copies = []
    for side in range(sides):
        for j in range(listed):
            start = pl.multiple_of(halo_ref[side, j] * block_size, block_size)
            copy = pltpu.make_async_copy(
                mixing_ref.at[:, pl.ds(start, block_size)],
                outs[side].at[:, pl.ds(j * block_size, block_size)],
                sems.at[side, j],
            )
            copy.start()
            copies.append(copy)
    slots = slots_ref[...]
    marked = marked_arrivals(received_refs, slots.shape[0])
    lane = lax.broadcasted_iota(jnp.int32, (1, block_size), 1)
    per_chunk = chunk // block_size
    for copy in copies:
        copy.wait()
    for side in range(sides):
        for part in range(listed // per_chunk):
            first = part * per_chunk
            where_to = jnp.concatenate(
                [lane + halo_ref[side, j] * block_size for j in range(first, first + per_chunk)],
                axis=1,
            )
            place = (where_to == slots).astype(jnp.bfloat16)
            placed = jnp.dot(marked, place, preferred_element_type=jnp.float32)
            hit = placed[species:species + 1]
            lanes = slice(first * block_size, (first + per_chunk) * block_size)
            outs[side][:, lanes] = jnp.where(
                hit > 0.5, placed[:species].astype(outs[side].dtype), outs[side][:, lanes]
            )


def vmem_whole(shape):
    return pl.BlockSpec(shape, lambda *_: (0,) * len(shape))


def migrate(mixing_ratio, send_rows, migrant_count, arrival_slot, halo_blocks, block_size):
    species, parcels = mixing_ratio.shape
    capacity = send_rows.shape[-1]
    offsets = peer_offsets()
    peer_count = len(offsets)
    chunk = 1024
    wanted = send_rows[0].reshape(1, -1)
    outgoing = pl.pallas_call(
        functools.partial(pick_kernel, chunk),
        grid=(1,),
        in_specs=[vmem_whole(mixing_ratio.shape), vmem_whole(wanted.shape)],
        out_specs=[vmem_whole((species, capacity))] * peer_count,
        out_shape=[jax.ShapeDtypeStruct((species, capacity), mixing_ratio.dtype)] * peer_count,
    )(mixing_ratio, wanted)
    arrived = []
    for column in range(peer_count):
        opposite = peer_count - 1 - column
        arrived.append(from_behind(outgoing[opposite], "region", -offsets[column]))
    lane_index = jnp.arange(capacity, dtype=jnp.int32)
    live_lane = lane_index[None, :] < migrant_count[0][:, None]
    slots = jnp.where(live_lane, arrival_slot[0], parcels).reshape(-1, 1)
    sides, listed = halo_blocks.shape[1:]
    halo_shape = (species, listed * block_size)
    grid_spec = pltpu.PrefetchScalarGridSpec(
        num_scalar_prefetch=1,
        grid=(1,),
        in_specs=[pl.BlockSpec(memory_space=pl.ANY)]
        + [vmem_whole((species, capacity))] * peer_count
        + [vmem_whole(slots.shape)],
        out_specs=[vmem_whole(halo_shape), vmem_whole(halo_shape)],
        scratch_shapes=[pltpu.SemaphoreType.DMA((sides, listed))],
    )
    to_lower, to_upper = pl.pallas_call(
        functools.partial(halo_kernel, chunk, block_size, peer_count),
        grid_spec=grid_spec,
        out_shape=[jax.ShapeDtypeStruct(halo_shape, mixing_ratio.dtype)] * sides,
    )(halo_blocks[0], mixing_ratio, *arrived, slots)
    migrated = pl.pallas_call(
        functools.partial(place_kernel, chunk, peer_count),
        grid=(1,),
        in_specs=[vmem_whole(mixing_ratio.shape)]
        + [vmem_whole((species, capacity))] * peer_count
        + [vmem_whole(slots.shape)],
        out_specs=vmem_whole(mixing_ratio.shape),
        out_shape=jax.ShapeDtypeStruct(mixing_ratio.shape, mixing_ratio.dtype),
    )(mixing_ratio, *arrived, slots)
    to_lower, to_upper, migrated = lax.optimization_barrier((to_lower, to_upper, migrated))
    from_lower = from_behind(to_upper, "region", 1)
    from_upper = from_behind(to_lower, "region", -1)
    return migrated, from_lower, from_upper


def split3(x):
    high = x.astype(jnp.bfloat16)
    low = (x - high.astype(jnp.float32)).astype(jnp.bfloat16)
    return high, low


def dot3(a_high, a_low, b_high, b_low):
    f32 = jnp.float32
    total = jnp.dot(a_high, b_high, preferred_element_type=f32)
    total = total + jnp.dot(a_high, b_low, preferred_element_type=f32)
    return total + jnp.dot(a_low, b_high, preferred_element_type=f32)


def mix_react_kernel(
    tile_blocks,
    neighbours,
    block_size,
    nb_ref,
    own_ref,
    weight_ref,
    temp_ref,
    order_ref,
    prod_ref,
    loss_ref,
    migrated_hbm,
    lower_hbm,
    upper_hbm,
    out_ref,
    picked,
    sems,
    mixed_ref,
    terms_ref,
    order_split,
    gain_split,
    gain_high,
):
    f32 = jnp.float32
    step = pl.program_id(0)
    steps = pl.num_programs(0)
    own_count = migrated_hbm.shape[1] // block_size
    halo_count = lower_hbm.shape[1] // block_size

    def fetch(at, slot, start):
        for t in range(tile_blocks):
            for k in range(neighbours):
                index = nb_ref[k, at * tile_blocks + t]
                target = picked.at[slot, t * neighbours + k]
                sem = sems.at[slot, t * neighbours + k]
                if not start:
                    pltpu.make_async_copy(
                        migrated_hbm.at[:, pl.ds(0, block_size)], target, sem
                    ).wait()
                    continue
                sources = (
                    (migrated_hbm, index, index < own_count),
                    (lower_hbm, index - own_count,
                     (index >= own_count) & (index < own_count + halo_count)),
                    (upper_hbm, index - own_count - halo_count,
                     index >= own_count + halo_count),
                )
                for source, local, chosen in sources:
                    limit = source.shape[1] // block_size - 1
                    local = jnp.minimum(jnp.maximum(local, 0), limit)

                    @pl.when(chosen)
                    def _():
                        begin = pl.multiple_of(local * block_size, block_size)
                        pltpu.make_async_copy(
                            source.at[:, pl.ds(begin, block_size)], target, sem
                        ).start()

    @pl.when(step == 0)
    def _():
        fetch(0, 0, True)
        order_high, order_low = split3(order_ref[...].T)
        reactions = order_high.shape[0]
        order_split[0:reactions] = order_high
        order_split[reactions:] = order_low
        gain_split[...] = jnp.zeros_like(gain_split)
        rows = prod_ref.shape[0]
        for part, source in enumerate((prod_ref, loss_ref)):
            high, low = split3(source[...])
            gain_split[pl.ds(2 * part * PAD_ROWS, rows)] = high
            gain_split[pl.ds((2 * part + 1) * PAD_ROWS, rows)] = low
            gain_high[pl.ds(part * PAD_ROWS, rows)] = high
        gain_high[...] = jnp.where(
            lax.broadcasted_iota(jnp.int32, gain_high.shape, 0) % PAD_ROWS < rows,
            gain_high[...],
            jnp.zeros_like(gain_high),
        )

    slot = step % 2

    @pl.when(step + 1 < steps)
    def _():
        fetch(step + 1, 1 - slot, True)

    fetch(step, slot, False)

    for t in range(tile_blocks):
        lanes = slice(t * block_size, (t + 1) * block_size)
        stacked = jnp.concatenate(
            [own_ref[:, lanes]] + [picked[slot, t * neighbours + k] for k in range(neighbours)],
            axis=1,
        )
        weight = weight_ref[t].reshape((neighbours + 1) * block_size, block_size)
        mixed_ref[:, lanes] = jnp.dot(stacked, weight, preferred_element_type=f32)
    mixed = mixed_ref[...]
    species = mixed.shape[0]
    terms_ref[0:species] = jnp.log(mixed)
    terms_ref[species:species + 1] = jnp.ones((1, mixed.shape[1]), f32)
    terms_ref[species + 1:species + 2] = temp_ref[...]
    log_high, log_low = split3(terms_ref[...])
    reactions = order_split.shape[0] // 2
    both = jnp.dot(order_split[...], log_high, preferred_element_type=f32)
    exponent = both[:reactions] + both[reactions:]
    exponent = exponent + jnp.dot(order_split[0:reactions], log_low, preferred_element_type=f32)
    rate = jnp.exp(exponent)
    rate_high, rate_low = split3(rate)
    by_high = jnp.dot(gain_split[...], rate_high, preferred_element_type=f32)
    by_low = jnp.dot(gain_high[...], rate_low, preferred_element_type=f32)
    gained = by_high[0:species] + by_high[PAD_ROWS:PAD_ROWS + species] + by_low[0:species]
    lost_mass = (
        by_high[2 * PAD_ROWS:2 * PAD_ROWS + species]
        + by_high[3 * PAD_ROWS:3 * PAD_ROWS + species]
        + by_low[PAD_ROWS:PAD_ROWS + species]
    )
    out_ref[...] = (mixed + gained) / (1.0 + lost_mass / mixed)


def mix_react(
    migrated,
    from_lower,
    from_upper,
    neighbour_block,
    mix_weight,
    inverse_temp,
    reactant_order,
    log_prefactor,
    activation_energy,
    production,
    loss_coefficient,
):
    species = migrated.shape[0]
    count_blocks, _, block_size, _ = mix_weight.shape
    neighbours = neighbour_block.shape[1]
    reactions = reactant_order.shape[0]
    tile_blocks = TILE_BLOCKS
    width = tile_blocks * block_size
    steps = count_blocks // tile_blocks

    def whole(shape):
        return pl.BlockSpec(shape, lambda i, nb: (0,) * len(shape))

    in_specs = [
        pl.BlockSpec((species, width), lambda i, nb: (0, i)),
        pl.BlockSpec((tile_blocks,) + mix_weight.shape[1:], lambda i, nb: (i, 0, 0, 0)),
        pl.BlockSpec((1, width), lambda i, nb: (0, i)),
        whole((species + 2, reactions)),
        whole(production.shape),
        whole(loss_coefficient.shape),
        pl.BlockSpec(memory_space=pl.ANY),
        pl.BlockSpec(memory_space=pl.ANY),
        pl.BlockSpec(memory_space=pl.ANY),
    ]
    bf16 = jnp.bfloat16
    grid_spec = pltpu.PrefetchScalarGridSpec(
        num_scalar_prefetch=1,
        grid=(steps,),
        in_specs=in_specs,
        out_specs=pl.BlockSpec((species, width), lambda i, nb: (0, i)),
        scratch_shapes=[
            pltpu.VMEM((2, tile_blocks * neighbours, species, block_size), bf16),
            pltpu.SemaphoreType.DMA((2, tile_blocks * neighbours)),
            pltpu.VMEM((species, width), jnp.float32),
            pltpu.VMEM((species + 2, width), jnp.float32),
            pltpu.VMEM((2 * reactions, species + 2), bf16),
            pltpu.VMEM((4 * PAD_ROWS, reactions), bf16),
            pltpu.VMEM((2 * PAD_ROWS, reactions), bf16),
        ],
    )
    kernel = functools.partial(mix_react_kernel, tile_blocks, neighbours, block_size)
    return pl.pallas_call(
        kernel,
        grid_spec=grid_spec,
        out_shape=jax.ShapeDtypeStruct((species, count_blocks * block_size), jnp.float32),
        compiler_params=pltpu.CompilerParams(dimension_semantics=("arbitrary",)),
    )(
        neighbour_block.T,
        migrated,
        mix_weight,
        inverse_temp.reshape(1, -1),
        jnp.concatenate(
            [reactant_order.T, log_prefactor[None, :], -activation_energy[None, :]], axis=0
        ),
        production,
        loss_coefficient,
        migrated,
        from_lower,
        from_upper,
    )


def shards(
    mixing_ratio,
    send_rows,
    migrant_count,
    arrival_slot,
    halo_blocks,
    neighbour_block,
    mix_weight,
    inverse_temp,
    reactant_order,
    log_prefactor,
    activation_energy,
    production,
    loss_coefficient,
):
    migrated, from_lower, from_upper = migrate(
        mixing_ratio, send_rows, migrant_count, arrival_slot, halo_blocks, mix_weight.shape[-1]
    )
    return mix_react(
        migrated,
        from_lower,
        from_upper,
        neighbour_block,
        mix_weight,
        inverse_temp,
        reactant_order,
        log_prefactor,
        activation_energy,
        production,
        loss_coefficient,
    )


def solution(mesh):
    placed = (
        P(None, "region"),
        P("region", None, None),
        P("region", None),
        P("region", None, None),
        P("region", None, None),
        P("region", None),
        P("region", None, None, None),
        P("region"),
        P(),
        P(),
        P(),
        P(),
        P(),
    )
    return jax.shard_map(
        shards, mesh=mesh, in_specs=placed, out_specs=P(None, "region"), check_vma=False
    )
```

```python
import functools

import jax
import jax.numpy as jnp
from jax import lax
from jax.experimental import pallas as pl
from jax.experimental.pallas import tpu as pltpu
from jax.sharding import PartitionSpec as P

HOP = 4
TILE_BLOCKS = 16
PAD_ROWS = 160


def from_behind(block, axis, distance):
    devices = range(lax.axis_size(axis))
    route = [((i - distance) % len(devices), i) for i in devices]
    return lax.ppermute(block, axis, route)


def peer_offsets():
    return [column - HOP if column < HOP else column - HOP + 1 for column in range(2 * HOP)]


def pick_kernel(chunk, mixing_ref, rows_ref, *out_refs):
    species, parcels = mixing_ref.shape
    wanted = rows_ref[...]
    total = jnp.zeros((species, wanted.shape[1]), jnp.float32)
    for part in range(parcels // chunk):
        position = lax.broadcasted_iota(jnp.int32, (chunk, wanted.shape[1]), 0) + part * chunk
        pick = (position == wanted).astype(jnp.bfloat16)
        total = total + jnp.dot(
            mixing_ref[:, part * chunk:(part + 1) * chunk], pick, preferred_element_type=jnp.float32
        )
    width = out_refs[0].shape[1]
    for column, out_ref in enumerate(out_refs):
        out_ref[...] = total[:, column * width:(column + 1) * width].astype(out_ref.dtype)


def marked_arrivals(received_refs, rows):
    received = jnp.concatenate([ref[...] for ref in received_refs], axis=1)
    species = received.shape[0]
    pad = (-species) % 16 or 16
    return jnp.concatenate([received, jnp.ones((pad, rows), received.dtype)], axis=0)


def place_kernel(chunk, peer_count, mixing_ref, *refs):
    received_refs = refs[:peer_count]
    slots_ref, migrated_ref = refs[peer_count:]
    species, parcels = mixing_ref.shape
    slots = slots_ref[...]
    marked = marked_arrivals(received_refs, slots.shape[0])
    for part in range(parcels // chunk):
        lanes = slice(part * chunk, (part + 1) * chunk)
        position = lax.broadcasted_iota(jnp.int32, (slots.shape[0], chunk), 1) + part * chunk
        place = (position == slots).astype(jnp.bfloat16)
        placed = jnp.dot(marked, place, preferred_element_type=jnp.float32)
        hit = placed[species:species + 1]
        migrated_ref[:, lanes] = jnp.where(
            hit > 0.5, placed[:species].astype(migrated_ref.dtype), mixing_ref[:, lanes]
        )


def halo_kernel(chunk, block_size, peer_count, halo_ref, mixing_ref, *refs):
    received_refs = refs[:peer_count]
    slots_ref, lower_ref, upper_ref, sems = refs[peer_count:]
    species = mixing_ref.shape[0]
    sides, listed = halo_ref.shape
    outs = (lower_ref, upper_ref)
    copies = []
    for side in range(sides):
        for j in range(listed):
            start = pl.multiple_of(halo_ref[side, j] * block_size, block_size)
            copy = pltpu.make_async_copy(
                mixing_ref.at[:, pl.ds(start, block_size)],
                outs[side].at[:, pl.ds(j * block_size, block_size)],
                sems.at[side, j],
            )
            copy.start()
            copies.append(copy)
    slots = slots_ref[...]
    marked = marked_arrivals(received_refs, slots.shape[0])
    lane = lax.broadcasted_iota(jnp.int32, (1, block_size), 1)
    per_chunk = chunk // block_size
    for copy in copies:
        copy.wait()
    for side in range(sides):
        for part in range(listed // per_chunk):
            first = part * per_chunk
            where_to = jnp.concatenate(
                [lane + halo_ref[side, j] * block_size for j in range(first, first + per_chunk)],
                axis=1,
            )
            place = (where_to == slots).astype(jnp.bfloat16)
            placed = jnp.dot(marked, place, preferred_element_type=jnp.float32)
            hit = placed[species:species + 1]
            lanes = slice(first * block_size, (first + per_chunk) * block_size)
            outs[side][:, lanes] = jnp.where(
                hit > 0.5, placed[:species].astype(outs[side].dtype), outs[side][:, lanes]
            )


def vmem_whole(shape):
    return pl.BlockSpec(shape, lambda *_: (0,) * len(shape))


def migrate(mixing_ratio, send_rows, migrant_count, arrival_slot, halo_blocks, block_size):
    species, parcels = mixing_ratio.shape
    capacity = send_rows.shape[-1]
    offsets = peer_offsets()
    peer_count = len(offsets)
    chunk = 1024
    wanted = send_rows[0].reshape(1, -1)
    outgoing = pl.pallas_call(
        functools.partial(pick_kernel, chunk),
        grid=(1,),
        in_specs=[vmem_whole(mixing_ratio.shape), vmem_whole(wanted.shape)],
        out_specs=[vmem_whole((species, capacity))] * peer_count,
        out_shape=[jax.ShapeDtypeStruct((species, capacity), mixing_ratio.dtype)] * peer_count,
    )(mixing_ratio, wanted)
    arrived = []
    for column in range(peer_count):
        opposite = peer_count - 1 - column
        arrived.append(from_behind(outgoing[opposite], "region", -offsets[column]))
    lane_index = jnp.arange(capacity, dtype=jnp.int32)
    live_lane = lane_index[None, :] < migrant_count[0][:, None]
    slots = jnp.where(live_lane, arrival_slot[0], parcels).reshape(-1, 1)
    sides, listed = halo_blocks.shape[1:]
    halo_shape = (species, listed * block_size)
    grid_spec = pltpu.PrefetchScalarGridSpec(
        num_scalar_prefetch=1,
        grid=(1,),
        in_specs=[pl.BlockSpec(memory_space=pl.ANY)]
        + [vmem_whole((species, capacity))] * peer_count
        + [vmem_whole(slots.shape)],
        out_specs=[vmem_whole(halo_shape), vmem_whole(halo_shape)],
        scratch_shapes=[pltpu.SemaphoreType.DMA((sides, listed))],
    )
    to_lower, to_upper = pl.pallas_call(
        functools.partial(halo_kernel, chunk, block_size, peer_count),
        grid_spec=grid_spec,
        out_shape=[jax.ShapeDtypeStruct(halo_shape, mixing_ratio.dtype)] * sides,
    )(halo_blocks[0], mixing_ratio, *arrived, slots)
    migrated = pl.pallas_call(
        functools.partial(place_kernel, chunk, peer_count),
        grid=(1,),
        in_specs=[vmem_whole(mixing_ratio.shape)]
        + [vmem_whole((species, capacity))] * peer_count
        + [vmem_whole(slots.shape)],
        out_specs=vmem_whole(mixing_ratio.shape),
        out_shape=jax.ShapeDtypeStruct(mixing_ratio.shape, mixing_ratio.dtype),
    )(mixing_ratio, *arrived, slots)
    from_lower = from_behind(to_upper, "region", 1)
    from_upper = from_behind(to_lower, "region", -1)
    return migrated, from_lower, from_upper


def split3(x):
    high = x.astype(jnp.bfloat16)
    low = (x - high.astype(jnp.float32)).astype(jnp.bfloat16)
    return high, low


def dot3(a_high, a_low, b_high, b_low):
    f32 = jnp.float32
    total = jnp.dot(a_high, b_high, preferred_element_type=f32)
    total = total + jnp.dot(a_high, b_low, preferred_element_type=f32)
    return total + jnp.dot(a_low, b_high, preferred_element_type=f32)


def mix_react_kernel(
    tile_blocks,
    neighbours,
    block_size,
    nb_ref,
    own_ref,
    weight_ref,
    temp_ref,
    order_ref,
    prod_ref,
    loss_ref,
    migrated_hbm,
    lower_hbm,
    upper_hbm,
    out_ref,
    picked,
    sems,
    mixed_ref,
    terms_ref,
    order_split,
    gain_split,
    gain_high,
):
    f32 = jnp.float32
    step = pl.program_id(0)
    steps = pl.num_programs(0)
    own_count = migrated_hbm.shape[1] // block_size
    halo_count = lower_hbm.shape[1] // block_size

    def fetch(at, slot, start):
        for t in range(tile_blocks):
            for k in range(neighbours):
                index = nb_ref[k, at * tile_blocks + t]
                target = picked.at[slot, t * neighbours + k]
                sem = sems.at[slot, t * neighbours + k]
                if not start:
                    pltpu.make_async_copy(
                        migrated_hbm.at[:, pl.ds(0, block_size)], target, sem
                    ).wait()
                    continue
                sources = (
                    (migrated_hbm, index, index < own_count),
                    (lower_hbm, index - own_count,
                     (index >= own_count) & (index < own_count + halo_count)),
                    (upper_hbm, index - own_count - halo_count,
                     index >= own_count + halo_count),
                )
                for source, local, chosen in sources:
                    limit = source.shape[1] // block_size - 1
                    local = jnp.minimum(jnp.maximum(local, 0), limit)

                    @pl.when(chosen)
                    def _():
                        begin = pl.multiple_of(local * block_size, block_size)
                        pltpu.make_async_copy(
                            source.at[:, pl.ds(begin, block_size)], target, sem
                        ).start()

    @pl.when(step == 0)
    def _():
        fetch(0, 0, True)
        order_high, order_low = split3(order_ref[...].T)
        reactions = order_high.shape[0]
        order_split[0:reactions] = order_high
        order_split[reactions:] = order_low
        gain_split[...] = jnp.zeros_like(gain_split)
        rows = prod_ref.shape[0]
        for part, source in enumerate((prod_ref, loss_ref)):
            high, low = split3(source[...])
            gain_split[pl.ds(2 * part * PAD_ROWS, rows)] = high
            gain_split[pl.ds((2 * part + 1) * PAD_ROWS, rows)] = low
            gain_high[pl.ds(part * PAD_ROWS, rows)] = high
        gain_high[...] = jnp.where(
            lax.broadcasted_iota(jnp.int32, gain_high.shape, 0) % PAD_ROWS < rows,
            gain_high[...],
            jnp.zeros_like(gain_high),
        )

    slot = step % 2

    @pl.when(step + 1 < steps)
    def _():
        fetch(step + 1, 1 - slot, True)

    fetch(step, slot, False)

    for t in range(tile_blocks):
        lanes = slice(t * block_size, (t + 1) * block_size)
        stacked = jnp.concatenate(
            [own_ref[:, lanes]] + [picked[slot, t * neighbours + k] for k in range(neighbours)],
            axis=1,
        )
        weight = weight_ref[t].reshape((neighbours + 1) * block_size, block_size)
        mixed_ref[:, lanes] = jnp.dot(stacked, weight, preferred_element_type=f32)
    mixed = mixed_ref[...]
    species = mixed.shape[0]
    terms_ref[0:species] = jnp.log(mixed)
    terms_ref[species:species + 1] = jnp.ones((1, mixed.shape[1]), f32)
    terms_ref[species + 1:species + 2] = temp_ref[...]
    log_high, log_low = split3(terms_ref[...])
    reactions = order_split.shape[0] // 2
    both = jnp.dot(order_split[...], log_high, preferred_element_type=f32)
    exponent = both[:reactions] + both[reactions:]
    exponent = exponent + jnp.dot(order_split[0:reactions], log_low, preferred_element_type=f32)
    rate = jnp.exp(exponent)
    rate_high, rate_low = split3(rate)
    by_high = jnp.dot(gain_split[...], rate_high, preferred_element_type=f32)
    by_low = jnp.dot(gain_high[...], rate_low, preferred_element_type=f32)
    gained = by_high[0:species] + by_high[PAD_ROWS:PAD_ROWS + species] + by_low[0:species]
    lost_mass = (
        by_high[2 * PAD_ROWS:2 * PAD_ROWS + species]
        + by_high[3 * PAD_ROWS:3 * PAD_ROWS + species]
        + by_low[PAD_ROWS:PAD_ROWS + species]
    )
    out_ref[...] = (mixed + gained) / (1.0 + lost_mass / mixed)


def mix_react(
    migrated,
    from_lower,
    from_upper,
    neighbour_block,
    mix_weight,
    inverse_temp,
    reactant_order,
    log_prefactor,
    activation_energy,
    production,
    loss_coefficient,
):
    species = migrated.shape[0]
    count_blocks, _, block_size, _ = mix_weight.shape
    neighbours = neighbour_block.shape[1]
    reactions = reactant_order.shape[0]
    tile_blocks = TILE_BLOCKS
    width = tile_blocks * block_size
    steps = count_blocks // tile_blocks

    def whole(shape):
        return pl.BlockSpec(shape, lambda i, nb: (0,) * len(shape))

    in_specs = [
        pl.BlockSpec((species, width), lambda i, nb: (0, i)),
        pl.BlockSpec((tile_blocks,) + mix_weight.shape[1:], lambda i, nb: (i, 0, 0, 0)),
        pl.BlockSpec((1, width), lambda i, nb: (0, i)),
        whole((species + 2, reactions)),
        whole(production.shape),
        whole(loss_coefficient.shape),
        pl.BlockSpec(memory_space=pl.ANY),
        pl.BlockSpec(memory_space=pl.ANY),
        pl.BlockSpec(memory_space=pl.ANY),
    ]
    bf16 = jnp.bfloat16
    grid_spec = pltpu.PrefetchScalarGridSpec(
        num_scalar_prefetch=1,
        grid=(steps,),
        in_specs=in_specs,
        out_specs=pl.BlockSpec((species, width), lambda i, nb: (0, i)),
        scratch_shapes=[
            pltpu.VMEM((2, tile_blocks * neighbours, species, block_size), bf16),
            pltpu.SemaphoreType.DMA((2, tile_blocks * neighbours)),
            pltpu.VMEM((species, width), jnp.float32),
            pltpu.VMEM((species + 2, width), jnp.float32),
            pltpu.VMEM((2 * reactions, species + 2), bf16),
            pltpu.VMEM((4 * PAD_ROWS, reactions), bf16),
            pltpu.VMEM((2 * PAD_ROWS, reactions), bf16),
        ],
    )
    kernel = functools.partial(mix_react_kernel, tile_blocks, neighbours, block_size)
    return pl.pallas_call(
        kernel,
        grid_spec=grid_spec,
        out_shape=jax.ShapeDtypeStruct((species, count_blocks * block_size), jnp.float32),
        compiler_params=pltpu.CompilerParams(dimension_semantics=("arbitrary",)),
    )(
        neighbour_block.T,
        migrated,
        mix_weight,
        inverse_temp.reshape(1, -1),
        jnp.concatenate(
            [reactant_order.T, log_prefactor[None, :], -activation_energy[None, :]], axis=0
        ),
        production,
        loss_coefficient,
        migrated,
        from_lower,
        from_upper,
    )


def shards(
    mixing_ratio,
    send_rows,
    migrant_count,
    arrival_slot,
    halo_blocks,
    neighbour_block,
    mix_weight,
    inverse_temp,
    reactant_order,
    log_prefactor,
    activation_energy,
    production,
    loss_coefficient,
):
    migrated, from_lower, from_upper = migrate(
        mixing_ratio, send_rows, migrant_count, arrival_slot, halo_blocks, mix_weight.shape[-1]
    )
    return mix_react(
        migrated,
        from_lower,
        from_upper,
        neighbour_block,
        mix_weight,
        inverse_temp,
        reactant_order,
        log_prefactor,
        activation_energy,
        production,
        loss_coefficient,
    )


def solution(mesh):
    placed = (
        P(None, "region"),
        P("region", None, None),
        P("region", None),
        P("region", None, None),
        P("region", None, None),
        P("region", None),
        P("region", None, None, None),
        P("region"),
        P(),
        P(),
        P(),
        P(),
        P(),
    )
    return jax.shard_map(
        shards, mesh=mesh, in_specs=placed, out_specs=P(None, "region"), check_vma=False
    )
```

```python
import functools

import jax
import jax.numpy as jnp
from jax import lax
from jax.experimental import pallas as pl
from jax.experimental.pallas import tpu as pltpu
from jax.sharding import PartitionSpec as P

HOP = 4
TILE_BLOCKS = 32
PAD_ROWS = 160


def from_behind(block, axis, distance):
    devices = range(lax.axis_size(axis))
    route = [((i - distance) % len(devices), i) for i in devices]
    return lax.ppermute(block, axis, route)


def peer_offsets():
    return [column - HOP if column < HOP else column - HOP + 1 for column in range(2 * HOP)]


def pick_kernel(chunk, mixing_ref, rows_ref, *out_refs):
    species, parcels = mixing_ref.shape
    wanted = rows_ref[...]
    total = jnp.zeros((species, wanted.shape[1]), jnp.float32)
    for part in range(parcels // chunk):
        position = lax.broadcasted_iota(jnp.int32, (chunk, wanted.shape[1]), 0) + part * chunk
        pick = (position == wanted).astype(jnp.bfloat16)
        total = total + jnp.dot(
            mixing_ref[:, part * chunk:(part + 1) * chunk], pick, preferred_element_type=jnp.float32
        )
    width = out_refs[0].shape[1]
    for column, out_ref in enumerate(out_refs):
        out_ref[...] = total[:, column * width:(column + 1) * width].astype(out_ref.dtype)


def marked_arrivals(received_refs, rows):
    received = jnp.concatenate([ref[...] for ref in received_refs], axis=1)
    species = received.shape[0]
    pad = (-species) % 16 or 16
    return jnp.concatenate([received, jnp.ones((pad, rows), received.dtype)], axis=0)


def place_kernel(chunk, peer_count, mixing_ref, *refs):
    received_refs = refs[:peer_count]
    slots_ref, migrated_ref = refs[peer_count:]
    species, parcels = mixing_ref.shape
    slots = slots_ref[...]
    marked = marked_arrivals(received_refs, slots.shape[0])
    for part in range(parcels // chunk):
        lanes = slice(part * chunk, (part + 1) * chunk)
        position = lax.broadcasted_iota(jnp.int32, (slots.shape[0], chunk), 1) + part * chunk
        place = (position == slots).astype(jnp.bfloat16)
        placed = jnp.dot(marked, place, preferred_element_type=jnp.float32)
        hit = placed[species:species + 1]
        migrated_ref[:, lanes] = jnp.where(
            hit > 0.5, placed[:species].astype(migrated_ref.dtype), mixing_ref[:, lanes]
        )


def halo_kernel(chunk, block_size, peer_count, halo_ref, mixing_ref, *refs):
    received_refs = refs[:peer_count]
    slots_ref, lower_ref, upper_ref, sems = refs[peer_count:]
    species = mixing_ref.shape[0]
    sides, listed = halo_ref.shape
    outs = (lower_ref, upper_ref)
    copies = []
    for side in range(sides):
        for j in range(listed):
            start = pl.multiple_of(halo_ref[side, j] * block_size, block_size)
            copy = pltpu.make_async_copy(
                mixing_ref.at[:, pl.ds(start, block_size)],
                outs[side].at[:, pl.ds(j * block_size, block_size)],
                sems.at[side, j],
            )
            copy.start()
            copies.append(copy)
    slots = slots_ref[...]
    marked = marked_arrivals(received_refs, slots.shape[0])
    lane = lax.broadcasted_iota(jnp.int32, (1, block_size), 1)
    per_chunk = chunk // block_size
    for copy in copies:
        copy.wait()
    for side in range(sides):
        for part in range(listed // per_chunk):
            first = part * per_chunk
            where_to = jnp.concatenate(
                [lane + halo_ref[side, j] * block_size for j in range(first, first + per_chunk)],
                axis=1,
            )
            place = (where_to == slots).astype(jnp.bfloat16)
            placed = jnp.dot(marked, place, preferred_element_type=jnp.float32)
            hit = placed[species:species + 1]
            lanes = slice(first * block_size, (first + per_chunk) * block_size)
            outs[side][:, lanes] = jnp.where(
                hit > 0.5, placed[:species].astype(outs[side].dtype), outs[side][:, lanes]
            )


def vmem_whole(shape):
    return pl.BlockSpec(shape, lambda *_: (0,) * len(shape))


def migrate(mixing_ratio, send_rows, migrant_count, arrival_slot, halo_blocks, block_size):
    species, parcels = mixing_ratio.shape
    capacity = send_rows.shape[-1]
    offsets = peer_offsets()
    peer_count = len(offsets)
    chunk = 1024
    wanted = send_rows[0].reshape(1, -1)
    outgoing = pl.pallas_call(
        functools.partial(pick_kernel, chunk),
        grid=(1,),
        in_specs=[vmem_whole(mixing_ratio.shape), vmem_whole(wanted.shape)],
        out_specs=[vmem_whole((species, capacity))] * peer_count,
        out_shape=[jax.ShapeDtypeStruct((species, capacity), mixing_ratio.dtype)] * peer_count,
    )(mixing_ratio, wanted)
    arrived = []
    for column in range(peer_count):
        opposite = peer_count - 1 - column
        arrived.append(from_behind(outgoing[opposite], "region", -offsets[column]))
    lane_index = jnp.arange(capacity, dtype=jnp.int32)
    live_lane = lane_index[None, :] < migrant_count[0][:, None]
    slots = jnp.where(live_lane, arrival_slot[0], parcels).reshape(-1, 1)
    sides, listed = halo_blocks.shape[1:]
    halo_shape = (species, listed * block_size)
    grid_spec = pltpu.PrefetchScalarGridSpec(
        num_scalar_prefetch=1,
        grid=(1,),
        in_specs=[pl.BlockSpec(memory_space=pl.ANY)]
        + [vmem_whole((species, capacity))] * peer_count
        + [vmem_whole(slots.shape)],
        out_specs=[vmem_whole(halo_shape), vmem_whole(halo_shape)],
        scratch_shapes=[pltpu.SemaphoreType.DMA((sides, listed))],
    )
    to_lower, to_upper = pl.pallas_call(
        functools.partial(halo_kernel, chunk, block_size, peer_count),
        grid_spec=grid_spec,
        out_shape=[jax.ShapeDtypeStruct(halo_shape, mixing_ratio.dtype)] * sides,
    )(halo_blocks[0], mixing_ratio, *arrived, slots)
    migrated = pl.pallas_call(
        functools.partial(place_kernel, chunk, peer_count),
        grid=(1,),
        in_specs=[vmem_whole(mixing_ratio.shape)]
        + [vmem_whole((species, capacity))] * peer_count
        + [vmem_whole(slots.shape)],
        out_specs=vmem_whole(mixing_ratio.shape),
        out_shape=jax.ShapeDtypeStruct(mixing_ratio.shape, mixing_ratio.dtype),
    )(mixing_ratio, *arrived, slots)
    from_lower = from_behind(to_upper, "region", 1)
    from_upper = from_behind(to_lower, "region", -1)
    return migrated, from_lower, from_upper


def split3(x):
    high = x.astype(jnp.bfloat16)
    low = (x - high.astype(jnp.float32)).astype(jnp.bfloat16)
    return high, low


def dot3(a_high, a_low, b_high, b_low):
    f32 = jnp.float32
    total = jnp.dot(a_high, b_high, preferred_element_type=f32)
    total = total + jnp.dot(a_high, b_low, preferred_element_type=f32)
    return total + jnp.dot(a_low, b_high, preferred_element_type=f32)


def mix_react_kernel(
    tile_blocks,
    neighbours,
    block_size,
    nb_ref,
    own_ref,
    weight_ref,
    temp_ref,
    order_ref,
    prod_ref,
    loss_ref,
    migrated_hbm,
    lower_hbm,
    upper_hbm,
    out_ref,
    picked,
    sems,
    mixed_ref,
    terms_ref,
    order_split,
    gain_split,
    gain_high,
):
    f32 = jnp.float32
    step = pl.program_id(0)
    steps = pl.num_programs(0)
    own_count = migrated_hbm.shape[1] // block_size
    halo_count = lower_hbm.shape[1] // block_size

    def fetch(at, slot, start):
        for t in range(tile_blocks):
            for k in range(neighbours):
                index = nb_ref[k, at * tile_blocks + t]
                target = picked.at[slot, t * neighbours + k]
                sem = sems.at[slot, t * neighbours + k]
                if not start:
                    pltpu.make_async_copy(
                        migrated_hbm.at[:, pl.ds(0, block_size)], target, sem
                    ).wait()
                    continue
                sources = (
                    (migrated_hbm, index, index < own_count),
                    (lower_hbm, index - own_count,
                     (index >= own_count) & (index < own_count + halo_count)),
                    (upper_hbm, index - own_count - halo_count,
                     index >= own_count + halo_count),
                )
                for source, local, chosen in sources:
                    limit = source.shape[1] // block_size - 1
                    local = jnp.minimum(jnp.maximum(local, 0), limit)

                    @pl.when(chosen)
                    def _():
                        begin = pl.multiple_of(local * block_size, block_size)
                        pltpu.make_async_copy(
                            source.at[:, pl.ds(begin, block_size)], target, sem
                        ).start()

    @pl.when(step == 0)
    def _():
        fetch(0, 0, True)
        order_high, order_low = split3(order_ref[...].T)
        reactions = order_high.shape[0]
        order_split[0:reactions] = order_high
        order_split[reactions:] = order_low
        gain_split[...] = jnp.zeros_like(gain_split)
        rows = prod_ref.shape[0]
        for part, source in enumerate((prod_ref, loss_ref)):
            high, low = split3(source[...])
            gain_split[pl.ds(2 * part * PAD_ROWS, rows)] = high
            gain_split[pl.ds((2 * part + 1) * PAD_ROWS, rows)] = low
            gain_high[pl.ds(part * PAD_ROWS, rows)] = high
        gain_high[...] = jnp.where(
            lax.broadcasted_iota(jnp.int32, gain_high.shape, 0) % PAD_ROWS < rows,
            gain_high[...],
            jnp.zeros_like(gain_high),
        )

    slot = step % 2

    @pl.when(step + 1 < steps)
    def _():
        fetch(step + 1, 1 - slot, True)

    fetch(step, slot, False)

    for t in range(tile_blocks):
        lanes = slice(t * block_size, (t + 1) * block_size)
        stacked = jnp.concatenate(
            [own_ref[:, lanes]] + [picked[slot, t * neighbours + k] for k in range(neighbours)],
            axis=1,
        )
        weight = weight_ref[t].reshape((neighbours + 1) * block_size, block_size)
        mixed_ref[:, lanes] = jnp.dot(stacked, weight, preferred_element_type=f32)
    mixed = mixed_ref[...]
    species = mixed.shape[0]
    terms_ref[0:species] = jnp.log(mixed)
    terms_ref[species:species + 1] = jnp.ones((1, mixed.shape[1]), f32)
    terms_ref[species + 1:species + 2] = temp_ref[...]
    log_high, log_low = split3(terms_ref[...])
    reactions = order_split.shape[0] // 2
    both = jnp.dot(order_split[...], log_high, preferred_element_type=f32)
    exponent = both[:reactions] + both[reactions:]
    exponent = exponent + jnp.dot(order_split[0:reactions], log_low, preferred_element_type=f32)
    rate = jnp.exp(exponent)
    rate_high, rate_low = split3(rate)
    by_high = jnp.dot(gain_split[...], rate_high, preferred_element_type=f32)
    by_low = jnp.dot(gain_high[...], rate_low, preferred_element_type=f32)
    gained = by_high[0:species] + by_high[PAD_ROWS:PAD_ROWS + species] + by_low[0:species]
    lost_mass = (
        by_high[2 * PAD_ROWS:2 * PAD_ROWS + species]
        + by_high[3 * PAD_ROWS:3 * PAD_ROWS + species]
        + by_low[PAD_ROWS:PAD_ROWS + species]
    )
    out_ref[...] = (mixed + gained) / (1.0 + lost_mass / mixed)


def mix_react(
    migrated,
    from_lower,
    from_upper,
    neighbour_block,
    mix_weight,
    inverse_temp,
    reactant_order,
    log_prefactor,
    activation_energy,
    production,
    loss_coefficient,
):
    species = migrated.shape[0]
    count_blocks, _, block_size, _ = mix_weight.shape
    neighbours = neighbour_block.shape[1]
    reactions = reactant_order.shape[0]
    tile_blocks = TILE_BLOCKS
    width = tile_blocks * block_size
    steps = count_blocks // tile_blocks

    def whole(shape):
        return pl.BlockSpec(shape, lambda i, nb: (0,) * len(shape))

    in_specs = [
        pl.BlockSpec((species, width), lambda i, nb: (0, i)),
        pl.BlockSpec((tile_blocks,) + mix_weight.shape[1:], lambda i, nb: (i, 0, 0, 0)),
        pl.BlockSpec((1, width), lambda i, nb: (0, i)),
        whole((species + 2, reactions)),
        whole(production.shape),
        whole(loss_coefficient.shape),
        pl.BlockSpec(memory_space=pl.ANY),
        pl.BlockSpec(memory_space=pl.ANY),
        pl.BlockSpec(memory_space=pl.ANY),
    ]
    bf16 = jnp.bfloat16
    grid_spec = pltpu.PrefetchScalarGridSpec(
        num_scalar_prefetch=1,
        grid=(steps,),
        in_specs=in_specs,
        out_specs=pl.BlockSpec((species, width), lambda i, nb: (0, i)),
        scratch_shapes=[
            pltpu.VMEM((2, tile_blocks * neighbours, species, block_size), bf16),
            pltpu.SemaphoreType.DMA((2, tile_blocks * neighbours)),
            pltpu.VMEM((species, width), jnp.float32),
            pltpu.VMEM((species + 2, width), jnp.float32),
            pltpu.VMEM((2 * reactions, species + 2), bf16),
            pltpu.VMEM((4 * PAD_ROWS, reactions), bf16),
            pltpu.VMEM((2 * PAD_ROWS, reactions), bf16),
        ],
    )
    kernel = functools.partial(mix_react_kernel, tile_blocks, neighbours, block_size)
    return pl.pallas_call(
        kernel,
        grid_spec=grid_spec,
        out_shape=jax.ShapeDtypeStruct((species, count_blocks * block_size), jnp.float32),
        compiler_params=pltpu.CompilerParams(dimension_semantics=("arbitrary",)),
    )(
        neighbour_block.T,
        migrated,
        mix_weight,
        inverse_temp.reshape(1, -1),
        jnp.concatenate(
            [reactant_order.T, log_prefactor[None, :], -activation_energy[None, :]], axis=0
        ),
        production,
        loss_coefficient,
        migrated,
        from_lower,
        from_upper,
    )


def shards(
    mixing_ratio,
    send_rows,
    migrant_count,
    arrival_slot,
    halo_blocks,
    neighbour_block,
    mix_weight,
    inverse_temp,
    reactant_order,
    log_prefactor,
    activation_energy,
    production,
    loss_coefficient,
):
    migrated, from_lower, from_upper = migrate(
        mixing_ratio, send_rows, migrant_count, arrival_slot, halo_blocks, mix_weight.shape[-1]
    )
    return mix_react(
        migrated,
        from_lower,
        from_upper,
        neighbour_block,
        mix_weight,
        inverse_temp,
        reactant_order,
        log_prefactor,
        activation_energy,
        production,
        loss_coefficient,
    )


def solution(mesh):
    placed = (
        P(None, "region"),
        P("region", None, None),
        P("region", None),
        P("region", None, None),
        P("region", None, None),
        P("region", None),
        P("region", None, None, None),
        P("region"),
        P(),
        P(),
        P(),
        P(),
        P(),
    )
    return jax.shard_map(
        shards, mesh=mesh, in_specs=placed, out_specs=P(None, "region"), check_vma=False
    )
```

```python
import functools

import jax
import jax.numpy as jnp
from jax import lax
from jax.experimental import pallas as pl
from jax.experimental.pallas import tpu as pltpu
from jax.sharding import PartitionSpec as P

HOP = 4
TILE_BLOCKS = 16
PAD_ROWS = 160


def from_behind(block, axis, distance):
    devices = range(lax.axis_size(axis))
    route = [((i - distance) % len(devices), i) for i in devices]
    return lax.ppermute(block, axis, route)


def peer_offsets():
    return [column - HOP if column < HOP else column - HOP + 1 for column in range(2 * HOP)]


def pick_kernel(chunk, mixing_ref, rows_ref, *out_refs):
    species, parcels = mixing_ref.shape
    wanted = rows_ref[...]
    total = jnp.zeros((species, wanted.shape[1]), jnp.float32)
    for part in range(parcels // chunk):
        position = lax.broadcasted_iota(jnp.int32, (chunk, wanted.shape[1]), 0) + part * chunk
        pick = (position == wanted).astype(jnp.bfloat16)
        total = total + jnp.dot(
            mixing_ref[:, part * chunk:(part + 1) * chunk], pick, preferred_element_type=jnp.float32
        )
    width = out_refs[0].shape[1]
    for column, out_ref in enumerate(out_refs):
        out_ref[...] = total[:, column * width:(column + 1) * width].astype(out_ref.dtype)


def marked_arrivals(received_refs, rows):
    received = jnp.concatenate([ref[...] for ref in received_refs], axis=1)
    species = received.shape[0]
    pad = (-species) % 16 or 16
    return jnp.concatenate([received, jnp.ones((pad, rows), received.dtype)], axis=0)


def place_kernel(chunk, peer_count, mixing_ref, *refs):
    received_refs = refs[:peer_count]
    slots_ref, migrated_ref = refs[peer_count:]
    species = mixing_ref.shape[0]
    slots = slots_ref[...]
    marked = marked_arrivals(received_refs, slots.shape[0])
    position = lax.broadcasted_iota(jnp.int32, (slots.shape[0], chunk), 1)
    place = (position + pl.program_id(0) * chunk == slots).astype(jnp.bfloat16)
    placed = jnp.dot(marked, place, preferred_element_type=jnp.float32)
    hit = placed[species:species + 1]
    migrated_ref[...] = jnp.where(
        hit > 0.5, placed[:species].astype(migrated_ref.dtype), mixing_ref[...]
    )


def halo_kernel(chunk, block_size, peer_count, halo_ref, mixing_ref, *refs):
    received_refs = refs[:peer_count]
    slots_ref, lower_ref, upper_ref, sems = refs[peer_count:]
    species = mixing_ref.shape[0]
    sides, listed = halo_ref.shape
    outs = (lower_ref, upper_ref)
    copies = []
    for side in range(sides):
        for j in range(listed):
            start = pl.multiple_of(halo_ref[side, j] * block_size, block_size)
            copy = pltpu.make_async_copy(
                mixing_ref.at[:, pl.ds(start, block_size)],
                outs[side].at[:, pl.ds(j * block_size, block_size)],
                sems.at[side, j],
            )
            copy.start()
            copies.append(copy)
    slots = slots_ref[...]
    marked = marked_arrivals(received_refs, slots.shape[0])
    lane = lax.broadcasted_iota(jnp.int32, (1, block_size), 1)
    per_chunk = chunk // block_size
    for copy in copies:
        copy.wait()
    for side in range(sides):
        for part in range(listed // per_chunk):
            first = part * per_chunk
            where_to = jnp.concatenate(
                [lane + halo_ref[side, j] * block_size for j in range(first, first + per_chunk)],
                axis=1,
            )
            place = (where_to == slots).astype(jnp.bfloat16)
            placed = jnp.dot(marked, place, preferred_element_type=jnp.float32)
            hit = placed[species:species + 1]
            lanes = slice(first * block_size, (first + per_chunk) * block_size)
            outs[side][:, lanes] = jnp.where(
                hit > 0.5, placed[:species].astype(outs[side].dtype), outs[side][:, lanes]
            )


def vmem_whole(shape):
    return pl.BlockSpec(shape, lambda *_: (0,) * len(shape))


def migrate(mixing_ratio, send_rows, migrant_count, arrival_slot, halo_blocks, block_size):
    species, parcels = mixing_ratio.shape
    capacity = send_rows.shape[-1]
    offsets = peer_offsets()
    peer_count = len(offsets)
    chunk = 1024
    wanted = send_rows[0].reshape(1, -1)
    outgoing = pl.pallas_call(
        functools.partial(pick_kernel, chunk),
        grid=(1,),
        in_specs=[vmem_whole(mixing_ratio.shape), vmem_whole(wanted.shape)],
        out_specs=[vmem_whole((species, capacity))] * peer_count,
        out_shape=[jax.ShapeDtypeStruct((species, capacity), mixing_ratio.dtype)] * peer_count,
    )(mixing_ratio, wanted)
    arrived = []
    for column in range(peer_count):
        opposite = peer_count - 1 - column
        arrived.append(from_behind(outgoing[opposite], "region", -offsets[column]))
    lane_index = jnp.arange(capacity, dtype=jnp.int32)
    live_lane = lane_index[None, :] < migrant_count[0][:, None]
    slots = jnp.where(live_lane, arrival_slot[0], parcels).reshape(-1, 1)
    sides, listed = halo_blocks.shape[1:]
    halo_shape = (species, listed * block_size)
    grid_spec = pltpu.PrefetchScalarGridSpec(
        num_scalar_prefetch=1,
        grid=(1,),
        in_specs=[pl.BlockSpec(memory_space=pl.ANY)]
        + [vmem_whole((species, capacity))] * peer_count
        + [vmem_whole(slots.shape)],
        out_specs=[vmem_whole(halo_shape), vmem_whole(halo_shape)],
        scratch_shapes=[pltpu.SemaphoreType.DMA((sides, listed))],
    )
    to_lower, to_upper = pl.pallas_call(
        functools.partial(halo_kernel, chunk, block_size, peer_count),
        grid_spec=grid_spec,
        out_shape=[jax.ShapeDtypeStruct(halo_shape, mixing_ratio.dtype)] * sides,
    )(halo_blocks[0], mixing_ratio, *arrived, slots)
    migrated = pl.pallas_call(
        functools.partial(place_kernel, chunk, peer_count),
        grid=(parcels // chunk,),
        in_specs=[pl.BlockSpec((species, chunk), lambda i: (0, i))]
        + [vmem_whole((species, capacity))] * peer_count
        + [vmem_whole(slots.shape)],
        out_specs=pl.BlockSpec((species, chunk), lambda i: (0, i)),
        out_shape=jax.ShapeDtypeStruct(mixing_ratio.shape, mixing_ratio.dtype),
    )(mixing_ratio, *arrived, slots)
    from_lower = from_behind(to_upper, "region", 1)
    from_upper = from_behind(to_lower, "region", -1)
    return migrated, from_lower, from_upper


def split3(x):
    high = x.astype(jnp.bfloat16)
    low = (x - high.astype(jnp.float32)).astype(jnp.bfloat16)
    return high, low


def dot3(a_high, a_low, b_high, b_low):
    f32 = jnp.float32
    total = jnp.dot(a_high, b_high, preferred_element_type=f32)
    total = total + jnp.dot(a_high, b_low, preferred_element_type=f32)
    return total + jnp.dot(a_low, b_high, preferred_element_type=f32)


def mix_react_kernel(
    tile_blocks,
    neighbours,
    block_size,
    nb_ref,
    own_ref,
    weight_ref,
    temp_ref,
    order_ref,
    prod_ref,
    loss_ref,
    migrated_hbm,
    lower_hbm,
    upper_hbm,
    out_ref,
    picked,
    sems,
    mixed_ref,
    terms_ref,
    order_split,
    gain_split,
    gain_high,
):
    f32 = jnp.float32
    step = pl.program_id(0)
    steps = pl.num_programs(0)
    own_count = migrated_hbm.shape[1] // block_size
    halo_count = lower_hbm.shape[1] // block_size

    def fetch(at, slot, start):
        for t in range(tile_blocks):
            for k in range(neighbours):
                index = nb_ref[k, at * tile_blocks + t]
                target = picked.at[slot, t * neighbours + k]
                sem = sems.at[slot, t * neighbours + k]
                if not start:
                    pltpu.make_async_copy(
                        migrated_hbm.at[:, pl.ds(0, block_size)], target, sem
                    ).wait()
                    continue
                sources = (
                    (migrated_hbm, index, index < own_count),
                    (lower_hbm, index - own_count,
                     (index >= own_count) & (index < own_count + halo_count)),
                    (upper_hbm, index - own_count - halo_count,
                     index >= own_count + halo_count),
                )
                for source, local, chosen in sources:
                    limit = source.shape[1] // block_size - 1
                    local = jnp.minimum(jnp.maximum(local, 0), limit)

                    @pl.when(chosen)
                    def _():
                        begin = pl.multiple_of(local * block_size, block_size)
                        pltpu.make_async_copy(
                            source.at[:, pl.ds(begin, block_size)], target, sem
                        ).start()

    @pl.when(step == 0)
    def _():
        fetch(0, 0, True)
        order_high, order_low = split3(order_ref[...].T)
        reactions = order_high.shape[0]
        order_split[0:reactions] = order_high
        order_split[reactions:] = order_low
        gain_split[...] = jnp.zeros_like(gain_split)
        rows = prod_ref.shape[0]
        for part, source in enumerate((prod_ref, loss_ref)):
            high, low = split3(source[...])
            gain_split[pl.ds(2 * part * PAD_ROWS, rows)] = high
            gain_split[pl.ds((2 * part + 1) * PAD_ROWS, rows)] = low
            gain_high[pl.ds(part * PAD_ROWS, rows)] = high
        gain_high[...] = jnp.where(
            lax.broadcasted_iota(jnp.int32, gain_high.shape, 0) % PAD_ROWS < rows,
            gain_high[...],
            jnp.zeros_like(gain_high),
        )

    slot = step % 2

    @pl.when(step + 1 < steps)
    def _():
        fetch(step + 1, 1 - slot, True)

    fetch(step, slot, False)

    for t in range(tile_blocks):
        lanes = slice(t * block_size, (t + 1) * block_size)
        stacked = jnp.concatenate(
            [own_ref[:, lanes]] + [picked[slot, t * neighbours + k] for k in range(neighbours)],
            axis=1,
        )
        weight = weight_ref[t].reshape((neighbours + 1) * block_size, block_size)
        mixed_ref[:, lanes] = jnp.dot(stacked, weight, preferred_element_type=f32)
    mixed = mixed_ref[...]
    species = mixed.shape[0]
    terms_ref[0:species] = jnp.log(mixed)
    terms_ref[species:species + 1] = jnp.ones((1, mixed.shape[1]), f32)
    terms_ref[species + 1:species + 2] = temp_ref[...]
    log_high, log_low = split3(terms_ref[...])
    reactions = order_split.shape[0] // 2
    both = jnp.dot(order_split[...], log_high, preferred_element_type=f32)
    exponent = both[:reactions] + both[reactions:]
    exponent = exponent + jnp.dot(order_split[0:reactions], log_low, preferred_element_type=f32)
    rate = jnp.exp(exponent)
    rate_high, rate_low = split3(rate)
    by_high = jnp.dot(gain_split[...], rate_high, preferred_element_type=f32)
    by_low = jnp.dot(gain_high[...], rate_low, preferred_element_type=f32)
    gained = by_high[0:species] + by_high[PAD_ROWS:PAD_ROWS + species] + by_low[0:species]
    lost_mass = (
        by_high[2 * PAD_ROWS:2 * PAD_ROWS + species]
        + by_high[3 * PAD_ROWS:3 * PAD_ROWS + species]
        + by_low[PAD_ROWS:PAD_ROWS + species]
    )
    out_ref[...] = (mixed + gained) / (1.0 + lost_mass / mixed)


def mix_react(
    migrated,
    from_lower,
    from_upper,
    neighbour_block,
    mix_weight,
    inverse_temp,
    reactant_order,
    log_prefactor,
    activation_energy,
    production,
    loss_coefficient,
):
    species = migrated.shape[0]
    count_blocks, _, block_size, _ = mix_weight.shape
    neighbours = neighbour_block.shape[1]
    reactions = reactant_order.shape[0]
    tile_blocks = TILE_BLOCKS
    width = tile_blocks * block_size
    steps = count_blocks // tile_blocks

    def whole(shape):
        return pl.BlockSpec(shape, lambda i, nb: (0,) * len(shape))

    in_specs = [
        pl.BlockSpec((species, width), lambda i, nb: (0, i)),
        pl.BlockSpec((tile_blocks,) + mix_weight.shape[1:], lambda i, nb: (i, 0, 0, 0)),
        pl.BlockSpec((1, width), lambda i, nb: (0, i)),
        whole((species + 2, reactions)),
        whole(production.shape),
        whole(loss_coefficient.shape),
        pl.BlockSpec(memory_space=pl.ANY),
        pl.BlockSpec(memory_space=pl.ANY),
        pl.BlockSpec(memory_space=pl.ANY),
    ]
    bf16 = jnp.bfloat16
    grid_spec = pltpu.PrefetchScalarGridSpec(
        num_scalar_prefetch=1,
        grid=(steps,),
        in_specs=in_specs,
        out_specs=pl.BlockSpec((species, width), lambda i, nb: (0, i)),
        scratch_shapes=[
            pltpu.VMEM((2, tile_blocks * neighbours, species, block_size), bf16),
            pltpu.SemaphoreType.DMA((2, tile_blocks * neighbours)),
            pltpu.VMEM((species, width), jnp.float32),
            pltpu.VMEM((species + 2, width), jnp.float32),
            pltpu.VMEM((2 * reactions, species + 2), bf16),
            pltpu.VMEM((4 * PAD_ROWS, reactions), bf16),
            pltpu.VMEM((2 * PAD_ROWS, reactions), bf16),
        ],
    )
    kernel = functools.partial(mix_react_kernel, tile_blocks, neighbours, block_size)
    return pl.pallas_call(
        kernel,
        grid_spec=grid_spec,
        out_shape=jax.ShapeDtypeStruct((species, count_blocks * block_size), jnp.float32),
        compiler_params=pltpu.CompilerParams(dimension_semantics=("arbitrary",)),
    )(
        neighbour_block.T,
        migrated,
        mix_weight,
        inverse_temp.reshape(1, -1),
        jnp.concatenate(
            [reactant_order.T, log_prefactor[None, :], -activation_energy[None, :]], axis=0
        ),
        production,
        loss_coefficient,
        migrated,
        from_lower,
        from_upper,
    )


def shards(
    mixing_ratio,
    send_rows,
    migrant_count,
    arrival_slot,
    halo_blocks,
    neighbour_block,
    mix_weight,
    inverse_temp,
    reactant_order,
    log_prefactor,
    activation_energy,
    production,
    loss_coefficient,
):
    migrated, from_lower, from_upper = migrate(
        mixing_ratio, send_rows, migrant_count, arrival_slot, halo_blocks, mix_weight.shape[-1]
    )
    return mix_react(
        migrated,
        from_lower,
        from_upper,
        neighbour_block,
        mix_weight,
        inverse_temp,
        reactant_order,
        log_prefactor,
        activation_energy,
        production,
        loss_coefficient,
    )


def solution(mesh):
    placed = (
        P(None, "region"),
        P("region", None, None),
        P("region", None),
        P("region", None, None),
        P("region", None, None),
        P("region", None),
        P("region", None, None, None),
        P("region"),
        P(),
        P(),
        P(),
        P(),
        P(),
    )
    return jax.shard_map(
        shards, mesh=mesh, in_specs=placed, out_specs=P(None, "region"), check_vma=False
    )
```

```python
import functools

import jax
import jax.numpy as jnp
from jax import lax
from jax.experimental import pallas as pl
from jax.experimental.pallas import tpu as pltpu
from jax.sharding import PartitionSpec as P

HOP = 4
TILE_BLOCKS = 16
PAD_ROWS = 160


def from_behind(block, axis, distance):
    devices = range(lax.axis_size(axis))
    route = [((i - distance) % len(devices), i) for i in devices]
    return lax.ppermute(block, axis, route)


def peer_offsets():
    return [column - HOP if column < HOP else column - HOP + 1 for column in range(2 * HOP)]


def pick_kernel(chunk, mixing_ref, rows_ref, *out_refs):
    species, parcels = mixing_ref.shape
    wanted = rows_ref[...]
    total = jnp.zeros((species, wanted.shape[1]), jnp.float32)
    for part in range(parcels // chunk):
        position = lax.broadcasted_iota(jnp.int32, (chunk, wanted.shape[1]), 0) + part * chunk
        pick = (position == wanted).astype(jnp.bfloat16)
        total = total + jnp.dot(
            mixing_ref[:, part * chunk:(part + 1) * chunk], pick, preferred_element_type=jnp.float32
        )
    width = out_refs[0].shape[1]
    for column, out_ref in enumerate(out_refs):
        out_ref[...] = total[:, column * width:(column + 1) * width].astype(out_ref.dtype)


def marked_arrivals(received_refs, rows):
    received = jnp.concatenate([ref[...] for ref in received_refs], axis=1)
    species = received.shape[0]
    pad = (-species) % 16 or 16
    return jnp.concatenate([received, jnp.ones((pad, rows), received.dtype)], axis=0)


def place_kernel(chunk, peer_count, mixing_ref, *refs):
    received_refs = refs[:peer_count]
    slots_ref, migrated_ref = refs[peer_count:]
    species, parcels = mixing_ref.shape
    slots = slots_ref[...]
    marked = marked_arrivals(received_refs, slots.shape[0])
    for part in range(parcels // chunk):
        lanes = slice(part * chunk, (part + 1) * chunk)
        position = lax.broadcasted_iota(jnp.int32, (slots.shape[0], chunk), 1) + part * chunk
        place = (position == slots).astype(jnp.bfloat16)
        placed = jnp.dot(marked, place, preferred_element_type=jnp.float32)
        hit = placed[species:species + 1]
        migrated_ref[:, lanes] = jnp.where(
            hit > 0.5, placed[:species].astype(migrated_ref.dtype), mixing_ref[:, lanes]
        )


def halo_kernel(chunk, block_size, peer_count, halo_ref, mixing_ref, *refs):
    received_refs = refs[:peer_count]
    slots_ref, lower_ref, upper_ref, sems = refs[peer_count:]
    species = mixing_ref.shape[0]
    sides, listed = halo_ref.shape
    outs = (lower_ref, upper_ref)
    copies = []
    for side in range(sides):
        for j in range(listed):
            start = pl.multiple_of(halo_ref[side, j] * block_size, block_size)
            copy = pltpu.make_async_copy(
                mixing_ref.at[:, pl.ds(start, block_size)],
                outs[side].at[:, pl.ds(j * block_size, block_size)],
                sems.at[side, j],
            )
            copy.start()
            copies.append(copy)
    slots = slots_ref[...]
    marked = marked_arrivals(received_refs, slots.shape[0])
    lane = lax.broadcasted_iota(jnp.int32, (1, block_size), 1)
    per_chunk = chunk // block_size
    for side in range(sides):
        for part in range(listed // per_chunk):
            first = part * per_chunk
            where_to = jnp.concatenate(
                [lane + halo_ref[side, j] * block_size for j in range(first, first + per_chunk)],
                axis=1,
            )
            place = (where_to == slots).astype(jnp.bfloat16)
            placed = jnp.dot(marked, place, preferred_element_type=jnp.float32)
            hit = placed[species:species + 1]
            lanes = slice(first * block_size, (first + per_chunk) * block_size)
            if side == 0 and part == 0:
                for copy in copies:
                    copy.wait()
            outs[side][:, lanes] = jnp.where(
                hit > 0.5, placed[:species].astype(outs[side].dtype), outs[side][:, lanes]
            )


def vmem_whole(shape):
    return pl.BlockSpec(shape, lambda *_: (0,) * len(shape))


def migrate(mixing_ratio, send_rows, migrant_count, arrival_slot, halo_blocks, block_size):
    species, parcels = mixing_ratio.shape
    capacity = send_rows.shape[-1]
    offsets = peer_offsets()
    peer_count = len(offsets)
    chunk = 1024
    wanted = send_rows[0].reshape(1, -1)
    outgoing = pl.pallas_call(
        functools.partial(pick_kernel, chunk),
        grid=(1,),
        in_specs=[vmem_whole(mixing_ratio.shape), vmem_whole(wanted.shape)],
        out_specs=[vmem_whole((species, capacity))] * peer_count,
        out_shape=[jax.ShapeDtypeStruct((species, capacity), mixing_ratio.dtype)] * peer_count,
    )(mixing_ratio, wanted)
    arrived = []
    for column in range(peer_count):
        opposite = peer_count - 1 - column
        arrived.append(from_behind(outgoing[opposite], "region", -offsets[column]))
    lane_index = jnp.arange(capacity, dtype=jnp.int32)
    live_lane = lane_index[None, :] < migrant_count[0][:, None]
    slots = jnp.where(live_lane, arrival_slot[0], parcels).reshape(-1, 1)
    sides, listed = halo_blocks.shape[1:]
    halo_shape = (species, listed * block_size)
    grid_spec = pltpu.PrefetchScalarGridSpec(
        num_scalar_prefetch=1,
        grid=(1,),
        in_specs=[pl.BlockSpec(memory_space=pl.ANY)]
        + [vmem_whole((species, capacity))] * peer_count
        + [vmem_whole(slots.shape)],
        out_specs=[vmem_whole(halo_shape), vmem_whole(halo_shape)],
        scratch_shapes=[pltpu.SemaphoreType.DMA((sides, listed))],
    )
    to_lower, to_upper = pl.pallas_call(
        functools.partial(halo_kernel, chunk, block_size, peer_count),
        grid_spec=grid_spec,
        out_shape=[jax.ShapeDtypeStruct(halo_shape, mixing_ratio.dtype)] * sides,
    )(halo_blocks[0], mixing_ratio, *arrived, slots)
    migrated = pl.pallas_call(
        functools.partial(place_kernel, chunk, peer_count),
        grid=(1,),
        in_specs=[vmem_whole(mixing_ratio.shape)]
        + [vmem_whole((species, capacity))] * peer_count
        + [vmem_whole(slots.shape)],
        out_specs=vmem_whole(mixing_ratio.shape),
        out_shape=jax.ShapeDtypeStruct(mixing_ratio.shape, mixing_ratio.dtype),
    )(mixing_ratio, *arrived, slots)
    from_lower = from_behind(to_upper, "region", 1)
    from_upper = from_behind(to_lower, "region", -1)
    return migrated, from_lower, from_upper


def split3(x):
    high = x.astype(jnp.bfloat16)
    low = (x - high.astype(jnp.float32)).astype(jnp.bfloat16)
    return high, low


def dot3(a_high, a_low, b_high, b_low):
    f32 = jnp.float32
    total = jnp.dot(a_high, b_high, preferred_element_type=f32)
    total = total + jnp.dot(a_high, b_low, preferred_element_type=f32)
    return total + jnp.dot(a_low, b_high, preferred_element_type=f32)


def mix_react_kernel(
    tile_blocks,
    neighbours,
    block_size,
    nb_ref,
    own_ref,
    weight_ref,
    temp_ref,
    order_ref,
    prod_ref,
    loss_ref,
    migrated_hbm,
    lower_hbm,
    upper_hbm,
    out_ref,
    picked,
    sems,
    mixed_ref,
    terms_ref,
    order_split,
    gain_split,
    gain_high,
):
    f32 = jnp.float32
    step = pl.program_id(0)
    steps = pl.num_programs(0)
    own_count = migrated_hbm.shape[1] // block_size
    halo_count = lower_hbm.shape[1] // block_size

    def fetch(at, slot, start):
        for t in range(tile_blocks):
            for k in range(neighbours):
                index = nb_ref[k, at * tile_blocks + t]
                target = picked.at[slot, t * neighbours + k]
                sem = sems.at[slot, t * neighbours + k]
                if not start:
                    pltpu.make_async_copy(
                        migrated_hbm.at[:, pl.ds(0, block_size)], target, sem
                    ).wait()
                    continue
                sources = (
                    (migrated_hbm, index, index < own_count),
                    (lower_hbm, index - own_count,
                     (index >= own_count) & (index < own_count + halo_count)),
                    (upper_hbm, index - own_count - halo_count,
                     index >= own_count + halo_count),
                )
                for source, local, chosen in sources:
                    limit = source.shape[1] // block_size - 1
                    local = jnp.minimum(jnp.maximum(local, 0), limit)

                    @pl.when(chosen)
                    def _():
                        begin = pl.multiple_of(local * block_size, block_size)
                        pltpu.make_async_copy(
                            source.at[:, pl.ds(begin, block_size)], target, sem
                        ).start()

    @pl.when(step == 0)
    def _():
        fetch(0, 0, True)
        order_high, order_low = split3(order_ref[...].T)
        reactions = order_high.shape[0]
        order_split[0:reactions] = order_high
        order_split[reactions:] = order_low
        gain_split[...] = jnp.zeros_like(gain_split)
        rows = prod_ref.shape[0]
        for part, source in enumerate((prod_ref, loss_ref)):
            high, low = split3(source[...])
            gain_split[pl.ds(2 * part * PAD_ROWS, rows)] = high
            gain_split[pl.ds((2 * part + 1) * PAD_ROWS, rows)] = low
            gain_high[pl.ds(part * PAD_ROWS, rows)] = high
        gain_high[...] = jnp.where(
            lax.broadcasted_iota(jnp.int32, gain_high.shape, 0) % PAD_ROWS < rows,
            gain_high[...],
            jnp.zeros_like(gain_high),
        )

    slot = step % 2

    @pl.when(step + 1 < steps)
    def _():
        fetch(step + 1, 1 - slot, True)

    fetch(step, slot, False)

    for t in range(tile_blocks):
        lanes = slice(t * block_size, (t + 1) * block_size)
        stacked = jnp.concatenate(
            [own_ref[:, lanes]] + [picked[slot, t * neighbours + k] for k in range(neighbours)],
            axis=1,
        )
        weight = weight_ref[t].reshape((neighbours + 1) * block_size, block_size)
        mixed_ref[:, lanes] = jnp.dot(stacked, weight, preferred_element_type=f32)
    mixed = mixed_ref[...]
    species = mixed.shape[0]
    terms_ref[0:species] = jnp.log(mixed)
    terms_ref[species:species + 1] = jnp.ones((1, mixed.shape[1]), f32)
    terms_ref[species + 1:species + 2] = temp_ref[...]
    log_high, log_low = split3(terms_ref[...])
    reactions = order_split.shape[0] // 2
    both = jnp.dot(order_split[...], log_high, preferred_element_type=f32)
    exponent = both[:reactions] + both[reactions:]
    exponent = exponent + jnp.dot(order_split[0:reactions], log_low, preferred_element_type=f32)
    rate = jnp.exp(exponent)
    rate_high, rate_low = split3(rate)
    by_high = jnp.dot(gain_split[...], rate_high, preferred_element_type=f32)
    by_low = jnp.dot(gain_high[...], rate_low, preferred_element_type=f32)
    gained = by_high[0:species] + by_high[PAD_ROWS:PAD_ROWS + species] + by_low[0:species]
    lost_mass = (
        by_high[2 * PAD_ROWS:2 * PAD_ROWS + species]
        + by_high[3 * PAD_ROWS:3 * PAD_ROWS + species]
        + by_low[PAD_ROWS:PAD_ROWS + species]
    )
    out_ref[...] = (mixed + gained) / (1.0 + lost_mass / mixed)


def mix_react(
    migrated,
    from_lower,
    from_upper,
    neighbour_block,
    mix_weight,
    inverse_temp,
    reactant_order,
    log_prefactor,
    activation_energy,
    production,
    loss_coefficient,
):
    species = migrated.shape[0]
    count_blocks, _, block_size, _ = mix_weight.shape
    neighbours = neighbour_block.shape[1]
    reactions = reactant_order.shape[0]
    tile_blocks = TILE_BLOCKS
    width = tile_blocks * block_size
    steps = count_blocks // tile_blocks

    def whole(shape):
        return pl.BlockSpec(shape, lambda i, nb: (0,) * len(shape))

    in_specs = [
        pl.BlockSpec((species, width), lambda i, nb: (0, i)),
        pl.BlockSpec((tile_blocks,) + mix_weight.shape[1:], lambda i, nb: (i, 0, 0, 0)),
        pl.BlockSpec((1, width), lambda i, nb: (0, i)),
        whole((species + 2, reactions)),
        whole(production.shape),
        whole(loss_coefficient.shape),
        pl.BlockSpec(memory_space=pl.ANY),
        pl.BlockSpec(memory_space=pl.ANY),
        pl.BlockSpec(memory_space=pl.ANY),
    ]
    bf16 = jnp.bfloat16
    grid_spec = pltpu.PrefetchScalarGridSpec(
        num_scalar_prefetch=1,
        grid=(steps,),
        in_specs=in_specs,
        out_specs=pl.BlockSpec((species, width), lambda i, nb: (0, i)),
        scratch_shapes=[
            pltpu.VMEM((2, tile_blocks * neighbours, species, block_size), bf16),
            pltpu.SemaphoreType.DMA((2, tile_blocks * neighbours)),
            pltpu.VMEM((species, width), jnp.float32),
            pltpu.VMEM((species + 2, width), jnp.float32),
            pltpu.VMEM((2 * reactions, species + 2), bf16),
            pltpu.VMEM((4 * PAD_ROWS, reactions), bf16),
            pltpu.VMEM((2 * PAD_ROWS, reactions), bf16),
        ],
    )
    kernel = functools.partial(mix_react_kernel, tile_blocks, neighbours, block_size)
    return pl.pallas_call(
        kernel,
        grid_spec=grid_spec,
        out_shape=jax.ShapeDtypeStruct((species, count_blocks * block_size), jnp.float32),
        compiler_params=pltpu.CompilerParams(dimension_semantics=("arbitrary",)),
    )(
        neighbour_block.T,
        migrated,
        mix_weight,
        inverse_temp.reshape(1, -1),
        jnp.concatenate(
            [reactant_order.T, log_prefactor[None, :], -activation_energy[None, :]], axis=0
        ),
        production,
        loss_coefficient,
        migrated,
        from_lower,
        from_upper,
    )


def shards(
    mixing_ratio,
    send_rows,
    migrant_count,
    arrival_slot,
    halo_blocks,
    neighbour_block,
    mix_weight,
    inverse_temp,
    reactant_order,
    log_prefactor,
    activation_energy,
    production,
    loss_coefficient,
):
    migrated, from_lower, from_upper = migrate(
        mixing_ratio, send_rows, migrant_count, arrival_slot, halo_blocks, mix_weight.shape[-1]
    )
    return mix_react(
        migrated,
        from_lower,
        from_upper,
        neighbour_block,
        mix_weight,
        inverse_temp,
        reactant_order,
        log_prefactor,
        activation_energy,
        production,
        loss_coefficient,
    )


def solution(mesh):
    placed = (
        P(None, "region"),
        P("region", None, None),
        P("region", None),
        P("region", None, None),
        P("region", None, None),
        P("region", None),
        P("region", None, None, None),
        P("region"),
        P(),
        P(),
        P(),
        P(),
        P(),
    )
    return jax.shard_map(
        shards, mesh=mesh, in_specs=placed, out_specs=P(None, "region"), check_vma=False
    )
```

```python
import functools

import jax
import jax.numpy as jnp
from jax import lax
from jax.experimental import pallas as pl
from jax.experimental.pallas import tpu as pltpu
from jax.sharding import PartitionSpec as P

HOP = 4
TILE_BLOCKS = 16
PAD_ROWS = 152


def from_behind(block, axis, distance):
    devices = range(lax.axis_size(axis))
    route = [((i - distance) % len(devices), i) for i in devices]
    return lax.ppermute(block, axis, route)


def peer_offsets():
    return [column - HOP if column < HOP else column - HOP + 1 for column in range(2 * HOP)]


def pick_kernel(chunk, mixing_ref, rows_ref, *out_refs):
    species, parcels = mixing_ref.shape
    wanted = rows_ref[...]
    total = jnp.zeros((species, wanted.shape[1]), jnp.float32)
    for part in range(parcels // chunk):
        position = lax.broadcasted_iota(jnp.int32, (chunk, wanted.shape[1]), 0) + part * chunk
        pick = (position == wanted).astype(jnp.bfloat16)
        total = total + jnp.dot(
            mixing_ref[:, part * chunk:(part + 1) * chunk], pick, preferred_element_type=jnp.float32
        )
    width = out_refs[0].shape[1]
    for column, out_ref in enumerate(out_refs):
        out_ref[...] = total[:, column * width:(column + 1) * width].astype(out_ref.dtype)


def marked_arrivals(received_refs, rows):
    received = jnp.concatenate([ref[...] for ref in received_refs], axis=1)
    species = received.shape[0]
    pad = (-species) % 16 or 16
    return jnp.concatenate([received, jnp.ones((pad, rows), received.dtype)], axis=0)


def place_kernel(chunk, peer_count, mixing_ref, *refs):
    received_refs = refs[:peer_count]
    slots_ref, migrated_ref = refs[peer_count:]
    species, parcels = mixing_ref.shape
    slots = slots_ref[...]
    marked = marked_arrivals(received_refs, slots.shape[0])
    for part in range(parcels // chunk):
        lanes = slice(part * chunk, (part + 1) * chunk)
        position = lax.broadcasted_iota(jnp.int32, (slots.shape[0], chunk), 1) + part * chunk
        place = (position == slots).astype(jnp.bfloat16)
        placed = jnp.dot(marked, place, preferred_element_type=jnp.float32)
        hit = placed[species:species + 1]
        migrated_ref[:, lanes] = jnp.where(
            hit > 0.5, placed[:species].astype(migrated_ref.dtype), mixing_ref[:, lanes]
        )


def halo_kernel(chunk, block_size, peer_count, halo_ref, mixing_ref, *refs):
    received_refs = refs[:peer_count]
    slots_ref, lower_ref, upper_ref, sems = refs[peer_count:]
    species = mixing_ref.shape[0]
    sides, listed = halo_ref.shape
    outs = (lower_ref, upper_ref)
    copies = []
    for side in range(sides):
        for j in range(listed):
            start = pl.multiple_of(halo_ref[side, j] * block_size, block_size)
            copy = pltpu.make_async_copy(
                mixing_ref.at[:, pl.ds(start, block_size)],
                outs[side].at[:, pl.ds(j * block_size, block_size)],
                sems.at[side, j],
            )
            copy.start()
            copies.append(copy)
    slots = slots_ref[...]
    marked = marked_arrivals(received_refs, slots.shape[0])
    lane = lax.broadcasted_iota(jnp.int32, (1, block_size), 1)
    per_chunk = chunk // block_size
    for copy in copies:
        copy.wait()
    for side in range(sides):
        for part in range(listed // per_chunk):
            first = part * per_chunk
            where_to = jnp.concatenate(
                [lane + halo_ref[side, j] * block_size for j in range(first, first + per_chunk)],
                axis=1,
            )
            place = (where_to == slots).astype(jnp.bfloat16)
            placed = jnp.dot(marked, place, preferred_element_type=jnp.float32)
            hit = placed[species:species + 1]
            lanes = slice(first * block_size, (first + per_chunk) * block_size)
            outs[side][:, lanes] = jnp.where(
                hit > 0.5, placed[:species].astype(outs[side].dtype), outs[side][:, lanes]
            )


def vmem_whole(shape):
    return pl.BlockSpec(shape, lambda *_: (0,) * len(shape))


def migrate(mixing_ratio, send_rows, migrant_count, arrival_slot, halo_blocks, block_size):
    species, parcels = mixing_ratio.shape
    capacity = send_rows.shape[-1]
    offsets = peer_offsets()
    peer_count = len(offsets)
    chunk = 1024
    wanted = send_rows[0].reshape(1, -1)
    outgoing = pl.pallas_call(
        functools.partial(pick_kernel, chunk),
        grid=(1,),
        in_specs=[vmem_whole(mixing_ratio.shape), vmem_whole(wanted.shape)],
        out_specs=[vmem_whole((species, capacity))] * peer_count,
        out_shape=[jax.ShapeDtypeStruct((species, capacity), mixing_ratio.dtype)] * peer_count,
    )(mixing_ratio, wanted)
    arrived = []
    for column in range(peer_count):
        opposite = peer_count - 1 - column
        arrived.append(from_behind(outgoing[opposite], "region", -offsets[column]))
    lane_index = jnp.arange(capacity, dtype=jnp.int32)
    live_lane = lane_index[None, :] < migrant_count[0][:, None]
    slots = jnp.where(live_lane, arrival_slot[0], parcels).reshape(-1, 1)
    sides, listed = halo_blocks.shape[1:]
    halo_shape = (species, listed * block_size)
    grid_spec = pltpu.PrefetchScalarGridSpec(
        num_scalar_prefetch=1,
        grid=(1,),
        in_specs=[pl.BlockSpec(memory_space=pl.ANY)]
        + [vmem_whole((species, capacity))] * peer_count
        + [vmem_whole(slots.shape)],
        out_specs=[vmem_whole(halo_shape), vmem_whole(halo_shape)],
        scratch_shapes=[pltpu.SemaphoreType.DMA((sides, listed))],
    )
    to_lower, to_upper = pl.pallas_call(
        functools.partial(halo_kernel, chunk, block_size, peer_count),
        grid_spec=grid_spec,
        out_shape=[jax.ShapeDtypeStruct(halo_shape, mixing_ratio.dtype)] * sides,
    )(halo_blocks[0], mixing_ratio, *arrived, slots)
    migrated = pl.pallas_call(
        functools.partial(place_kernel, chunk, peer_count),
        grid=(1,),
        in_specs=[vmem_whole(mixing_ratio.shape)]
        + [vmem_whole((species, capacity))] * peer_count
        + [vmem_whole(slots.shape)],
        out_specs=vmem_whole(mixing_ratio.shape),
        out_shape=jax.ShapeDtypeStruct(mixing_ratio.shape, mixing_ratio.dtype),
    )(mixing_ratio, *arrived, slots)
    from_lower = from_behind(to_upper, "region", 1)
    from_upper = from_behind(to_lower, "region", -1)
    return migrated, from_lower, from_upper


def split3(x):
    high = x.astype(jnp.bfloat16)
    low = (x - high.astype(jnp.float32)).astype(jnp.bfloat16)
    return high, low


def dot3(a_high, a_low, b_high, b_low):
    f32 = jnp.float32
    total = jnp.dot(a_high, b_high, preferred_element_type=f32)
    total = total + jnp.dot(a_high, b_low, preferred_element_type=f32)
    return total + jnp.dot(a_low, b_high, preferred_element_type=f32)


def mix_react_kernel(
    tile_blocks,
    neighbours,
    block_size,
    nb_ref,
    own_ref,
    weight_ref,
    temp_ref,
    order_ref,
    prod_ref,
    loss_ref,
    migrated_hbm,
    lower_hbm,
    upper_hbm,
    out_ref,
    picked,
    sems,
    mixed_ref,
    terms_ref,
    order_split,
    gain_split,
    gain_high,
):
    f32 = jnp.float32
    step = pl.program_id(0)
    steps = pl.num_programs(0)
    own_count = migrated_hbm.shape[1] // block_size
    halo_count = lower_hbm.shape[1] // block_size

    def fetch(at, slot, start):
        for t in range(tile_blocks):
            for k in range(neighbours):
                index = nb_ref[k, at * tile_blocks + t]
                target = picked.at[slot, t * neighbours + k]
                sem = sems.at[slot, t * neighbours + k]
                if not start:
                    pltpu.make_async_copy(
                        migrated_hbm.at[:, pl.ds(0, block_size)], target, sem
                    ).wait()
                    continue
                sources = (
                    (migrated_hbm, index, index < own_count),
                    (lower_hbm, index - own_count,
                     (index >= own_count) & (index < own_count + halo_count)),
                    (upper_hbm, index - own_count - halo_count,
                     index >= own_count + halo_count),
                )
                for source, local, chosen in sources:
                    limit = source.shape[1] // block_size - 1
                    local = jnp.minimum(jnp.maximum(local, 0), limit)

                    @pl.when(chosen)
                    def _():
                        begin = pl.multiple_of(local * block_size, block_size)
                        pltpu.make_async_copy(
                            source.at[:, pl.ds(begin, block_size)], target, sem
                        ).start()

    @pl.when(step == 0)
    def _():
        fetch(0, 0, True)
        order_high, order_low = split3(order_ref[...].T)
        reactions = order_high.shape[0]
        order_split[0:reactions] = order_high
        order_split[reactions:] = order_low
        gain_split[...] = jnp.zeros_like(gain_split)
        rows = prod_ref.shape[0]
        for part, source in enumerate((prod_ref, loss_ref)):
            high, low = split3(source[...])
            gain_split[pl.ds(2 * part * PAD_ROWS, rows)] = high
            gain_split[pl.ds((2 * part + 1) * PAD_ROWS, rows)] = low
            gain_high[pl.ds(part * PAD_ROWS, rows)] = high
        gain_high[...] = jnp.where(
            lax.broadcasted_iota(jnp.int32, gain_high.shape, 0) % PAD_ROWS < rows,
            gain_high[...],
            jnp.zeros_like(gain_high),
        )

    slot = step % 2

    @pl.when(step + 1 < steps)
    def _():
        fetch(step + 1, 1 - slot, True)

    fetch(step, slot, False)

    for t in range(tile_blocks):
        lanes = slice(t * block_size, (t + 1) * block_size)
        stacked = jnp.concatenate(
            [own_ref[:, lanes]] + [picked[slot, t * neighbours + k] for k in range(neighbours)],
            axis=1,
        )
        weight = weight_ref[t].reshape((neighbours + 1) * block_size, block_size)
        mixed_ref[:, lanes] = jnp.dot(stacked, weight, preferred_element_type=f32)
    mixed = mixed_ref[...]
    species = mixed.shape[0]
    terms_ref[0:species] = jnp.log(mixed)
    terms_ref[species:species + 1] = jnp.ones((1, mixed.shape[1]), f32)
    terms_ref[species + 1:species + 2] = temp_ref[...]
    log_high, log_low = split3(terms_ref[...])
    reactions = order_split.shape[0] // 2
    both = jnp.dot(order_split[...], log_high, preferred_element_type=f32)
    exponent = both[:reactions] + both[reactions:]
    exponent = exponent + jnp.dot(order_split[0:reactions], log_low, preferred_element_type=f32)
    rate = jnp.exp(exponent)
    rate_high, rate_low = split3(rate)
    by_high = jnp.dot(gain_split[...], rate_high, preferred_element_type=f32)
    by_low = jnp.dot(gain_high[...], rate_low, preferred_element_type=f32)
    gained = by_high[0:species] + by_high[PAD_ROWS:PAD_ROWS + species] + by_low[0:species]
    lost_mass = (
        by_high[2 * PAD_ROWS:2 * PAD_ROWS + species]
        + by_high[3 * PAD_ROWS:3 * PAD_ROWS + species]
        + by_low[PAD_ROWS:PAD_ROWS + species]
    )
    out_ref[...] = (mixed + gained) / (1.0 + lost_mass / mixed)


def mix_react(
    migrated,
    from_lower,
    from_upper,
    neighbour_block,
    mix_weight,
    inverse_temp,
    reactant_order,
    log_prefactor,
    activation_energy,
    production,
    loss_coefficient,
):
    species = migrated.shape[0]
    count_blocks, _, block_size, _ = mix_weight.shape
    neighbours = neighbour_block.shape[1]
    reactions = reactant_order.shape[0]
    tile_blocks = TILE_BLOCKS
    width = tile_blocks * block_size
    steps = count_blocks // tile_blocks

    def whole(shape):
        return pl.BlockSpec(shape, lambda i, nb: (0,) * len(shape))

    in_specs = [
        pl.BlockSpec((species, width), lambda i, nb: (0, i)),
        pl.BlockSpec((tile_blocks,) + mix_weight.shape[1:], lambda i, nb: (i, 0, 0, 0)),
        pl.BlockSpec((1, width), lambda i, nb: (0, i)),
        whole((species + 2, reactions)),
        whole(production.shape),
        whole(loss_coefficient.shape),
        pl.BlockSpec(memory_space=pl.ANY),
        pl.BlockSpec(memory_space=pl.ANY),
        pl.BlockSpec(memory_space=pl.ANY),
    ]
    bf16 = jnp.bfloat16
    grid_spec = pltpu.PrefetchScalarGridSpec(
        num_scalar_prefetch=1,
        grid=(steps,),
        in_specs=in_specs,
        out_specs=pl.BlockSpec((species, width), lambda i, nb: (0, i)),
        scratch_shapes=[
            pltpu.VMEM((2, tile_blocks * neighbours, species, block_size), bf16),
            pltpu.SemaphoreType.DMA((2, tile_blocks * neighbours)),
            pltpu.VMEM((species, width), jnp.float32),
            pltpu.VMEM((species + 2, width), jnp.float32),
            pltpu.VMEM((2 * reactions, species + 2), bf16),
            pltpu.VMEM((4 * PAD_ROWS, reactions), bf16),
            pltpu.VMEM((2 * PAD_ROWS, reactions), bf16),
        ],
    )
    kernel = functools.partial(mix_react_kernel, tile_blocks, neighbours, block_size)
    return pl.pallas_call(
        kernel,
        grid_spec=grid_spec,
        out_shape=jax.ShapeDtypeStruct((species, count_blocks * block_size), jnp.float32),
        compiler_params=pltpu.CompilerParams(dimension_semantics=("arbitrary",)),
    )(
        neighbour_block.T,
        migrated,
        mix_weight,
        inverse_temp.reshape(1, -1),
        jnp.concatenate(
            [reactant_order.T, log_prefactor[None, :], -activation_energy[None, :]], axis=0
        ),
        production,
        loss_coefficient,
        migrated,
        from_lower,
        from_upper,
    )


def shards(
    mixing_ratio,
    send_rows,
    migrant_count,
    arrival_slot,
    halo_blocks,
    neighbour_block,
    mix_weight,
    inverse_temp,
    reactant_order,
    log_prefactor,
    activation_energy,
    production,
    loss_coefficient,
):
    migrated, from_lower, from_upper = migrate(
        mixing_ratio, send_rows, migrant_count, arrival_slot, halo_blocks, mix_weight.shape[-1]
    )
    return mix_react(
        migrated,
        from_lower,
        from_upper,
        neighbour_block,
        mix_weight,
        inverse_temp,
        reactant_order,
        log_prefactor,
        activation_energy,
        production,
        loss_coefficient,
    )


def solution(mesh):
    placed = (
        P(None, "region"),
        P("region", None, None),
        P("region", None),
        P("region", None, None),
        P("region", None, None),
        P("region", None),
        P("region", None, None, None),
        P("region"),
        P(),
        P(),
        P(),
        P(),
        P(),
    )
    return jax.shard_map(
        shards, mesh=mesh, in_specs=placed, out_specs=P(None, "region"), check_vma=False
    )
```
